32 devices in a mesh: ens: 8 (over z, y), col: 4 (over x, core).
Axes of the slice: x: 2, y: 2, z: 4, core: 2. Of those that a mesh axis runs over, the one named last changes fastest.
Arguments:
- state: float32 [256, 3, 8, 4096], P('ens', None, None, 'col'), may hold values from -4 to 4
- noise: float32 [256, 3, 8, 4096], P('ens', None, None, 'col'), may hold values from -1 to 1
- parents: int32 [256], replicated, may hold values from 0 to 255, as said below
Outputs:
- forecast: float32 [256, 3, 8, 4096], P('ens', None, None, 'col')
The draws below stay inside these ranges and needn't reach their ends.
Inputs may be any that keep to these rules, and one draw needn't show every extreme that they name: Children are in aligned blocks of 32, parents likewise. For any block of children and any block of parents, at most 8 of those children have their parent in that block; in every block of children each block of parents that is used supplies exactly 8, and these 8 children have exactly 4 distinct parents, each the parent of two of them.
All inputs are finite; a program needn't handle non-finite values.
Results may differ from the reference program's by a relative error of at most 0.0003.
Values sent between devices are 32-bit elements; how exact they have to be, the bound alone decides.
No kernel may reach another device: no remote copies, remote signals or barrier semaphores. Data moves between devices by JAX's collectives and lax.ppermute only.
A program may use at most 128 MiB of HBM per device.

```python
import jax
import jax.numpy as jnp
from jax import lax

PART_DEV = 32
ROWS = 8
COLS = 4096
STEPS = 4
PARTICLES = 256
CAP = 8
DIST = 4


def draw_parents(key, part):
    blocks = PARTICLES // PART_DEV
    groups = PART_DEV // CAP
    base = jax.random.fold_in(key, 11)
    first_key, second_key, third_key = jax.random.split(base, 3)
    offsets = jax.vmap(lambda sub: jax.random.permutation(sub, blocks))(jax.random.split(first_key, blocks))
    offsets = offsets[:, :groups]
    sorted_ranking = jax.vmap(lambda sub: jax.random.permutation(sub, PART_DEV))(jax.random.split(second_key, blocks))
    group_of = sorted_ranking // CAP
    incoming_rank = sorted_ranking % CAP
    chosen = jnp.take_along_axis(offsets, group_of, axis=1)
    block_ids = jnp.arange(blocks, dtype=jnp.int32)[:, None]
    source = (block_ids + chosen) % blocks
    row_lookup_tables = jax.vmap(lambda sub: jax.random.permutation(sub, PART_DEV))(jax.random.split(third_key, blocks * groups))
    row_lookup_tables = row_lookup_tables.reshape(blocks, groups, PART_DEV)[:, :, :DIST]
    flat_tables = row_lookup_tables.reshape(blocks, groups * DIST)
    local_row = jnp.take_along_axis(flat_tables, group_of * DIST + incoming_rank % DIST, axis=1)
    return (source * PART_DEV + local_row).reshape(-1).astype(jnp.int32)


def block_scale(own_key, extent, cuts, least, top_value):
    gain, own = 1.0, jax.random.fold_in(own_key, 6)
    for position, shards_of in cuts:
        heights = jnp.exp(jax.random.uniform(jax.random.fold_in(own, position), (shards_of,), jnp.float32, least / len(cuts), top_value / len(cuts)))
        gain = gain * jnp.repeat(heights, extent[position] // shards_of).reshape([-1 if axis == position else 1 for axis in range(len(extent))])
    return gain


def centred(key, shape, width, bound, cuts=(), held_as=jnp.bfloat16):
    factor_of = block_scale(key, shape, cuts, -0.22, 0.18) if cuts else 1.0
    array = jax.random.normal(key, shape, jnp.float32) * width * factor_of
    return jnp.minimum(jnp.maximum(array, -bound), bound).astype(held_as)


def setup_inputs(seed: int = 0) -> dict:
    seeds = jax.random.split(jax.random.key(seed), 4)
    return {
        "state": centred(seeds[0], (PARTICLES, 3, ROWS, COLS), 0.5, 4.0, ((0, 8), (3, 4)), jnp.float32),
        "noise": centred(seeds[1], (PARTICLES, 3, ROWS, COLS), 0.2, 1.0, ((0, 8), (3, 4)), jnp.float32),
        "parents": draw_parents(jax.random.fold_in(seeds[3], 71), 0),
    }


time_step = 0.3
coriolis = 0.2
gravity = 1.0


def diff_x(values):
    return 0.5 * (values[..., 2:] - values[..., :-2])


def diff_y(values):
    middle = values[..., 1:-1]
    return 0.5 * (jnp.roll(middle, -1, axis=-2) - jnp.roll(middle, 1, axis=-2))


def neighbour_mean(values):
    middle = values[..., 1:-1]
    return 0.25 * (values[..., 2:] + values[..., :-2] + jnp.roll(middle, -1, axis=-2) + jnp.roll(middle, 1, axis=-2))


def advance(fields):
    surface = fields[:, 0]
    zonal = fields[:, 1]
    meridional = fields[:, 2]
    water_depth = 1.0 + surface
    centre_zonal = zonal[..., 1:-1]
    centre_merid = meridional[..., 1:-1]
    new_surface = neighbour_mean(surface) - time_step * (diff_x(water_depth * zonal) + diff_y(water_depth * meridional))
    new_zonal = neighbour_mean(zonal) - time_step * (centre_zonal * diff_x(zonal) + centre_merid * diff_y(zonal) - coriolis * centre_merid + gravity * diff_x(surface))
    new_merid = neighbour_mean(meridional) - time_step * (centre_zonal * diff_x(meridional) + centre_merid * diff_y(meridional) + coriolis * centre_zonal + gravity * diff_y(surface))
    return jnp.stack([new_surface, new_zonal, new_merid], axis=1)


def reference(state, noise, parents):
    blocks = PARTICLES // PART_DEV
    ancestor_blocks = parents.reshape(blocks, PART_DEV)
    random_noise_blocks = noise.reshape(blocks, PART_DEV, 3, ROWS, COLS)

    def prediction_block(matched_couple):
        indices, jitter = matched_couple
        fields = jnp.take(state, indices.astype(jnp.int32), axis=0) + jitter
        for repeat in range(STEPS):
            fields = advance(jnp.pad(fields, ((0, 0), (0, 0), (0, 0), (1, 1)), mode="wrap"))
        return fields

    final_outcome = lax.map(prediction_block, (ancestor_blocks, random_noise_blocks))
    return final_outcome.reshape(PARTICLES, 3, ROWS, COLS)
```

```python
import jax
import jax.numpy as jnp
from jax import lax
from jax.experimental import pallas as pl
from jax.experimental.pallas import tpu as pltpu
from jax.sharding import PartitionSpec as P

STEPS = 4
LANES = 128

time_step = 0.3
coriolis = 0.2
gravity = 1.0


def routing(parents, count, per_dev, dist, me):
    blocks = parents.reshape(count, per_dev)
    owner = blocks // per_dev
    local = blocks % per_dev
    ids = jnp.arange(per_dev, dtype=jnp.int32)
    same = blocks[:, :, None] == blocks[:, None, :]
    earlier = ids[None, :] < ids[:, None]
    first = jnp.logical_not(jnp.any(same & earlier[None], axis=2))
    below = (
        (owner[:, :, None] == owner[:, None, :])
        & (blocks[:, None, :] < blocks[:, :, None])
        & first[:, None, :]
    )
    slot = jnp.sum(below.astype(jnp.int32), axis=2)
    slots = jnp.arange(dist, dtype=jnp.int32)
    pick = (owner == me)[:, None, :] & first[:, None, :] & (slot[:, None, :] == slots[None, :, None])
    send_index = jnp.sum(pick.astype(jnp.int32) * local[:, None, :], axis=2).reshape(-1)
    my_owner = lax.dynamic_index_in_dim(owner, me, 0, keepdims=False)
    my_slot = lax.dynamic_index_in_dim(slot, me, 0, keepdims=False)
    return send_index, my_owner * dist + my_slot


def advance(e, u, v):
    width = e.shape[-1]
    rows = e.shape[-2]

    def xp(a):
        return pltpu.roll(a, width - 1, 1)

    def xm(a):
        return pltpu.roll(a, 1, 1)

    def yp(a):
        return pltpu.roll(a, rows - 1, 0)

    def ym(a):
        return pltpu.roll(a, 1, 0)

    depth = 1.0 + e
    hu = depth * u
    hv = depth * v
    e_xp, e_xm, e_yp, e_ym = xp(e), xm(e), yp(e), ym(e)
    u_xp, u_xm, u_yp, u_ym = xp(u), xm(u), yp(u), ym(u)
    v_xp, v_xm, v_yp, v_ym = xp(v), xm(v), yp(v), ym(v)
    mean_e = 0.25 * (e_xp + e_xm + e_yp + e_ym)
    mean_u = 0.25 * (u_xp + u_xm + u_yp + u_ym)
    mean_v = 0.25 * (v_xp + v_xm + v_yp + v_ym)
    dx_hu = 0.5 * (xp(hu) - xm(hu))
    dy_hv = 0.5 * (yp(hv) - ym(hv))
    dx_e = 0.5 * (e_xp - e_xm)
    dy_e = 0.5 * (e_yp - e_ym)
    dx_u = 0.5 * (u_xp - u_xm)
    dy_u = 0.5 * (u_yp - u_ym)
    dx_v = 0.5 * (v_xp - v_xm)
    dy_v = 0.5 * (v_yp - v_ym)
    new_e = mean_e - time_step * (dx_hu + dy_hv)
    new_u = mean_u - time_step * (u * dx_u + v * dy_u - coriolis * v + gravity * dx_e)
    new_v = mean_v - time_step * (u * dx_v + v * dy_v + coriolis * u + gravity * dy_e)
    return new_e, new_u, new_v


def forecast_kernel(pos_ref, inc_ref, noise_ref, halo_ref, out_ref):
    cols = out_ref.shape[-1]
    fields = []
    for f in range(3):
        body = inc_ref[0, f] + noise_ref[0, f]
        fields.append(jnp.concatenate([body, halo_ref[0, f]], axis=-1))
    e, u, v = fields
    for _ in range(STEPS):
        e, u, v = advance(e, u, v)
    out_ref[0, 0] = e[:, :cols]
    out_ref[0, 1] = u[:, :cols]
    out_ref[0, 2] = v[:, :cols]


def forecast(position, incoming, noise, halo):
    per_dev, nf, rows, cols = noise.shape
    grid_spec = pltpu.PrefetchScalarGridSpec(
        num_scalar_prefetch=1,
        grid=(per_dev,),
        in_specs=[
            pl.BlockSpec((1, nf, rows, cols), lambda i, pos: (pos[i], 0, 0, 0)),
            pl.BlockSpec((1, nf, rows, cols), lambda i, pos: (i, 0, 0, 0)),
            pl.BlockSpec((1, nf, rows, LANES), lambda i, pos: (i, 0, 0, 0)),
        ],
        out_specs=pl.BlockSpec((1, nf, rows, cols), lambda i, pos: (i, 0, 0, 0)),
    )
    return pl.pallas_call(
        forecast_kernel,
        grid_spec=grid_spec,
        out_shape=jax.ShapeDtypeStruct(noise.shape, noise.dtype),
    )(position, incoming, noise, halo)


def shards(state, noise, parents):
    count = lax.axis_size("ens")
    me = lax.axis_index("ens")
    per_dev = state.shape[0]
    dist = max(1, -(-per_dev // count))
    send_index, position = routing(parents, count, per_dev, dist, me)
    outgoing = jnp.take(state, send_index, axis=0)
    incoming = lax.all_to_all(outgoing, "ens", split_axis=0, concat_axis=0, tiled=True)

    width = STEPS
    left_edge = jnp.take(incoming[..., :width], position, axis=0) + noise[..., :width]
    right_edge = jnp.take(incoming[..., -width:], position, axis=0) + noise[..., -width:]
    ring = lax.axis_size("col")
    from_left = lax.ppermute(right_edge, "col", [(i, (i + 1) % ring) for i in range(ring)])
    from_right = lax.ppermute(left_edge, "col", [(i, (i - 1) % ring) for i in range(ring)])
    gap = jnp.zeros(from_left.shape[:-1] + (LANES - 2 * width,), from_left.dtype)
    halo = jnp.concatenate([from_right, gap, from_left], axis=-1)
    return forecast(position, incoming, noise, halo)


def solution(mesh):
    placed = (P("ens", None, None, "col"), P("ens", None, None, "col"), P())
    return jax.shard_map(
        shards, mesh=mesh, in_specs=placed, out_specs=P("ens", None, None, "col"), check_vma=False
    )
```

```python
import jax
import jax.numpy as jnp
from jax import lax
from jax.experimental import pallas as pl
from jax.experimental.pallas import tpu as pltpu
from jax.sharding import PartitionSpec as P

STEPS = 4
LANES = 128
BLOCK = 4

time_step = 0.3
coriolis = 0.2
gravity = 1.0


def routing(parents, count, per_dev, dist, me):
    blocks = parents.reshape(count, per_dev)
    owner = blocks // per_dev
    local = blocks % per_dev
    ids = jnp.arange(per_dev, dtype=jnp.int32)
    same = blocks[:, :, None] == blocks[:, None, :]
    earlier = ids[None, :] < ids[:, None]
    first = jnp.logical_not(jnp.any(same & earlier[None], axis=2))
    below = (
        (owner[:, :, None] == owner[:, None, :])
        & (blocks[:, None, :] < blocks[:, :, None])
        & first[:, None, :]
    )
    slot = jnp.sum(below.astype(jnp.int32), axis=2)
    slots = jnp.arange(dist, dtype=jnp.int32)
    pick = (owner == me)[:, None, :] & first[:, None, :] & (slot[:, None, :] == slots[None, :, None])
    send_index = jnp.sum(pick.astype(jnp.int32) * local[:, None, :], axis=2).reshape(-1)
    my_owner = lax.dynamic_index_in_dim(owner, me, 0, keepdims=False)
    my_slot = lax.dynamic_index_in_dim(slot, me, 0, keepdims=False)
    return send_index, my_owner * dist + my_slot


def sweep(src, dst, ncol):
    rows = src.shape[-2]
    lane = lax.broadcasted_iota(jnp.int32, (rows, LANES), 1)
    first_lane = lane == 0
    last_lane = lane == LANES - 1

    def load(j):
        window = pl.ds((j % ncol) * LANES, LANES)
        e = src[0, :, window]
        u = src[1, :, window]
        v = src[2, :, window]
        depth = 1.0 + e
        return e, u, v, depth

    def ahead(vals):
        e, u, v, depth = vals
        return tuple(pltpu.roll(a, LANES - 1, 1) for a in (e, u, v, depth * u))

    def behind(vals):
        e, u, v, depth = vals
        return tuple(pltpu.roll(a, 1, 1) for a in (e, u, v, depth * u))

    def yp(a):
        return pltpu.roll(a, rows - 1, 0)

    def ym(a):
        return pltpu.roll(a, 1, 0)

    here = load(0)
    prev_behind = behind(load(ncol - 1)) if ncol > 1 else behind(here)
    here_behind = behind(here)
    here_ahead = ahead(here)
    for j in range(ncol):
        if ncol > 1:
            nxt = load(j + 1)
            nxt_ahead = ahead(nxt)
            nxt_behind = behind(nxt)
        else:
            nxt, nxt_ahead, nxt_behind = here, here_ahead, here_behind
        xp = [jnp.where(last_lane, a, b) for a, b in zip(nxt_ahead, here_ahead)]
        xm = [jnp.where(first_lane, a, b) for a, b in zip(prev_behind, here_behind)]
        e, u, v, depth = here
        e_xp, u_xp, v_xp, hu_xp = xp
        e_xm, u_xm, v_xm, hu_xm = xm
        hv = depth * v
        e_yp, e_ym = yp(e), ym(e)
        u_yp, u_ym = yp(u), ym(u)
        v_yp, v_ym = yp(v), ym(v)
        hv_yp, hv_ym = yp(hv), ym(hv)
        half_step = 0.5 * time_step
        new_e = 0.25 * (e_xp + e_xm + e_yp + e_ym) - half_step * ((hu_xp - hu_xm) + (hv_yp - hv_ym))
        new_u = (
            0.25 * (u_xp + u_xm + u_yp + u_ym)
            - half_step * (u * (u_xp - u_xm) + v * (u_yp - u_ym) + gravity * (e_xp - e_xm))
            + (time_step * coriolis) * v
        )
        new_v = (
            0.25 * (v_xp + v_xm + v_yp + v_ym)
            - half_step * (u * (v_xp - v_xm) + v * (v_yp - v_ym) + gravity * (e_yp - e_ym))
            - (time_step * coriolis) * u
        )
        window = pl.ds(j * LANES, LANES)
        dst[0, :, window] = new_e
        dst[1, :, window] = new_u
        dst[2, :, window] = new_v
        prev_behind = here_behind
        here, here_behind, here_ahead = nxt, nxt_behind, nxt_ahead


def run_steps(src, out, first, second, ncol):
    chain = [src] + [first if s % 2 == 0 else second for s in range(STEPS - 1)] + [out]
    for s in range(STEPS):
        sweep(chain[s], chain[s + 1], ncol)


def main_kernel(ch_ref, out_ref, first, second):
    ncol = ch_ref.shape[-1] // LANES

    def particle(i, carry):
        run_steps(ch_ref.at[i], out_ref.at[i], first, second, ncol)
        return carry

    lax.fori_loop(0, ch_ref.shape[0], particle, 0)


def main_forecast(children):
    per_dev, nf, rows, cols = children.shape
    block = BLOCK if per_dev % BLOCK == 0 else 1
    spec = pl.BlockSpec((block, nf, rows, cols), lambda i: (i, 0, 0, 0))
    return pl.pallas_call(
        main_kernel,
        grid=(per_dev // block,),
        in_specs=[spec],
        out_specs=spec,
        out_shape=jax.ShapeDtypeStruct(children.shape, children.dtype),
        scratch_shapes=[pltpu.VMEM((nf, rows, cols), jnp.float32)] * 2,
    )(children)


def edge_kernel(lblk, rblk, from_left, from_right, body_ref, out_ref, packed, first, second, result):
    side = pl.program_id(0)
    rows = lblk.shape[-2]
    lane = lax.broadcasted_iota(jnp.int32, (rows, LANES), 1)
    half = LANES // 2
    width = STEPS

    @pl.when(side == 0)
    def _():
        def particle(i, carry):
            for f in range(3):
                left = jnp.where(lane >= LANES - width, from_left[i, f], lblk[i, f])
                right = jnp.where(lane < width, from_right[i, f], rblk[i, f])
                right = pltpu.roll(right, half, 1)
                keep_left = (lane < 2 * width) | (lane >= LANES - width)
                packed[f] = jnp.where(keep_left, left, right)
            run_steps(packed, result.at[i], first, second, 1)
            return carry

        lax.fori_loop(0, lblk.shape[0], particle, 0)
        out_ref[...] = jnp.where(lane < width, result[...], body_ref[...])

    @pl.when(side == 1)
    def _():
        def particle(i, carry):
            for f in range(3):
                out_ref[i, f] = jnp.where(
                    lane >= LANES - width, pltpu.roll(result[i, f], half, 1), body_ref[i, f]
                )
            return carry

        lax.fori_loop(0, lblk.shape[0], particle, 0)


def edge_fix(lblk, rblk, from_left, from_right, body):
    per_dev, nf, rows, cols = body.shape
    ncol = cols // LANES
    whole = pl.BlockSpec((per_dev, nf, rows, LANES), lambda s: (0, 0, 0, 0))
    edge = pl.BlockSpec((per_dev, nf, rows, LANES), lambda s: (0, 0, 0, s * (ncol - 1)))
    return pl.pallas_call(
        edge_kernel,
        grid=(2,),
        in_specs=[whole, whole, whole, whole, edge],
        out_specs=edge,
        out_shape=jax.ShapeDtypeStruct(body.shape, body.dtype),
        scratch_shapes=[
            pltpu.VMEM((nf, rows, LANES), jnp.float32),
            pltpu.VMEM((nf, rows, LANES), jnp.float32),
            pltpu.VMEM((nf, rows, LANES), jnp.float32),
            pltpu.VMEM((per_dev, nf, rows, LANES), jnp.float32),
        ],
        input_output_aliases={4: 0},
    )(lblk, rblk, from_left, from_right, body)


def shards(state, noise, parents):
    count = lax.axis_size("ens")
    me = lax.axis_index("ens")
    per_dev = state.shape[0]
    dist = max(1, -(-per_dev // count))
    send_index, position = routing(parents, count, per_dev, dist, me)
    outgoing = jnp.take(state, send_index, axis=0, mode="clip")
    incoming = lax.all_to_all(outgoing, "ens", split_axis=0, concat_axis=0, tiled=True)
    children = jnp.take(incoming, position, axis=0, mode="clip") + noise

    lblk = children[..., :LANES]
    rblk = children[..., -LANES:]
    ring = lax.axis_size("col")
    from_left = lax.ppermute(rblk, "col", [(i, (i + 1) % ring) for i in range(ring)])
    from_right = lax.ppermute(lblk, "col", [(i, (i - 1) % ring) for i in range(ring)])
    body = main_forecast(children)
    return edge_fix(lblk, rblk, from_left, from_right, body)


def solution(mesh):
    placed = (P("ens", None, None, "col"), P("ens", None, None, "col"), P())
    return jax.shard_map(
        shards, mesh=mesh, in_specs=placed, out_specs=P("ens", None, None, "col"), check_vma=False
    )
```

```python
import jax
import jax.numpy as jnp
from jax import lax
from jax.experimental import pallas as pl
from jax.experimental.pallas import tpu as pltpu
from jax.sharding import PartitionSpec as P

STEPS = 4
LANES = 128
PAIR = 2
EDGE_GROUP = 8

time_step = 0.3
coriolis = 0.2
gravity = 1.0


def routing(parents, count, per_dev, dist, me):
    blocks = parents.reshape(count, per_dev)
    owner = blocks // per_dev
    local = blocks % per_dev
    ids = jnp.arange(per_dev, dtype=jnp.int32)
    same = blocks[:, :, None] == blocks[:, None, :]
    earlier = ids[None, :] < ids[:, None]
    first = jnp.logical_not(jnp.any(same & earlier[None], axis=2))
    below = (
        (owner[:, :, None] == owner[:, None, :])
        & (blocks[:, None, :] < blocks[:, :, None])
        & first[:, None, :]
    )
    slot = jnp.sum(below.astype(jnp.int32), axis=2)
    slots = jnp.arange(dist, dtype=jnp.int32)
    pick = (owner == me)[:, None, :] & first[:, None, :] & (slot[:, None, :] == slots[None, :, None])
    send_index = jnp.sum(pick.astype(jnp.int32) * local[:, None, :], axis=2).reshape(-1)
    my_owner = lax.dynamic_index_in_dim(owner, me, 0, keepdims=False)
    my_slot = lax.dynamic_index_in_dim(slot, me, 0, keepdims=False)
    return send_index, my_owner * dist + my_slot


def sweep(src, dst, ncol, extra=None):
    rows = src.shape[-2]
    lane = lax.broadcasted_iota(jnp.int32, (rows, LANES), 1)
    first_lane = lane == 0
    last_lane = lane == LANES - 1

    def load(j):
        window = pl.ds((j % ncol) * LANES, LANES)
        e = src[0, :, window]
        u = src[1, :, window]
        v = src[2, :, window]
        if extra is not None:
            e = e + extra[0, :, window]
            u = u + extra[1, :, window]
            v = v + extra[2, :, window]
        depth = 1.0 + e
        return e, u, v, depth

    def ahead(vals):
        e, u, v, depth = vals
        return tuple(pltpu.roll(a, LANES - 1, 1) for a in (e, u, v, depth * u))

    def behind(vals):
        e, u, v, depth = vals
        return tuple(pltpu.roll(a, 1, 1) for a in (e, u, v, depth * u))

    def yp(a):
        return pltpu.roll(a, rows - 1, 0)

    def ym(a):
        return pltpu.roll(a, 1, 0)

    here = load(0)
    prev_behind = behind(load(ncol - 1)) if ncol > 1 else behind(here)
    here_behind = behind(here)
    here_ahead = ahead(here)
    for j in range(ncol):
        if ncol > 1:
            nxt = load(j + 1)
            nxt_ahead = ahead(nxt)
            nxt_behind = behind(nxt)
        else:
            nxt, nxt_ahead, nxt_behind = here, here_ahead, here_behind
        xp = [jnp.where(last_lane, a, b) for a, b in zip(nxt_ahead, here_ahead)]
        xm = [jnp.where(first_lane, a, b) for a, b in zip(prev_behind, here_behind)]
        e, u, v, depth = here
        e_xp, u_xp, v_xp, hu_xp = xp
        e_xm, u_xm, v_xm, hu_xm = xm
        hv = depth * v
        e_yp, e_ym = yp(e), ym(e)
        u_yp, u_ym = yp(u), ym(u)
        v_yp, v_ym = yp(v), ym(v)
        hv_yp, hv_ym = yp(hv), ym(hv)
        half_step = 0.5 * time_step
        new_e = 0.25 * (e_xp + e_xm + e_yp + e_ym) - half_step * ((hu_xp - hu_xm) + (hv_yp - hv_ym))
        new_u = (
            0.25 * (u_xp + u_xm + u_yp + u_ym)
            - half_step * (u * (u_xp - u_xm) + v * (u_yp - u_ym) + gravity * (e_xp - e_xm))
            + (time_step * coriolis) * v
        )
        new_v = (
            0.25 * (v_xp + v_xm + v_yp + v_ym)
            - half_step * (u * (v_xp - v_xm) + v * (v_yp - v_ym) + gravity * (e_yp - e_ym))
            - (time_step * coriolis) * u
        )
        window = pl.ds(j * LANES, LANES)
        dst[0, :, window] = new_e
        dst[1, :, window] = new_u
        dst[2, :, window] = new_v
        prev_behind = here_behind
        here, here_behind, here_ahead = nxt, nxt_behind, nxt_ahead


def run_steps(chains, extras, ncol):
    for s in range(STEPS):
        for chain, extra in zip(chains, extras):
            sweep(chain[s], chain[s + 1], ncol, extra if s == 0 else None)


def chain_of(src, out, first, second):
    return [src] + [first if s % 2 == 0 else second for s in range(STEPS - 1)] + [out]


def main_kernel(pos_ref, *refs):
    incs = refs[:-4]
    noise_ref, out_ref, first, second = refs[-4:]
    ncol = noise_ref.shape[-1] // LANES
    chains = [chain_of(incs[k].at[0], out_ref.at[k], first.at[k], second.at[k]) for k in range(len(incs))]
    extras = [noise_ref.at[k] for k in range(len(incs))]
    run_steps(chains, extras, ncol)


def main_forecast(position, incoming, noise):
    per_dev, nf, rows, cols = noise.shape
    group = PAIR if per_dev % PAIR == 0 else 1

    def row_map(k):
        return lambda i, pos: (pos[i * group + k], 0, 0, 0)

    in_specs = [pl.BlockSpec((1, nf, rows, cols), row_map(k)) for k in range(group)]
    spec = pl.BlockSpec((group, nf, rows, cols), lambda i, pos: (i, 0, 0, 0))
    grid_spec = pltpu.PrefetchScalarGridSpec(
        num_scalar_prefetch=1,
        grid=(per_dev // group,),
        in_specs=in_specs + [spec],
        out_specs=spec,
        scratch_shapes=[pltpu.VMEM((group, nf, rows, cols), jnp.float32)] * 2,
    )
    return pl.pallas_call(
        main_kernel,
        grid_spec=grid_spec,
        out_shape=jax.ShapeDtypeStruct(noise.shape, noise.dtype),
    )(position, *([incoming] * group), noise)


def edge_kernel(lblk, rblk, from_left, from_right, body_ref, out_ref, packed, first, second, result):
    side = pl.program_id(0)
    rows = lblk.shape[-2]
    group = packed.shape[0]
    lane = lax.broadcasted_iota(jnp.int32, (rows, LANES), 1)
    half = LANES // 2
    width = STEPS

    @pl.when(side == 0)
    def _():
        def block(g, carry):
            base = g * group
            for k in range(group):
                i = base + k
                for f in range(3):
                    left = jnp.where(lane >= LANES - width, from_left[i, f], lblk[i, f])
                    right = jnp.where(lane < width, from_right[i, f], rblk[i, f])
                    right = pltpu.roll(right, half, 1)
                    keep_left = (lane < 2 * width) | (lane >= LANES - width)
                    packed[k, f] = jnp.where(keep_left, left, right)
            chains = [
                chain_of(packed.at[k], result.at[base + k], first.at[k], second.at[k]) for k in range(group)
            ]
            run_steps(chains, [None] * group, 1)
            return carry

        lax.fori_loop(0, lblk.shape[0] // group, block, 0)
        out_ref[...] = jnp.where(lane < width, result[...], body_ref[...])

    @pl.when(side == 1)
    def _():
        def particle(i, carry):
            for f in range(3):
                out_ref[i, f] = jnp.where(
                    lane >= LANES - width, pltpu.roll(result[i, f], half, 1), body_ref[i, f]
                )
            return carry

        lax.fori_loop(0, lblk.shape[0], particle, 0)


def edge_fix(lblk, rblk, from_left, from_right, body):
    per_dev, nf, rows, cols = body.shape
    ncol = cols // LANES
    group = EDGE_GROUP if per_dev % EDGE_GROUP == 0 else 1
    whole = pl.BlockSpec((per_dev, nf, rows, LANES), lambda s: (0, 0, 0, 0))
    edge = pl.BlockSpec((per_dev, nf, rows, LANES), lambda s: (0, 0, 0, s * (ncol - 1)))
    return pl.pallas_call(
        edge_kernel,
        grid=(2,),
        in_specs=[whole, whole, whole, whole, edge],
        out_specs=edge,
        out_shape=jax.ShapeDtypeStruct(body.shape, body.dtype),
        scratch_shapes=[
            pltpu.VMEM((group, nf, rows, LANES), jnp.float32),
            pltpu.VMEM((group, nf, rows, LANES), jnp.float32),
            pltpu.VMEM((group, nf, rows, LANES), jnp.float32),
            pltpu.VMEM((per_dev, nf, rows, LANES), jnp.float32),
        ],
        input_output_aliases={4: 0},
    )(lblk, rblk, from_left, from_right, body)


def shards(state, noise, parents):
    count = lax.axis_size("ens")
    me = lax.axis_index("ens")
    per_dev = state.shape[0]
    dist = max(1, -(-per_dev // count))
    send_index, position = routing(parents, count, per_dev, dist, me)
    outgoing = jnp.take(state, send_index, axis=0, mode="clip")
    incoming = lax.all_to_all(outgoing, "ens", split_axis=0, concat_axis=0, tiled=True)
    lblk = jnp.take(incoming[..., :LANES], position, axis=0, mode="clip") + noise[..., :LANES]
    rblk = jnp.take(incoming[..., -LANES:], position, axis=0, mode="clip") + noise[..., -LANES:]
    ring = lax.axis_size("col")
    from_left = lax.ppermute(rblk, "col", [(i, (i + 1) % ring) for i in range(ring)])
    from_right = lax.ppermute(lblk, "col", [(i, (i - 1) % ring) for i in range(ring)])
    body = main_forecast(position, incoming, noise)
    return edge_fix(lblk, rblk, from_left, from_right, body)


def solution(mesh):
    placed = (P("ens", None, None, "col"), P("ens", None, None, "col"), P())
    return jax.shard_map(
        shards, mesh=mesh, in_specs=placed, out_specs=P("ens", None, None, "col"), check_vma=False
    )
```

```python
import jax
import jax.numpy as jnp
from jax import lax
from jax.experimental import pallas as pl
from jax.experimental.pallas import tpu as pltpu
from jax.sharding import PartitionSpec as P

STEPS = 4
LANES = 128
PAIR = 2
EDGE_GROUP = 32
GATHER_GROUP = 8

time_step = 0.3
coriolis = 0.2
gravity = 1.0


def routing(parents, count, per_dev, dist, me):
    blocks = parents.reshape(count, per_dev)
    owner = blocks // per_dev
    local = blocks % per_dev
    ids = jnp.arange(per_dev, dtype=jnp.int32)
    same = blocks[:, :, None] == blocks[:, None, :]
    earlier = ids[None, :] < ids[:, None]
    first = jnp.logical_not(jnp.any(same & earlier[None], axis=2))
    below = (
        (owner[:, :, None] == owner[:, None, :])
        & (blocks[:, None, :] < blocks[:, :, None])
        & first[:, None, :]
    )
    slot = jnp.sum(below.astype(jnp.int32), axis=2)
    slots = jnp.arange(dist, dtype=jnp.int32)
    pick = (owner == me)[:, None, :] & first[:, None, :] & (slot[:, None, :] == slots[None, :, None])
    send_index = jnp.sum(pick.astype(jnp.int32) * local[:, None, :], axis=2).reshape(-1)
    my_owner = lax.dynamic_index_in_dim(owner, me, 0, keepdims=False)
    my_slot = lax.dynamic_index_in_dim(slot, me, 0, keepdims=False)
    return send_index, my_owner * dist + my_slot


def sweep(src, dst, ncol, extra=None):
    rows = src.shape[-2]
    lane = lax.broadcasted_iota(jnp.int32, (rows, LANES), 1)
    first_lane = lane == 0
    last_lane = lane == LANES - 1

    def load(j):
        window = pl.ds((j % ncol) * LANES, LANES)
        e = src[0, :, window]
        u = src[1, :, window]
        v = src[2, :, window]
        if extra is not None:
            e = e + extra[0, :, window]
            u = u + extra[1, :, window]
            v = v + extra[2, :, window]
        depth = 1.0 + e
        return e, u, v, depth

    def ahead(vals):
        e, u, v, depth = vals
        return tuple(pltpu.roll(a, LANES - 1, 1) for a in (e, u, v, depth * u))

    def behind(vals):
        e, u, v, depth = vals
        return tuple(pltpu.roll(a, 1, 1) for a in (e, u, v, depth * u))

    def yp(a):
        return pltpu.roll(a, rows - 1, 0)

    def ym(a):
        return pltpu.roll(a, 1, 0)

    here = load(0)
    prev_behind = behind(load(ncol - 1)) if ncol > 1 else behind(here)
    here_behind = behind(here)
    here_ahead = ahead(here)
    for j in range(ncol):
        if ncol > 1:
            nxt = load(j + 1)
            nxt_ahead = ahead(nxt)
            nxt_behind = behind(nxt)
        else:
            nxt, nxt_ahead, nxt_behind = here, here_ahead, here_behind
        xp = [jnp.where(last_lane, a, b) for a, b in zip(nxt_ahead, here_ahead)]
        xm = [jnp.where(first_lane, a, b) for a, b in zip(prev_behind, here_behind)]
        e, u, v, depth = here
        e_xp, u_xp, v_xp, hu_xp = xp
        e_xm, u_xm, v_xm, hu_xm = xm
        hv = depth * v
        e_yp, e_ym = yp(e), ym(e)
        u_yp, u_ym = yp(u), ym(u)
        v_yp, v_ym = yp(v), ym(v)
        hv_yp, hv_ym = yp(hv), ym(hv)
        half_step = 0.5 * time_step
        new_e = 0.25 * (e_xp + e_xm + e_yp + e_ym) - half_step * ((hu_xp - hu_xm) + (hv_yp - hv_ym))
        new_u = (
            0.25 * (u_xp + u_xm + u_yp + u_ym)
            - half_step * (u * (u_xp - u_xm) + v * (u_yp - u_ym) + gravity * (e_xp - e_xm))
            + (time_step * coriolis) * v
        )
        new_v = (
            0.25 * (v_xp + v_xm + v_yp + v_ym)
            - half_step * (u * (v_xp - v_xm) + v * (v_yp - v_ym) + gravity * (e_yp - e_ym))
            - (time_step * coriolis) * u
        )
        window = pl.ds(j * LANES, LANES)
        dst[0, :, window] = new_e
        dst[1, :, window] = new_u
        dst[2, :, window] = new_v
        prev_behind = here_behind
        here, here_behind, here_ahead = nxt, nxt_behind, nxt_ahead


def run_steps(chains, extras, ncol):
    for s in range(STEPS):
        for chain, extra in zip(chains, extras):
            sweep(chain[s], chain[s + 1], ncol, extra if s == 0 else None)


def chain_of(src, out, first, second):
    return [src] + [first if s % 2 == 0 else second for s in range(STEPS - 1)] + [out]


def main_kernel(pos_ref, *refs):
    incs = refs[:-4]
    noise_ref, out_ref, first, second = refs[-4:]
    ncol = noise_ref.shape[-1] // LANES
    chains = [chain_of(incs[k].at[0], out_ref.at[k], first.at[k], second.at[k]) for k in range(len(incs))]
    extras = [noise_ref.at[k] for k in range(len(incs))]
    run_steps(chains, extras, ncol)


def main_forecast(position, incoming, noise):
    per_dev, nf, rows, cols = noise.shape
    group = PAIR if per_dev % PAIR == 0 else 1

    def row_map(k):
        return lambda i, pos: (pos[i * group + k], 0, 0, 0)

    in_specs = [pl.BlockSpec((1, nf, rows, cols), row_map(k)) for k in range(group)]
    spec = pl.BlockSpec((group, nf, rows, cols), lambda i, pos: (i, 0, 0, 0))
    grid_spec = pltpu.PrefetchScalarGridSpec(
        num_scalar_prefetch=1,
        grid=(per_dev // group,),
        in_specs=in_specs + [spec],
        out_specs=spec,
        scratch_shapes=[pltpu.VMEM((group, nf, rows, cols), jnp.float32)] * 2,
    )
    return pl.pallas_call(
        main_kernel,
        grid_spec=grid_spec,
        out_shape=jax.ShapeDtypeStruct(noise.shape, noise.dtype),
    )(position, *([incoming] * group), noise)


def edges_kernel(pos_ref, *refs):
    group = (len(refs) - 4) // 2
    left_rows, right_rows = refs[:group], refs[group:2 * group]
    noise_left, noise_right, lblk, rblk = refs[2 * group:]
    for k in range(group):
        lblk[k] = left_rows[k][0] + noise_left[k]
        rblk[k] = right_rows[k][0] + noise_right[k]


def edge_blocks(position, incoming, noise):
    per_dev, nf, rows, cols = noise.shape
    last = cols // LANES - 1
    group = GATHER_GROUP if per_dev % GATHER_GROUP == 0 else 1

    def row_map(k, col):
        return lambda i, pos: (pos[i * group + k], 0, 0, col)

    left_specs = [pl.BlockSpec((1, nf, rows, LANES), row_map(k, 0)) for k in range(group)]
    right_specs = [pl.BlockSpec((1, nf, rows, LANES), row_map(k, last)) for k in range(group)]
    left = pl.BlockSpec((group, nf, rows, LANES), lambda i, pos: (i, 0, 0, 0))
    right = pl.BlockSpec((group, nf, rows, LANES), lambda i, pos: (i, 0, 0, last))
    out = pl.BlockSpec((group, nf, rows, LANES), lambda i, pos: (i, 0, 0, 0))
    edge_shape = jax.ShapeDtypeStruct((per_dev, nf, rows, LANES), noise.dtype)
    grid_spec = pltpu.PrefetchScalarGridSpec(
        num_scalar_prefetch=1,
        grid=(per_dev // group,),
        in_specs=left_specs + right_specs + [left, right],
        out_specs=[out, out],
    )
    return pl.pallas_call(
        edges_kernel,
        grid_spec=grid_spec,
        out_shape=[edge_shape, edge_shape],
    )(position, *([incoming] * (2 * group)), noise, noise)


def edge_kernel(lblk, rblk, from_left, from_right, body_ref, out_ref, packed, first, second, result):
    side = pl.program_id(0)
    rows = lblk.shape[-2]
    group = packed.shape[0]
    lane = lax.broadcasted_iota(jnp.int32, (rows, LANES), 1)
    half = LANES // 2
    width = STEPS

    @pl.when(side == 0)
    def _():
        def block(g, carry):
            base = g * group
            for k in range(group):
                i = base + k
                for f in range(3):
                    left = jnp.where(lane >= LANES - width, from_left[i, f], lblk[i, f])
                    right = jnp.where(lane < width, from_right[i, f], rblk[i, f])
                    right = pltpu.roll(right, half, 1)
                    keep_left = (lane < 2 * width) | (lane >= LANES - width)
                    packed[k, f] = jnp.where(keep_left, left, right)
            chains = [
                chain_of(packed.at[k], result.at[base + k], first.at[k], second.at[k]) for k in range(group)
            ]
            run_steps(chains, [None] * group, 1)
            return carry

        lax.fori_loop(0, lblk.shape[0] // group, block, 0)
        out_ref[...] = jnp.where(lane < width, result[...], body_ref[...])

    @pl.when(side == 1)
    def _():
        def particle(i, carry):
            for f in range(3):
                out_ref[i, f] = jnp.where(
                    lane >= LANES - width, pltpu.roll(result[i, f], half, 1), body_ref[i, f]
                )
            return carry

        lax.fori_loop(0, lblk.shape[0], particle, 0)


def edge_fix(lblk, rblk, from_left, from_right, body):
    per_dev, nf, rows, cols = body.shape
    ncol = cols // LANES
    group = EDGE_GROUP if per_dev % EDGE_GROUP == 0 else 1
    whole = pl.BlockSpec((per_dev, nf, rows, LANES), lambda s: (0, 0, 0, 0))
    edge = pl.BlockSpec((per_dev, nf, rows, LANES), lambda s: (0, 0, 0, s * (ncol - 1)))
    return pl.pallas_call(
        edge_kernel,
        grid=(2,),
        in_specs=[whole, whole, whole, whole, edge],
        out_specs=edge,
        out_shape=jax.ShapeDtypeStruct(body.shape, body.dtype),
        scratch_shapes=[
            pltpu.VMEM((group, nf, rows, LANES), jnp.float32),
            pltpu.VMEM((group, nf, rows, LANES), jnp.float32),
            pltpu.VMEM((group, nf, rows, LANES), jnp.float32),
            pltpu.VMEM((per_dev, nf, rows, LANES), jnp.float32),
        ],
        input_output_aliases={4: 0},
    )(lblk, rblk, from_left, from_right, body)


def shards(state, noise, parents):
    count = lax.axis_size("ens")
    me = lax.axis_index("ens")
    per_dev = state.shape[0]
    dist = max(1, -(-per_dev // count))
    send_index, position = routing(parents, count, per_dev, dist, me)
    outgoing = jnp.take(state, send_index, axis=0, mode="clip")
    incoming = lax.all_to_all(outgoing, "ens", split_axis=0, concat_axis=0, tiled=True)
    lblk, rblk = edge_blocks(position, incoming, noise)
    ring = lax.axis_size("col")
    from_left = lax.ppermute(rblk, "col", [(i, (i + 1) % ring) for i in range(ring)])
    from_right = lax.ppermute(lblk, "col", [(i, (i - 1) % ring) for i in range(ring)])
    body = main_forecast(position, incoming, noise)
    return edge_fix(lblk, rblk, from_left, from_right, body)


def solution(mesh):
    placed = (P("ens", None, None, "col"), P("ens", None, None, "col"), P())
    return jax.shard_map(
        shards, mesh=mesh, in_specs=placed, out_specs=P("ens", None, None, "col"), check_vma=False
    )
```

```python
import jax
import jax.numpy as jnp
from jax import lax
from jax.experimental import pallas as pl
from jax.experimental.pallas import tpu as pltpu
from jax.sharding import PartitionSpec as P

STEPS = 4
LANES = 128
PAIR = 2
EDGE_GROUP = 8
GATHER_GROUP = 32

time_step = 0.3
coriolis = 0.2
gravity = 1.0


def routing(parents, count, per_dev, dist, me):
    blocks = parents.reshape(count, per_dev)
    owner = blocks // per_dev
    local = blocks % per_dev
    ids = jnp.arange(per_dev, dtype=jnp.int32)
    same = blocks[:, :, None] == blocks[:, None, :]
    earlier = ids[None, :] < ids[:, None]
    first = jnp.logical_not(jnp.any(same & earlier[None], axis=2))
    below = (
        (owner[:, :, None] == owner[:, None, :])
        & (blocks[:, None, :] < blocks[:, :, None])
        & first[:, None, :]
    )
    slot = jnp.sum(below.astype(jnp.int32), axis=2)
    slots = jnp.arange(dist, dtype=jnp.int32)
    pick = (owner == me)[:, None, :] & first[:, None, :] & (slot[:, None, :] == slots[None, :, None])
    send_index = jnp.sum(pick.astype(jnp.int32) * local[:, None, :], axis=2).reshape(-1)
    my_owner = lax.dynamic_index_in_dim(owner, me, 0, keepdims=False)
    my_slot = lax.dynamic_index_in_dim(slot, me, 0, keepdims=False)
    return send_index, my_owner * dist + my_slot


def update(e, u, v, depth, xp, xm):
    rows = e.shape[-2]

    def yp(a):
        return pltpu.roll(a, rows - 1, 0)

    def ym(a):
        return pltpu.roll(a, 1, 0)

    e_xp, u_xp, v_xp, hu_xp = xp
    e_xm, u_xm, v_xm, hu_xm = xm
    hv = depth * v
    e_yp, e_ym = yp(e), ym(e)
    u_yp, u_ym = yp(u), ym(u)
    v_yp, v_ym = yp(v), ym(v)
    hv_yp, hv_ym = yp(hv), ym(hv)
    half_step = 0.5 * time_step
    new_e = 0.25 * (e_xp + e_xm + e_yp + e_ym) - half_step * ((hu_xp - hu_xm) + (hv_yp - hv_ym))
    new_u = (
        0.25 * (u_xp + u_xm + u_yp + u_ym)
        - half_step * (u * (u_xp - u_xm) + v * (u_yp - u_ym) + gravity * (e_xp - e_xm))
        + (time_step * coriolis) * v
    )
    new_v = (
        0.25 * (v_xp + v_xm + v_yp + v_ym)
        - half_step * (u * (v_xp - v_xm) + v * (v_yp - v_ym) + gravity * (e_yp - e_ym))
        - (time_step * coriolis) * u
    )
    return new_e, new_u, new_v


def advance_vreg(e, u, v):
    depth = 1.0 + e
    hu = depth * u
    xp = tuple(pltpu.roll(a, LANES - 1, 1) for a in (e, u, v, hu))
    xm = tuple(pltpu.roll(a, 1, 1) for a in (e, u, v, hu))
    return update(e, u, v, depth, xp, xm)


def sweep(src, dst, ncol, extra=None):
    rows = src.shape[-2]
    lane = lax.broadcasted_iota(jnp.int32, (rows, LANES), 1)
    first_lane = lane == 0
    last_lane = lane == LANES - 1

    def load(j):
        window = pl.ds((j % ncol) * LANES, LANES)
        e = src[0, :, window]
        u = src[1, :, window]
        v = src[2, :, window]
        if extra is not None:
            e = e + extra[0, :, window]
            u = u + extra[1, :, window]
            v = v + extra[2, :, window]
        depth = 1.0 + e
        return e, u, v, depth, depth * u

    def ahead(vals):
        e, u, v, depth, hu = vals
        return tuple(pltpu.roll(a, LANES - 1, 1) for a in (e, u, v, hu))

    def behind(vals):
        e, u, v, depth, hu = vals
        return tuple(pltpu.roll(a, 1, 1) for a in (e, u, v, hu))

    here = load(0)
    prev_behind = behind(load(ncol - 1)) if ncol > 1 else behind(here)
    here_behind = behind(here)
    here_ahead = ahead(here)
    for j in range(ncol):
        if ncol > 1:
            nxt = load(j + 1)
            nxt_ahead = ahead(nxt)
            nxt_behind = behind(nxt)
        else:
            nxt, nxt_ahead, nxt_behind = here, here_ahead, here_behind
        xp = [jnp.where(last_lane, a, b) for a, b in zip(nxt_ahead, here_ahead)]
        xm = [jnp.where(first_lane, a, b) for a, b in zip(prev_behind, here_behind)]
        e, u, v, depth, _ = here
        new_e, new_u, new_v = update(e, u, v, depth, xp, xm)
        window = pl.ds(j * LANES, LANES)
        dst[0, :, window] = new_e
        dst[1, :, window] = new_u
        dst[2, :, window] = new_v
        prev_behind = here_behind
        here, here_behind, here_ahead = nxt, nxt_behind, nxt_ahead


def run_steps(chains, extras, ncol):
    for s in range(STEPS):
        for chain, extra in zip(chains, extras):
            sweep(chain[s], chain[s + 1], ncol, extra if s == 0 else None)


def chain_of(src, out, first, second):
    return [src] + [first if s % 2 == 0 else second for s in range(STEPS - 1)] + [out]


def main_kernel(pos_ref, *refs):
    incs = refs[:-4]
    noise_ref, out_ref, first, second = refs[-4:]
    ncol = noise_ref.shape[-1] // LANES
    chains = [chain_of(incs[k].at[0], out_ref.at[k], first.at[k], second.at[k]) for k in range(len(incs))]
    extras = [noise_ref.at[k] for k in range(len(incs))]
    run_steps(chains, extras, ncol)


def main_forecast(position, incoming, noise):
    per_dev, nf, rows, cols = noise.shape
    group = PAIR if per_dev % PAIR == 0 else 1

    def row_map(k):
        return lambda i, pos: (pos[i * group + k], 0, 0, 0)

    in_specs = [pl.BlockSpec((1, nf, rows, cols), row_map(k)) for k in range(group)]
    spec = pl.BlockSpec((group, nf, rows, cols), lambda i, pos: (i, 0, 0, 0))
    grid_spec = pltpu.PrefetchScalarGridSpec(
        num_scalar_prefetch=1,
        grid=(per_dev // group,),
        in_specs=in_specs + [spec],
        out_specs=spec,
        scratch_shapes=[pltpu.VMEM((group, nf, rows, cols), jnp.float32)] * 2,
    )
    return pl.pallas_call(
        main_kernel,
        grid_spec=grid_spec,
        out_shape=jax.ShapeDtypeStruct(noise.shape, noise.dtype),
    )(position, *([incoming] * group), noise)


def edges_kernel(pos_ref, *refs):
    group = (len(refs) - 4) // 2
    left_rows, right_rows = refs[:group], refs[group:2 * group]
    noise_left, noise_right, lblk, rblk = refs[2 * group:]
    for k in range(group):
        lblk[k] = left_rows[k][0] + noise_left[k]
        rblk[k] = right_rows[k][0] + noise_right[k]


def edge_blocks(position, incoming, noise):
    per_dev, nf, rows, cols = noise.shape
    last = cols // LANES - 1
    group = GATHER_GROUP if per_dev % GATHER_GROUP == 0 else 1

    def row_map(k, col):
        return lambda i, pos: (pos[i * group + k], 0, 0, col)

    left_specs = [pl.BlockSpec((1, nf, rows, LANES), row_map(k, 0)) for k in range(group)]
    right_specs = [pl.BlockSpec((1, nf, rows, LANES), row_map(k, last)) for k in range(group)]
    left = pl.BlockSpec((group, nf, rows, LANES), lambda i, pos: (i, 0, 0, 0))
    right = pl.BlockSpec((group, nf, rows, LANES), lambda i, pos: (i, 0, 0, last))
    out = pl.BlockSpec((group, nf, rows, LANES), lambda i, pos: (i, 0, 0, 0))
    edge_shape = jax.ShapeDtypeStruct((per_dev, nf, rows, LANES), noise.dtype)
    grid_spec = pltpu.PrefetchScalarGridSpec(
        num_scalar_prefetch=1,
        grid=(per_dev // group,),
        in_specs=left_specs + right_specs + [left, right],
        out_specs=[out, out],
    )
    return pl.pallas_call(
        edges_kernel,
        grid_spec=grid_spec,
        out_shape=[edge_shape, edge_shape],
    )(position, *([incoming] * (2 * group)), noise, noise)


def edge_kernel(lblk, rblk, from_left, from_right, body_ref, out_ref, packed, first, second, result):
    side = pl.program_id(0)
    rows = lblk.shape[-2]
    group = packed.shape[0]
    lane = lax.broadcasted_iota(jnp.int32, (rows, LANES), 1)
    half = LANES // 2
    width = STEPS

    @pl.when(side == 0)
    def _():
        def block(g, carry):
            base = g * group
            for k in range(group):
                i = base + k
                fields = []
                for f in range(3):
                    left = jnp.where(lane >= LANES - width, from_left[i, f], lblk[i, f])
                    right = jnp.where(lane < width, from_right[i, f], rblk[i, f])
                    right = pltpu.roll(right, half, 1)
                    keep_left = (lane < 2 * width) | (lane >= LANES - width)
                    fields.append(jnp.where(keep_left, left, right))
                e, u, v = fields
                for _ in range(STEPS):
                    e, u, v = advance_vreg(e, u, v)
                result[i, 0] = e
                result[i, 1] = u
                result[i, 2] = v
            return carry

        lax.fori_loop(0, lblk.shape[0] // group, block, 0)
        out_ref[...] = jnp.where(lane < width, result[...], body_ref[...])

    @pl.when(side == 1)
    def _():
        def particle(i, carry):
            for f in range(3):
                out_ref[i, f] = jnp.where(
                    lane >= LANES - width, pltpu.roll(result[i, f], half, 1), body_ref[i, f]
                )
            return carry

        lax.fori_loop(0, lblk.shape[0], particle, 0)


def edge_fix(lblk, rblk, from_left, from_right, body):
    per_dev, nf, rows, cols = body.shape
    ncol = cols // LANES
    group = EDGE_GROUP if per_dev % EDGE_GROUP == 0 else 1
    whole = pl.BlockSpec((per_dev, nf, rows, LANES), lambda s: (0, 0, 0, 0))
    edge = pl.BlockSpec((per_dev, nf, rows, LANES), lambda s: (0, 0, 0, s * (ncol - 1)))
    return pl.pallas_call(
        edge_kernel,
        grid=(2,),
        in_specs=[whole, whole, whole, whole, edge],
        out_specs=edge,
        out_shape=jax.ShapeDtypeStruct(body.shape, body.dtype),
        scratch_shapes=[
            pltpu.VMEM((group, nf, rows, LANES), jnp.float32),
            pltpu.VMEM((group, nf, rows, LANES), jnp.float32),
            pltpu.VMEM((group, nf, rows, LANES), jnp.float32),
            pltpu.VMEM((per_dev, nf, rows, LANES), jnp.float32),
        ],
        input_output_aliases={4: 0},
    )(lblk, rblk, from_left, from_right, body)


def shards(state, noise, parents):
    count = lax.axis_size("ens")
    me = lax.axis_index("ens")
    per_dev = state.shape[0]
    dist = max(1, -(-per_dev // count))
    send_index, position = routing(parents, count, per_dev, dist, me)
    outgoing = jnp.take(state, send_index, axis=0, mode="clip")
    incoming = lax.all_to_all(outgoing, "ens", split_axis=0, concat_axis=0, tiled=True)
    lblk, rblk = edge_blocks(position, incoming, noise)
    ring = lax.axis_size("col")
    from_left = lax.ppermute(rblk, "col", [(i, (i + 1) % ring) for i in range(ring)])
    from_right = lax.ppermute(lblk, "col", [(i, (i - 1) % ring) for i in range(ring)])
    body = main_forecast(position, incoming, noise)
    return edge_fix(lblk, rblk, from_left, from_right, body)


def solution(mesh):
    placed = (P("ens", None, None, "col"), P("ens", None, None, "col"), P())
    return jax.shard_map(
        shards, mesh=mesh, in_specs=placed, out_specs=P("ens", None, None, "col"), check_vma=False
    )
```

```python
import jax
import jax.numpy as jnp
from jax import lax
from jax.experimental import pallas as pl
from jax.experimental.pallas import tpu as pltpu
from jax.sharding import PartitionSpec as P

STEPS = 4
LANES = 128
PAIR = 2
EDGE_GROUP = 8
GATHER_GROUP = 32

time_step = 0.3
coriolis = 0.2
gravity = 1.0


def routing(parents, count, per_dev, dist, me):
    blocks = parents.reshape(count, per_dev)
    owner = blocks // per_dev
    local = blocks % per_dev
    ids = jnp.arange(per_dev, dtype=jnp.int32)
    same = blocks[:, :, None] == blocks[:, None, :]
    earlier = ids[None, :] < ids[:, None]
    first = jnp.logical_not(jnp.any(same & earlier[None], axis=2))
    below = (
        (owner[:, :, None] == owner[:, None, :])
        & (blocks[:, None, :] < blocks[:, :, None])
        & first[:, None, :]
    )
    slot = jnp.sum(below.astype(jnp.int32), axis=2)
    slots = jnp.arange(dist, dtype=jnp.int32)
    pick = (owner == me)[:, None, :] & first[:, None, :] & (slot[:, None, :] == slots[None, :, None])
    send_index = jnp.sum(pick.astype(jnp.int32) * local[:, None, :], axis=2).reshape(-1)
    my_owner = lax.dynamic_index_in_dim(owner, me, 0, keepdims=False)
    my_slot = lax.dynamic_index_in_dim(slot, me, 0, keepdims=False)
    return send_index, my_owner * dist + my_slot


def update(e, u, v, xp, xm):
    rows = e.shape[-2]

    def yp(a):
        return pltpu.roll(a, rows - 1, 0)

    def ym(a):
        return pltpu.roll(a, 1, 0)

    e_xp, u_xp, v_xp = xp
    e_xm, u_xm, v_xm = xm
    e_yp, e_ym = yp(e), ym(e)
    u_yp, u_ym = yp(u), ym(u)
    v_yp, v_ym = yp(v), ym(v)
    hu_xp = (1.0 + e_xp) * u_xp
    hu_xm = (1.0 + e_xm) * u_xm
    hv_yp = (1.0 + e_yp) * v_yp
    hv_ym = (1.0 + e_ym) * v_ym
    half_step = 0.5 * time_step
    new_e = 0.25 * (e_xp + e_xm + e_yp + e_ym) - half_step * ((hu_xp - hu_xm) + (hv_yp - hv_ym))
    new_u = (
        0.25 * (u_xp + u_xm + u_yp + u_ym)
        - half_step * (u * (u_xp - u_xm) + v * (u_yp - u_ym) + gravity * (e_xp - e_xm))
        + (time_step * coriolis) * v
    )
    new_v = (
        0.25 * (v_xp + v_xm + v_yp + v_ym)
        - half_step * (u * (v_xp - v_xm) + v * (v_yp - v_ym) + gravity * (e_yp - e_ym))
        - (time_step * coriolis) * u
    )
    return new_e, new_u, new_v


def advance_vreg(e, u, v):
    xp = tuple(pltpu.roll(a, LANES - 1, 1) for a in (e, u, v))
    xm = tuple(pltpu.roll(a, 1, 1) for a in (e, u, v))
    return update(e, u, v, xp, xm)


def sweep(src, dst, ncol, extra=None):
    rows = src.shape[-2]
    lane = lax.broadcasted_iota(jnp.int32, (rows, LANES), 1)
    first_lane = lane == 0
    last_lane = lane == LANES - 1

    def load(j):
        window = pl.ds((j % ncol) * LANES, LANES)
        e = src[0, :, window]
        u = src[1, :, window]
        v = src[2, :, window]
        if extra is not None:
            e = e + extra[0, :, window]
            u = u + extra[1, :, window]
            v = v + extra[2, :, window]
        return e, u, v

    def ahead(vals):
        return tuple(pltpu.roll(a, LANES - 1, 1) for a in vals)

    def behind(vals):
        return tuple(pltpu.roll(a, 1, 1) for a in vals)

    here = load(0)
    prev_behind = behind(load(ncol - 1)) if ncol > 1 else behind(here)
    here_behind = behind(here)
    here_ahead = ahead(here)
    for j in range(ncol):
        if ncol > 1:
            nxt = load(j + 1)
            nxt_ahead = ahead(nxt)
            nxt_behind = behind(nxt)
        else:
            nxt, nxt_ahead, nxt_behind = here, here_ahead, here_behind
        xp = [jnp.where(last_lane, a, b) for a, b in zip(nxt_ahead, here_ahead)]
        xm = [jnp.where(first_lane, a, b) for a, b in zip(prev_behind, here_behind)]
        e, u, v = here
        new_e, new_u, new_v = update(e, u, v, xp, xm)
        window = pl.ds(j * LANES, LANES)
        dst[0, :, window] = new_e
        dst[1, :, window] = new_u
        dst[2, :, window] = new_v
        prev_behind = here_behind
        here, here_behind, here_ahead = nxt, nxt_behind, nxt_ahead


def run_steps(chains, extras, ncol):
    for s in range(STEPS):
        for chain, extra in zip(chains, extras):
            sweep(chain[s], chain[s + 1], ncol, extra if s == 0 else None)


def chain_of(src, out, first, second):
    return [src] + [first if s % 2 == 0 else second for s in range(STEPS - 1)] + [out]


def main_kernel(pos_ref, *refs):
    incs = refs[:-4]
    noise_ref, out_ref, first, second = refs[-4:]
    ncol = noise_ref.shape[-1] // LANES
    chains = [chain_of(incs[k].at[0], out_ref.at[k], first.at[k], second.at[k]) for k in range(len(incs))]
    extras = [noise_ref.at[k] for k in range(len(incs))]
    run_steps(chains, extras, ncol)


def main_forecast(position, incoming, noise):
    per_dev, nf, rows, cols = noise.shape
    group = PAIR if per_dev % PAIR == 0 else 1

    def row_map(k):
        return lambda i, pos: (pos[i * group + k], 0, 0, 0)

    in_specs = [pl.BlockSpec((1, nf, rows, cols), row_map(k)) for k in range(group)]
    spec = pl.BlockSpec((group, nf, rows, cols), lambda i, pos: (i, 0, 0, 0))
    grid_spec = pltpu.PrefetchScalarGridSpec(
        num_scalar_prefetch=1,
        grid=(per_dev // group,),
        in_specs=in_specs + [spec],
        out_specs=spec,
        scratch_shapes=[pltpu.VMEM((group, nf, rows, cols), jnp.float32)] * 2,
    )
    return pl.pallas_call(
        main_kernel,
        grid_spec=grid_spec,
        out_shape=jax.ShapeDtypeStruct(noise.shape, noise.dtype),
    )(position, *([incoming] * group), noise)


def edges_kernel(pos_ref, *refs):
    group = (len(refs) - 4) // 2
    left_rows, right_rows = refs[:group], refs[group:2 * group]
    noise_left, noise_right, lblk, rblk = refs[2 * group:]
    for k in range(group):
        lblk[k] = left_rows[k][0] + noise_left[k]
        rblk[k] = right_rows[k][0] + noise_right[k]


def edge_blocks(position, incoming, noise):
    per_dev, nf, rows, cols = noise.shape
    last = cols // LANES - 1
    group = GATHER_GROUP if per_dev % GATHER_GROUP == 0 else 1

    def row_map(k, col):
        return lambda i, pos: (pos[i * group + k], 0, 0, col)

    left_specs = [pl.BlockSpec((1, nf, rows, LANES), row_map(k, 0)) for k in range(group)]
    right_specs = [pl.BlockSpec((1, nf, rows, LANES), row_map(k, last)) for k in range(group)]
    left = pl.BlockSpec((group, nf, rows, LANES), lambda i, pos: (i, 0, 0, 0))
    right = pl.BlockSpec((group, nf, rows, LANES), lambda i, pos: (i, 0, 0, last))
    out = pl.BlockSpec((group, nf, rows, LANES), lambda i, pos: (i, 0, 0, 0))
    edge_shape = jax.ShapeDtypeStruct((per_dev, nf, rows, LANES), noise.dtype)
    grid_spec = pltpu.PrefetchScalarGridSpec(
        num_scalar_prefetch=1,
        grid=(per_dev // group,),
        in_specs=left_specs + right_specs + [left, right],
        out_specs=[out, out],
    )
    return pl.pallas_call(
        edges_kernel,
        grid_spec=grid_spec,
        out_shape=[edge_shape, edge_shape],
    )(position, *([incoming] * (2 * group)), noise, noise)


def edge_kernel(lblk, rblk, from_left, from_right, body_ref, out_ref, packed, first, second, result):
    side = pl.program_id(0)
    rows = lblk.shape[-2]
    group = packed.shape[0]
    lane = lax.broadcasted_iota(jnp.int32, (rows, LANES), 1)
    half = LANES // 2
    width = STEPS

    @pl.when(side == 0)
    def _():
        def block(g, carry):
            base = g * group
            for k in range(group):
                i = base + k
                fields = []
                for f in range(3):
                    left = jnp.where(lane >= LANES - width, from_left[i, f], lblk[i, f])
                    right = jnp.where(lane < width, from_right[i, f], rblk[i, f])
                    right = pltpu.roll(right, half, 1)
                    keep_left = (lane < 2 * width) | (lane >= LANES - width)
                    fields.append(jnp.where(keep_left, left, right))
                e, u, v = fields
                for _ in range(STEPS):
                    e, u, v = advance_vreg(e, u, v)
                result[i, 0] = e
                result[i, 1] = u
                result[i, 2] = v
            return carry

        lax.fori_loop(0, lblk.shape[0] // group, block, 0)
        out_ref[...] = jnp.where(lane < width, result[...], body_ref[...])

    @pl.when(side == 1)
    def _():
        def particle(i, carry):
            for f in range(3):
                out_ref[i, f] = jnp.where(
                    lane >= LANES - width, pltpu.roll(result[i, f], half, 1), body_ref[i, f]
                )
            return carry

        lax.fori_loop(0, lblk.shape[0], particle, 0)


def edge_fix(lblk, rblk, from_left, from_right, body):
    per_dev, nf, rows, cols = body.shape
    ncol = cols // LANES
    group = EDGE_GROUP if per_dev % EDGE_GROUP == 0 else 1
    whole = pl.BlockSpec((per_dev, nf, rows, LANES), lambda s: (0, 0, 0, 0))
    edge = pl.BlockSpec((per_dev, nf, rows, LANES), lambda s: (0, 0, 0, s * (ncol - 1)))
    return pl.pallas_call(
        edge_kernel,
        grid=(2,),
        in_specs=[whole, whole, whole, whole, edge],
        out_specs=edge,
        out_shape=jax.ShapeDtypeStruct(body.shape, body.dtype),
        scratch_shapes=[
            pltpu.VMEM((group, nf, rows, LANES), jnp.float32),
            pltpu.VMEM((group, nf, rows, LANES), jnp.float32),
            pltpu.VMEM((group, nf, rows, LANES), jnp.float32),
            pltpu.VMEM((per_dev, nf, rows, LANES), jnp.float32),
        ],
        input_output_aliases={4: 0},
    )(lblk, rblk, from_left, from_right, body)


def shards(state, noise, parents):
    count = lax.axis_size("ens")
    me = lax.axis_index("ens")
    per_dev = state.shape[0]
    dist = max(1, -(-per_dev // count))
    send_index, position = routing(parents, count, per_dev, dist, me)
    outgoing = jnp.take(state, send_index, axis=0, mode="clip")
    incoming = lax.all_to_all(outgoing, "ens", split_axis=0, concat_axis=0, tiled=True)
    lblk, rblk = edge_blocks(position, incoming, noise)
    ring = lax.axis_size("col")
    from_left = lax.ppermute(rblk, "col", [(i, (i + 1) % ring) for i in range(ring)])
    from_right = lax.ppermute(lblk, "col", [(i, (i - 1) % ring) for i in range(ring)])
    body = main_forecast(position, incoming, noise)
    return edge_fix(lblk, rblk, from_left, from_right, body)


def solution(mesh):
    placed = (P("ens", None, None, "col"), P("ens", None, None, "col"), P())
    return jax.shard_map(
        shards, mesh=mesh, in_specs=placed, out_specs=P("ens", None, None, "col"), check_vma=False
    )
```

```python
import jax
import jax.numpy as jnp
from jax import lax
from jax.experimental import pallas as pl
from jax.experimental.pallas import tpu as pltpu
from jax.sharding import PartitionSpec as P

STEPS = 4
LANES = 128
PAIR = 2

time_step = 0.3
coriolis = 0.2
gravity = 1.0


def routing(parents, count, per_dev, dist, me):
    blocks = parents.reshape(count, per_dev)
    owner = blocks // per_dev
    local = blocks % per_dev
    ids = jnp.arange(per_dev, dtype=jnp.int32)
    same = blocks[:, :, None] == blocks[:, None, :]
    earlier = ids[None, :] < ids[:, None]
    first = jnp.logical_not(jnp.any(same & earlier[None], axis=2))
    below = (
        (owner[:, :, None] == owner[:, None, :])
        & (blocks[:, None, :] < blocks[:, :, None])
        & first[:, None, :]
    )
    slot = jnp.sum(below.astype(jnp.int32), axis=2)
    slots = jnp.arange(dist, dtype=jnp.int32)
    pick = (owner == me)[:, None, :] & first[:, None, :] & (slot[:, None, :] == slots[None, :, None])
    send_index = jnp.sum(pick.astype(jnp.int32) * local[:, None, :], axis=2).reshape(-1)
    my_owner = lax.dynamic_index_in_dim(owner, me, 0, keepdims=False)
    my_slot = lax.dynamic_index_in_dim(slot, me, 0, keepdims=False)
    return send_index, my_owner * dist + my_slot


def update(e, u, v, xp, xm):
    rows = e.shape[-2]

    def yp(a):
        return pltpu.roll(a, rows - 1, 0)

    def ym(a):
        return pltpu.roll(a, 1, 0)

    e_xp, u_xp, v_xp = xp
    e_xm, u_xm, v_xm = xm
    e_yp, e_ym = yp(e), ym(e)
    u_yp, u_ym = yp(u), ym(u)
    v_yp, v_ym = yp(v), ym(v)
    hu_xp = (1.0 + e_xp) * u_xp
    hu_xm = (1.0 + e_xm) * u_xm
    hv_yp = (1.0 + e_yp) * v_yp
    hv_ym = (1.0 + e_ym) * v_ym
    half_step = 0.5 * time_step
    new_e = 0.25 * (e_xp + e_xm + e_yp + e_ym) - half_step * ((hu_xp - hu_xm) + (hv_yp - hv_ym))
    new_u = (
        0.25 * (u_xp + u_xm + u_yp + u_ym)
        - half_step * (u * (u_xp - u_xm) + v * (u_yp - u_ym) + gravity * (e_xp - e_xm))
        + (time_step * coriolis) * v
    )
    new_v = (
        0.25 * (v_xp + v_xm + v_yp + v_ym)
        - half_step * (u * (v_xp - v_xm) + v * (v_yp - v_ym) + gravity * (e_yp - e_ym))
        - (time_step * coriolis) * u
    )
    return new_e, new_u, new_v


def advance_vreg(e, u, v):
    xp = tuple(pltpu.roll(a, LANES - 1, 1) for a in (e, u, v))
    xm = tuple(pltpu.roll(a, 1, 1) for a in (e, u, v))
    return update(e, u, v, xp, xm)


def sweep(load, store, ncol):
    rows = load(0)[0].shape[-2]
    lane = lax.broadcasted_iota(jnp.int32, (rows, LANES), 1)
    first_lane = lane == 0
    last_lane = lane == LANES - 1

    def fetch(j):
        return load(j % ncol)

    def ahead(vals):
        return tuple(pltpu.roll(a, LANES - 1, 1) for a in vals)

    def behind(vals):
        return tuple(pltpu.roll(a, 1, 1) for a in vals)

    here = fetch(0)
    prev_behind = behind(fetch(ncol - 1))
    here_behind = behind(here)
    here_ahead = ahead(here)
    for j in range(ncol):
        nxt = fetch(j + 1)
        nxt_ahead = ahead(nxt)
        nxt_behind = behind(nxt)
        xp = [jnp.where(last_lane, a, b) for a, b in zip(nxt_ahead, here_ahead)]
        xm = [jnp.where(first_lane, a, b) for a, b in zip(prev_behind, here_behind)]
        e, u, v = here
        store(j, update(e, u, v, xp, xm))
        prev_behind = here_behind
        here, here_behind, here_ahead = nxt, nxt_behind, nxt_ahead


def ref_loader(ref):
    def load(j):
        window = pl.ds(j * LANES, LANES)
        return tuple(ref[f, :, window] for f in range(3))

    return load


def ref_storer(ref, limit):
    def store(j, values):
        if j < limit:
            window = pl.ds(j * LANES, LANES)
            for f in range(3):
                ref[f, :, window] = values[f]

    return store


def child_loader(inc, noise, halo, ncol):
    def load(j):
        if j == ncol:
            return tuple(halo[f] for f in range(3))
        window = pl.ds(j * LANES, LANES)
        return tuple(inc[f, :, window] + noise[f, :, window] for f in range(3))

    return load


def main_kernel(pos_ref, *refs):
    incs = refs[:-5]
    noise_ref, halo_ref, out_ref, first, second = refs[-5:]
    ncol = noise_ref.shape[-1] // LANES
    wide = ncol + 1
    for s in range(STEPS):
        for k in range(len(incs)):
            if s == 0:
                load = child_loader(incs[k].at[0], noise_ref.at[k], halo_ref.at[k], ncol)
            else:
                load = ref_loader((first if s % 2 == 1 else second).at[k])
            if s == STEPS - 1:
                store = ref_storer(out_ref.at[k], ncol)
            else:
                store = ref_storer((first if s % 2 == 0 else second).at[k], wide)
            sweep(load, store, wide)


def main_forecast(position, incoming, noise, halo):
    per_dev, nf, rows, cols = noise.shape
    group = PAIR if per_dev % PAIR == 0 else 1

    def row_map(k):
        return lambda i, pos: (pos[i * group + k], 0, 0, 0)

    in_specs = [pl.BlockSpec((1, nf, rows, cols), row_map(k)) for k in range(group)]
    spec = pl.BlockSpec((group, nf, rows, cols), lambda i, pos: (i, 0, 0, 0))
    halo_spec = pl.BlockSpec((group, nf, rows, LANES), lambda i, pos: (i, 0, 0, 0))
    grid_spec = pltpu.PrefetchScalarGridSpec(
        num_scalar_prefetch=1,
        grid=(per_dev // group,),
        in_specs=in_specs + [spec, halo_spec],
        out_specs=spec,
        scratch_shapes=[pltpu.VMEM((group, nf, rows, cols + LANES), jnp.float32)] * 2,
    )
    return pl.pallas_call(
        main_kernel,
        grid_spec=grid_spec,
        out_shape=jax.ShapeDtypeStruct(noise.shape, noise.dtype),
    )(position, *([incoming] * group), noise, halo)


def halo_block(state, noise, parents, me):
    per_dev, nf, rows, cols = state.shape
    width = STEPS

    def edges(a):
        return jnp.concatenate([a[..., :width], a[..., -width:]], axis=-1).reshape(a.shape[0], -1)

    everyone = lax.all_gather(edges(state), "ens", axis=0, tiled=True)
    mine = lax.dynamic_slice_in_dim(parents, me * per_dev, per_dev)
    child_edges = jnp.take(everyone, mine, axis=0, mode="clip") + edges(noise)
    ring = lax.axis_size("col")
    from_left = lax.ppermute(child_edges, "col", [(i, (i + 1) % ring) for i in range(ring)])
    from_right = lax.ppermute(child_edges, "col", [(i, (i - 1) % ring) for i in range(ring)])
    from_left = from_left.reshape(per_dev, nf, rows, 2 * width)
    from_right = from_right.reshape(per_dev, nf, rows, 2 * width)
    gap = jnp.zeros((per_dev, nf, rows, LANES - 2 * width), state.dtype)
    return jnp.concatenate([from_right[..., :width], gap, from_left[..., width:]], axis=-1)


def shards(state, noise, parents):
    count = lax.axis_size("ens")
    me = lax.axis_index("ens")
    per_dev = state.shape[0]
    dist = max(1, -(-per_dev // count))
    send_index, position = routing(parents, count, per_dev, dist, me)
    outgoing = jnp.take(state, send_index, axis=0, mode="clip")
    incoming = lax.all_to_all(outgoing, "ens", split_axis=0, concat_axis=0, tiled=True)
    halo = halo_block(state, noise, parents, me)
    return main_forecast(position, incoming, noise, halo)


def solution(mesh):
    placed = (P("ens", None, None, "col"), P("ens", None, None, "col"), P())
    return jax.shard_map(
        shards, mesh=mesh, in_specs=placed, out_specs=P("ens", None, None, "col"), check_vma=False
    )
```

```python
import jax
import jax.numpy as jnp
from jax import lax
from jax.experimental import pallas as pl
from jax.experimental.pallas import tpu as pltpu
from jax.sharding import PartitionSpec as P

STEPS = 4
LANES = 128
PAIR = 2

time_step = 0.3
coriolis = 0.2
gravity = 1.0


def routing(parents, count, per_dev, dist, me):
    blocks = parents.reshape(count, per_dev)
    owner = blocks // per_dev
    local = blocks % per_dev
    ids = jnp.arange(per_dev, dtype=jnp.int32)
    same = blocks[:, :, None] == blocks[:, None, :]
    earlier = ids[None, :] < ids[:, None]
    first = jnp.logical_not(jnp.any(same & earlier[None], axis=2))
    below = (
        (owner[:, :, None] == owner[:, None, :])
        & (blocks[:, None, :] < blocks[:, :, None])
        & first[:, None, :]
    )
    slot = jnp.sum(below.astype(jnp.int32), axis=2)
    slots = jnp.arange(dist, dtype=jnp.int32)
    pick = (owner == me)[:, None, :] & first[:, None, :] & (slot[:, None, :] == slots[None, :, None])
    send_index = jnp.sum(pick.astype(jnp.int32) * local[:, None, :], axis=2).reshape(-1)
    my_owner = lax.dynamic_index_in_dim(owner, me, 0, keepdims=False)
    my_slot = lax.dynamic_index_in_dim(slot, me, 0, keepdims=False)
    return send_index, my_owner * dist + my_slot


def update(e, u, v, xp, xm):
    rows = e.shape[-2]

    def yp(a):
        return pltpu.roll(a, rows - 1, 0)

    def ym(a):
        return pltpu.roll(a, 1, 0)

    e_xp, u_xp, v_xp = xp
    e_xm, u_xm, v_xm = xm
    e_yp, e_ym = yp(e), ym(e)
    u_yp, u_ym = yp(u), ym(u)
    v_yp, v_ym = yp(v), ym(v)
    hu_xp = (1.0 + e_xp) * u_xp
    hu_xm = (1.0 + e_xm) * u_xm
    hv_yp = (1.0 + e_yp) * v_yp
    hv_ym = (1.0 + e_ym) * v_ym
    half_step = 0.5 * time_step
    new_e = 0.25 * (e_xp + e_xm + e_yp + e_ym) - half_step * ((hu_xp - hu_xm) + (hv_yp - hv_ym))
    new_u = (
        0.25 * (u_xp + u_xm + u_yp + u_ym)
        - half_step * (u * (u_xp - u_xm) + v * (u_yp - u_ym) + gravity * (e_xp - e_xm))
        + (time_step * coriolis) * v
    )
    new_v = (
        0.25 * (v_xp + v_xm + v_yp + v_ym)
        - half_step * (u * (v_xp - v_xm) + v * (v_yp - v_ym) + gravity * (e_yp - e_ym))
        - (time_step * coriolis) * u
    )
    return new_e, new_u, new_v


def advance_vreg(e, u, v):
    xp = tuple(pltpu.roll(a, LANES - 1, 1) for a in (e, u, v))
    xm = tuple(pltpu.roll(a, 1, 1) for a in (e, u, v))
    return update(e, u, v, xp, xm)


def sweep(load, store, ncol):
    rows = load(0)[0].shape[-2]
    lane = lax.broadcasted_iota(jnp.int32, (rows, LANES), 1)
    first_lane = lane == 0
    last_lane = lane == LANES - 1

    def fetch(j):
        return load(j % ncol)

    def ahead(vals):
        return tuple(pltpu.roll(a, LANES - 1, 1) for a in vals)

    def behind(vals):
        return tuple(pltpu.roll(a, 1, 1) for a in vals)

    here = fetch(0)
    prev_behind = behind(fetch(ncol - 1))
    here_behind = behind(here)
    here_ahead = ahead(here)
    for j in range(ncol):
        nxt = fetch(j + 1)
        nxt_ahead = ahead(nxt)
        nxt_behind = behind(nxt)
        xp = [jnp.where(last_lane, a, b) for a, b in zip(nxt_ahead, here_ahead)]
        xm = [jnp.where(first_lane, a, b) for a, b in zip(prev_behind, here_behind)]
        e, u, v = here
        store(j, update(e, u, v, xp, xm))
        prev_behind = here_behind
        here, here_behind, here_ahead = nxt, nxt_behind, nxt_ahead


def ref_loader(ref):
    def load(j):
        window = pl.ds(j * LANES, LANES)
        return tuple(ref[f, :, window] for f in range(3))

    return load


def ref_storer(ref, limit):
    def store(j, values):
        if j < limit:
            window = pl.ds(j * LANES, LANES)
            for f in range(3):
                ref[f, :, window] = values[f]

    return store


def child_loader(inc, noise, halo, ncol):
    def load(j):
        if j == ncol:
            return tuple(halo[f] for f in range(3))
        window = pl.ds(j * LANES, LANES)
        return tuple(inc[f, :, window] + noise[f, :, window] for f in range(3))

    return load


def main_kernel(pos_ref, *refs):
    incs = refs[:-5]
    noise_ref, halo_ref, out_ref, first, second = refs[-5:]
    ncol = noise_ref.shape[-1] // LANES
    wide = ncol + 1
    for s in range(STEPS):
        for k in range(len(incs)):
            if s == 0:
                load = child_loader(incs[k].at[0], noise_ref.at[k], halo_ref.at[k], ncol)
            else:
                load = ref_loader((first if s % 2 == 1 else second).at[k])
            if s == STEPS - 1:
                store = ref_storer(out_ref.at[k], ncol)
            else:
                store = ref_storer((first if s % 2 == 0 else second).at[k], wide)
            sweep(load, store, wide)


def main_forecast(position, incoming, noise, halo):
    per_dev, nf, rows, cols = noise.shape
    group = PAIR if per_dev % PAIR == 0 else 1

    def row_map(k):
        return lambda i, pos: (pos[i * group + k], 0, 0, 0)

    in_specs = [pl.BlockSpec((1, nf, rows, cols), row_map(k)) for k in range(group)]
    spec = pl.BlockSpec((group, nf, rows, cols), lambda i, pos: (i, 0, 0, 0))
    halo_spec = pl.BlockSpec((group, nf, rows, LANES), lambda i, pos: (i, 0, 0, 0))
    grid_spec = pltpu.PrefetchScalarGridSpec(
        num_scalar_prefetch=1,
        grid=(per_dev // group,),
        in_specs=in_specs + [spec, halo_spec],
        out_specs=spec,
        scratch_shapes=[pltpu.VMEM((group, nf, rows, cols + LANES), jnp.float32)] * 2,
    )
    return pl.pallas_call(
        main_kernel,
        grid_spec=grid_spec,
        out_shape=jax.ShapeDtypeStruct(noise.shape, noise.dtype),
    )(position, *([incoming] * group), noise, halo)


def edges(a):
    return jnp.concatenate([a[..., :STEPS], a[..., -STEPS:]], axis=-1).reshape(a.shape[0], -1)


def halo_block(everyone, state, noise, parents, me):
    per_dev, nf, rows, cols = state.shape
    width = STEPS
    mine = lax.dynamic_slice_in_dim(parents, me * per_dev, per_dev)
    child_edges = jnp.take(everyone, mine, axis=0, mode="clip") + edges(noise)
    ring = lax.axis_size("col")
    from_left = lax.ppermute(child_edges, "col", [(i, (i + 1) % ring) for i in range(ring)])
    from_right = lax.ppermute(child_edges, "col", [(i, (i - 1) % ring) for i in range(ring)])
    from_left = from_left.reshape(per_dev, nf, rows, 2 * width)
    from_right = from_right.reshape(per_dev, nf, rows, 2 * width)
    gap = jnp.zeros((per_dev, nf, rows, LANES - 2 * width), state.dtype)
    return jnp.concatenate([from_right[..., :width], gap, from_left[..., width:]], axis=-1)


def shards(state, noise, parents):
    count = lax.axis_size("ens")
    me = lax.axis_index("ens")
    per_dev = state.shape[0]
    dist = max(1, -(-per_dev // count))
    send_index, position = routing(parents, count, per_dev, dist, me)
    outgoing = jnp.take(state, send_index, axis=0, mode="clip")
    everyone = lax.all_gather(edges(state), "ens", axis=0, tiled=True)
    everyone, outgoing = lax.optimization_barrier((everyone, outgoing))
    incoming = lax.all_to_all(outgoing, "ens", split_axis=0, concat_axis=0, tiled=True)
    halo = halo_block(everyone, state, noise, parents, me)
    return main_forecast(position, incoming, noise, halo)


def solution(mesh):
    placed = (P("ens", None, None, "col"), P("ens", None, None, "col"), P())
    return jax.shard_map(
        shards, mesh=mesh, in_specs=placed, out_specs=P("ens", None, None, "col"), check_vma=False
    )
```

```python
import jax
import jax.numpy as jnp
from jax import lax
from jax.experimental import pallas as pl
from jax.experimental.pallas import tpu as pltpu
from jax.sharding import PartitionSpec as P

STEPS = 4
LANES = 128
PAIR = 4
EDGE_GROUP = 8
GATHER_GROUP = 32

time_step = 0.3
coriolis = 0.2
gravity = 1.0


def routing(parents, count, per_dev, dist, me):
    blocks = parents.reshape(count, per_dev)
    owner = blocks // per_dev
    local = blocks % per_dev
    ids = jnp.arange(per_dev, dtype=jnp.int32)
    same = blocks[:, :, None] == blocks[:, None, :]
    earlier = ids[None, :] < ids[:, None]
    first = jnp.logical_not(jnp.any(same & earlier[None], axis=2))
    below = (
        (owner[:, :, None] == owner[:, None, :])
        & (blocks[:, None, :] < blocks[:, :, None])
        & first[:, None, :]
    )
    slot = jnp.sum(below.astype(jnp.int32), axis=2)
    slots = jnp.arange(dist, dtype=jnp.int32)
    pick = (owner == me)[:, None, :] & first[:, None, :] & (slot[:, None, :] == slots[None, :, None])
    send_index = jnp.sum(pick.astype(jnp.int32) * local[:, None, :], axis=2).reshape(-1)
    my_owner = lax.dynamic_index_in_dim(owner, me, 0, keepdims=False)
    my_slot = lax.dynamic_index_in_dim(slot, me, 0, keepdims=False)
    return send_index, my_owner * dist + my_slot


def update(e, u, v, xp, xm):
    rows = e.shape[-2]

    def yp(a):
        return pltpu.roll(a, rows - 1, 0)

    def ym(a):
        return pltpu.roll(a, 1, 0)

    e_xp, u_xp, v_xp = xp
    e_xm, u_xm, v_xm = xm
    e_yp, e_ym = yp(e), ym(e)
    u_yp, u_ym = yp(u), ym(u)
    v_yp, v_ym = yp(v), ym(v)
    hu_xp = (1.0 + e_xp) * u_xp
    hu_xm = (1.0 + e_xm) * u_xm
    hv_yp = (1.0 + e_yp) * v_yp
    hv_ym = (1.0 + e_ym) * v_ym
    half_step = 0.5 * time_step
    new_e = 0.25 * (e_xp + e_xm + e_yp + e_ym) - half_step * ((hu_xp - hu_xm) + (hv_yp - hv_ym))
    new_u = (
        0.25 * (u_xp + u_xm + u_yp + u_ym)
        - half_step * (u * (u_xp - u_xm) + v * (u_yp - u_ym) + gravity * (e_xp - e_xm))
        + (time_step * coriolis) * v
    )
    new_v = (
        0.25 * (v_xp + v_xm + v_yp + v_ym)
        - half_step * (u * (v_xp - v_xm) + v * (v_yp - v_ym) + gravity * (e_yp - e_ym))
        - (time_step * coriolis) * u
    )
    return new_e, new_u, new_v


def advance_vreg(e, u, v):
    xp = tuple(pltpu.roll(a, LANES - 1, 1) for a in (e, u, v))
    xm = tuple(pltpu.roll(a, 1, 1) for a in (e, u, v))
    return update(e, u, v, xp, xm)


def sweep(src, dst, ncol, extra=None):
    rows = src.shape[-2]
    lane = lax.broadcasted_iota(jnp.int32, (rows, LANES), 1)
    first_lane = lane == 0
    last_lane = lane == LANES - 1

    def load(j):
        window = pl.ds((j % ncol) * LANES, LANES)
        e = src[0, :, window]
        u = src[1, :, window]
        v = src[2, :, window]
        if extra is not None:
            e = e + extra[0, :, window]
            u = u + extra[1, :, window]
            v = v + extra[2, :, window]
        return e, u, v

    def ahead(vals):
        return tuple(pltpu.roll(a, LANES - 1, 1) for a in vals)

    def behind(vals):
        return tuple(pltpu.roll(a, 1, 1) for a in vals)

    here = load(0)
    prev_behind = behind(load(ncol - 1)) if ncol > 1 else behind(here)
    here_behind = behind(here)
    here_ahead = ahead(here)
    for j in range(ncol):
        if ncol > 1:
            nxt = load(j + 1)
            nxt_ahead = ahead(nxt)
            nxt_behind = behind(nxt)
        else:
            nxt, nxt_ahead, nxt_behind = here, here_ahead, here_behind
        xp = [jnp.where(last_lane, a, b) for a, b in zip(nxt_ahead, here_ahead)]
        xm = [jnp.where(first_lane, a, b) for a, b in zip(prev_behind, here_behind)]
        e, u, v = here
        new_e, new_u, new_v = update(e, u, v, xp, xm)
        window = pl.ds(j * LANES, LANES)
        dst[0, :, window] = new_e
        dst[1, :, window] = new_u
        dst[2, :, window] = new_v
        prev_behind = here_behind
        here, here_behind, here_ahead = nxt, nxt_behind, nxt_ahead


def run_steps(chains, extras, ncol):
    for s in range(STEPS):
        for chain, extra in zip(chains, extras):
            sweep(chain[s], chain[s + 1], ncol, extra if s == 0 else None)


def chain_of(src, out, first, second):
    return [src] + [first if s % 2 == 0 else second for s in range(STEPS - 1)] + [out]


def main_kernel(pos_ref, *refs):
    incs = refs[:-4]
    noise_ref, out_ref, first, second = refs[-4:]
    ncol = noise_ref.shape[-1] // LANES
    chains = [chain_of(incs[k].at[0], out_ref.at[k], first.at[k], second.at[k]) for k in range(len(incs))]
    extras = [noise_ref.at[k] for k in range(len(incs))]
    run_steps(chains, extras, ncol)


def main_forecast(position, incoming, noise):
    per_dev, nf, rows, cols = noise.shape
    group = PAIR if per_dev % PAIR == 0 else 1

    def row_map(k):
        return lambda i, pos: (pos[i * group + k], 0, 0, 0)

    in_specs = [pl.BlockSpec((1, nf, rows, cols), row_map(k)) for k in range(group)]
    spec = pl.BlockSpec((group, nf, rows, cols), lambda i, pos: (i, 0, 0, 0))
    grid_spec = pltpu.PrefetchScalarGridSpec(
        num_scalar_prefetch=1,
        grid=(per_dev // group,),
        in_specs=in_specs + [spec],
        out_specs=spec,
        scratch_shapes=[pltpu.VMEM((group, nf, rows, cols), jnp.float32)] * 2,
    )
    return pl.pallas_call(
        main_kernel,
        grid_spec=grid_spec,
        out_shape=jax.ShapeDtypeStruct(noise.shape, noise.dtype),
    )(position, *([incoming] * group), noise)


def edges_kernel(pos_ref, *refs):
    group = (len(refs) - 4) // 2
    left_rows, right_rows = refs[:group], refs[group:2 * group]
    noise_left, noise_right, lblk, rblk = refs[2 * group:]
    for k in range(group):
        lblk[k] = left_rows[k][0] + noise_left[k]
        rblk[k] = right_rows[k][0] + noise_right[k]


def edge_blocks(position, incoming, noise):
    per_dev, nf, rows, cols = noise.shape
    last = cols // LANES - 1
    group = GATHER_GROUP if per_dev % GATHER_GROUP == 0 else 1

    def row_map(k, col):
        return lambda i, pos: (pos[i * group + k], 0, 0, col)

    left_specs = [pl.BlockSpec((1, nf, rows, LANES), row_map(k, 0)) for k in range(group)]
    right_specs = [pl.BlockSpec((1, nf, rows, LANES), row_map(k, last)) for k in range(group)]
    left = pl.BlockSpec((group, nf, rows, LANES), lambda i, pos: (i, 0, 0, 0))
    right = pl.BlockSpec((group, nf, rows, LANES), lambda i, pos: (i, 0, 0, last))
    out = pl.BlockSpec((group, nf, rows, LANES), lambda i, pos: (i, 0, 0, 0))
    edge_shape = jax.ShapeDtypeStruct((per_dev, nf, rows, LANES), noise.dtype)
    grid_spec = pltpu.PrefetchScalarGridSpec(
        num_scalar_prefetch=1,
        grid=(per_dev // group,),
        in_specs=left_specs + right_specs + [left, right],
        out_specs=[out, out],
    )
    return pl.pallas_call(
        edges_kernel,
        grid_spec=grid_spec,
        out_shape=[edge_shape, edge_shape],
    )(position, *([incoming] * (2 * group)), noise, noise)


def edge_kernel(lblk, rblk, from_left, from_right, body_ref, out_ref, packed, first, second, result):
    side = pl.program_id(0)
    rows = lblk.shape[-2]
    group = packed.shape[0]
    lane = lax.broadcasted_iota(jnp.int32, (rows, LANES), 1)
    half = LANES // 2
    width = STEPS

    @pl.when(side == 0)
    def _():
        def block(g, carry):
            base = g * group
            for k in range(group):
                i = base + k
                fields = []
                for f in range(3):
                    left = jnp.where(lane >= LANES - width, from_left[i, f], lblk[i, f])
                    right = jnp.where(lane < width, from_right[i, f], rblk[i, f])
                    right = pltpu.roll(right, half, 1)
                    keep_left = (lane < 2 * width) | (lane >= LANES - width)
                    fields.append(jnp.where(keep_left, left, right))
                e, u, v = fields
                for _ in range(STEPS):
                    e, u, v = advance_vreg(e, u, v)
                result[i, 0] = e
                result[i, 1] = u
                result[i, 2] = v
            return carry

        lax.fori_loop(0, lblk.shape[0] // group, block, 0)
        out_ref[...] = jnp.where(lane < width, result[...], body_ref[...])

    @pl.when(side == 1)
    def _():
        def particle(i, carry):
            for f in range(3):
                out_ref[i, f] = jnp.where(
                    lane >= LANES - width, pltpu.roll(result[i, f], half, 1), body_ref[i, f]
                )
            return carry

        lax.fori_loop(0, lblk.shape[0], particle, 0)


def edge_fix(lblk, rblk, from_left, from_right, body):
    per_dev, nf, rows, cols = body.shape
    ncol = cols // LANES
    group = EDGE_GROUP if per_dev % EDGE_GROUP == 0 else 1
    whole = pl.BlockSpec((per_dev, nf, rows, LANES), lambda s: (0, 0, 0, 0))
    edge = pl.BlockSpec((per_dev, nf, rows, LANES), lambda s: (0, 0, 0, s * (ncol - 1)))
    return pl.pallas_call(
        edge_kernel,
        grid=(2,),
        in_specs=[whole, whole, whole, whole, edge],
        out_specs=edge,
        out_shape=jax.ShapeDtypeStruct(body.shape, body.dtype),
        scratch_shapes=[
            pltpu.VMEM((group, nf, rows, LANES), jnp.float32),
            pltpu.VMEM((group, nf, rows, LANES), jnp.float32),
            pltpu.VMEM((group, nf, rows, LANES), jnp.float32),
            pltpu.VMEM((per_dev, nf, rows, LANES), jnp.float32),
        ],
        input_output_aliases={4: 0},
    )(lblk, rblk, from_left, from_right, body)


def shards(state, noise, parents):
    count = lax.axis_size("ens")
    me = lax.axis_index("ens")
    per_dev = state.shape[0]
    dist = max(1, -(-per_dev // count))
    send_index, position = routing(parents, count, per_dev, dist, me)
    outgoing = jnp.take(state, send_index, axis=0, mode="clip")
    incoming = lax.all_to_all(outgoing, "ens", split_axis=0, concat_axis=0, tiled=True)
    lblk, rblk = edge_blocks(position, incoming, noise)
    ring = lax.axis_size("col")
    from_left = lax.ppermute(rblk, "col", [(i, (i + 1) % ring) for i in range(ring)])
    from_right = lax.ppermute(lblk, "col", [(i, (i - 1) % ring) for i in range(ring)])
    body = main_forecast(position, incoming, noise)
    return edge_fix(lblk, rblk, from_left, from_right, body)


def solution(mesh):
    placed = (P("ens", None, None, "col"), P("ens", None, None, "col"), P())
    return jax.shard_map(
        shards, mesh=mesh, in_specs=placed, out_specs=P("ens", None, None, "col"), check_vma=False
    )
```

```python
import jax
import jax.numpy as jnp
from jax import lax
from jax.experimental import pallas as pl
from jax.experimental.pallas import tpu as pltpu
from jax.sharding import PartitionSpec as P

STEPS = 4
LANES = 128
PAIR = 4
EDGE_GROUP = 8
GATHER_GROUP = 32

time_step = 0.3
coriolis = 0.2
gravity = 1.0


def routing(parents, count, per_dev, dist, me):
    blocks = parents.reshape(count, per_dev)
    owner = blocks // per_dev
    local = blocks % per_dev
    ids = jnp.arange(per_dev, dtype=jnp.int32)
    same = blocks[:, :, None] == blocks[:, None, :]
    earlier = ids[None, :] < ids[:, None]
    first = jnp.logical_not(jnp.any(same & earlier[None], axis=2))
    below = (
        (owner[:, :, None] == owner[:, None, :])
        & (blocks[:, None, :] < blocks[:, :, None])
        & first[:, None, :]
    )
    slot = jnp.sum(below.astype(jnp.int32), axis=2)
    slots = jnp.arange(dist, dtype=jnp.int32)
    pick = (owner == me)[:, None, :] & first[:, None, :] & (slot[:, None, :] == slots[None, :, None])
    send_index = jnp.sum(pick.astype(jnp.int32) * local[:, None, :], axis=2).reshape(-1)
    my_owner = lax.dynamic_index_in_dim(owner, me, 0, keepdims=False)
    my_slot = lax.dynamic_index_in_dim(slot, me, 0, keepdims=False)
    return send_index, my_owner * dist + my_slot


def update(e, u, v, xp, xm):
    rows = e.shape[-2]

    def yp(a):
        return pltpu.roll(a, rows - 1, 0)

    def ym(a):
        return pltpu.roll(a, 1, 0)

    e_xp, u_xp, v_xp = xp
    e_xm, u_xm, v_xm = xm
    e_yp, e_ym = yp(e), ym(e)
    u_yp, u_ym = yp(u), ym(u)
    v_yp, v_ym = yp(v), ym(v)
    hu_xp = (1.0 + e_xp) * u_xp
    hu_xm = (1.0 + e_xm) * u_xm
    hv_yp = (1.0 + e_yp) * v_yp
    hv_ym = (1.0 + e_ym) * v_ym
    half_step = 0.5 * time_step
    new_e = 0.25 * (e_xp + e_xm + e_yp + e_ym) - half_step * ((hu_xp - hu_xm) + (hv_yp - hv_ym))
    new_u = (
        0.25 * (u_xp + u_xm + u_yp + u_ym)
        - half_step * (u * (u_xp - u_xm) + v * (u_yp - u_ym) + gravity * (e_xp - e_xm))
        + (time_step * coriolis) * v
    )
    new_v = (
        0.25 * (v_xp + v_xm + v_yp + v_ym)
        - half_step * (u * (v_xp - v_xm) + v * (v_yp - v_ym) + gravity * (e_yp - e_ym))
        - (time_step * coriolis) * u
    )
    return new_e, new_u, new_v


def advance_vreg(e, u, v):
    xp = tuple(pltpu.roll(a, LANES - 1, 1) for a in (e, u, v))
    xm = tuple(pltpu.roll(a, 1, 1) for a in (e, u, v))
    return update(e, u, v, xp, xm)


def sweep(src, dst, ncol, extra=None):
    rows = src.shape[-2]
    lane = lax.broadcasted_iota(jnp.int32, (rows, LANES), 1)
    first_lane = lane == 0
    last_lane = lane == LANES - 1

    def load(j):
        window = pl.ds((j % ncol) * LANES, LANES)
        e = src[0, :, window]
        u = src[1, :, window]
        v = src[2, :, window]
        if extra is not None:
            e = e + extra[0, :, window]
            u = u + extra[1, :, window]
            v = v + extra[2, :, window]
        return e, u, v

    def ahead(vals):
        return tuple(pltpu.roll(a, LANES - 1, 1) for a in vals)

    def behind(vals):
        return tuple(pltpu.roll(a, 1, 1) for a in vals)

    here = load(0)
    prev_behind = behind(load(ncol - 1)) if ncol > 1 else behind(here)
    here_behind = behind(here)
    here_ahead = ahead(here)
    for j in range(ncol):
        if ncol > 1:
            nxt = load(j + 1)
            nxt_ahead = ahead(nxt)
            nxt_behind = behind(nxt)
        else:
            nxt, nxt_ahead, nxt_behind = here, here_ahead, here_behind
        xp = [jnp.where(last_lane, a, b) for a, b in zip(nxt_ahead, here_ahead)]
        xm = [jnp.where(first_lane, a, b) for a, b in zip(prev_behind, here_behind)]
        e, u, v = here
        new_e, new_u, new_v = update(e, u, v, xp, xm)
        window = pl.ds(j * LANES, LANES)
        dst[0, :, window] = new_e
        dst[1, :, window] = new_u
        dst[2, :, window] = new_v
        prev_behind = here_behind
        here, here_behind, here_ahead = nxt, nxt_behind, nxt_ahead


def run_steps(chains, extras, ncol):
    for s in range(STEPS):
        for chain, extra in zip(chains, extras):
            sweep(chain[s], chain[s + 1], ncol, extra if s == 0 else None)


def chain_of(src, out, first, second):
    return [src] + [first if s % 2 == 0 else second for s in range(STEPS - 1)] + [out]


def main_kernel(pos_ref, *refs):
    incs = refs[:-4]
    noise_ref, out_ref, first, second = refs[-4:]
    ncol = noise_ref.shape[-1] // LANES
    chains = [chain_of(incs[k].at[0], out_ref.at[k], first.at[k], second.at[k]) for k in range(len(incs))]
    extras = [noise_ref.at[k] for k in range(len(incs))]
    run_steps(chains, extras, ncol)


def main_forecast(position, incoming, noise):
    per_dev, nf, rows, cols = noise.shape
    group = PAIR if per_dev % PAIR == 0 else 1

    def row_map(k):
        return lambda i, pos: (pos[i * group + k], 0, 0, 0)

    in_specs = [pl.BlockSpec((1, nf, rows, cols), row_map(k)) for k in range(group)]
    spec = pl.BlockSpec((group, nf, rows, cols), lambda i, pos: (i, 0, 0, 0))
    grid_spec = pltpu.PrefetchScalarGridSpec(
        num_scalar_prefetch=1,
        grid=(per_dev // group,),
        in_specs=in_specs + [spec],
        out_specs=spec,
        scratch_shapes=[pltpu.VMEM((group, nf, rows, cols), jnp.float32)] * 2,
    )
    return pl.pallas_call(
        main_kernel,
        grid_spec=grid_spec,
        out_shape=jax.ShapeDtypeStruct(noise.shape, noise.dtype),
    )(position, *([incoming] * group), noise)


def edges_kernel(pos_ref, *refs):
    group = (len(refs) - 3) // 2
    left_rows, right_rows = refs[:group], refs[group:2 * group]
    noise_left, noise_right, own = refs[2 * group:]
    rows = own.shape[-2]
    lane = lax.broadcasted_iota(jnp.int32, (rows, LANES), 1)
    keep_left = (lane < 2 * STEPS) | (lane >= LANES - STEPS)
    for k in range(group):
        for f in range(3):
            left = left_rows[k][0, f] + noise_left[k, f]
            right = pltpu.roll(right_rows[k][0, f] + noise_right[k, f], LANES // 2, 1)
            own[k, f] = jnp.where(keep_left, left, right)


def edge_blocks(position, incoming, noise):
    per_dev, nf, rows, cols = noise.shape
    last = cols // LANES - 1
    group = GATHER_GROUP if per_dev % GATHER_GROUP == 0 else 1

    def row_map(k, col):
        return lambda i, pos: (pos[i * group + k], 0, 0, col)

    left_specs = [pl.BlockSpec((1, nf, rows, LANES), row_map(k, 0)) for k in range(group)]
    right_specs = [pl.BlockSpec((1, nf, rows, LANES), row_map(k, last)) for k in range(group)]
    left = pl.BlockSpec((group, nf, rows, LANES), lambda i, pos: (i, 0, 0, 0))
    right = pl.BlockSpec((group, nf, rows, LANES), lambda i, pos: (i, 0, 0, last))
    out = pl.BlockSpec((group, nf, rows, LANES), lambda i, pos: (i, 0, 0, 0))
    grid_spec = pltpu.PrefetchScalarGridSpec(
        num_scalar_prefetch=1,
        grid=(per_dev // group,),
        in_specs=left_specs + right_specs + [left, right],
        out_specs=out,
    )
    return pl.pallas_call(
        edges_kernel,
        grid_spec=grid_spec,
        out_shape=jax.ShapeDtypeStruct((per_dev, nf, rows, LANES), noise.dtype),
    )(position, *([incoming] * (2 * group)), noise, noise)


def edge_kernel(own, from_left, from_right, body, out, patch, first_buf, last_buf, sems):
    rows = own.shape[-2]
    cols = body.shape[-1]
    group = EDGE_GROUP if own.shape[0] % EDGE_GROUP == 0 else 1
    lane = lax.broadcasted_iota(jnp.int32, (rows, LANES), 1)
    halo_lanes = (lane >= LANES - STEPS) | ((lane >= LANES // 2) & (lane < LANES // 2 + STEPS))
    first_in = pltpu.make_async_copy(body.at[:, :, :, pl.ds(0, LANES)], first_buf, sems.at[0])
    last_in = pltpu.make_async_copy(body.at[:, :, :, pl.ds(cols - LANES, LANES)], last_buf, sems.at[1])
    first_in.start()
    last_in.start()

    def block(g, carry):
        base = g * group
        for k in range(group):
            i = base + k
            fields = []
            for f in range(3):
                received = jnp.where(lane < STEPS, from_right[i, f], from_left[i, f])
                received = pltpu.roll(received, LANES // 2, 1)
                fields.append(jnp.where(halo_lanes, received, own[i, f]))
            e, u, v = fields
            for _ in range(STEPS):
                e, u, v = advance_vreg(e, u, v)
            patch[i, 0] = e
            patch[i, 1] = u
            patch[i, 2] = v
        return carry

    lax.fori_loop(0, own.shape[0] // group, block, 0)
    first_in.wait()
    last_in.wait()

    def merge(i, carry):
        for f in range(3):
            values = patch[i, f]
            first_buf[i, f] = jnp.where(lane < STEPS, values, first_buf[i, f])
            last_buf[i, f] = jnp.where(
                lane >= LANES - STEPS, pltpu.roll(values, LANES // 2, 1), last_buf[i, f]
            )
        return carry

    lax.fori_loop(0, own.shape[0], merge, 0)
    first_out = pltpu.make_async_copy(first_buf, out.at[:, :, :, pl.ds(0, LANES)], sems.at[0])
    last_out = pltpu.make_async_copy(last_buf, out.at[:, :, :, pl.ds(cols - LANES, LANES)], sems.at[1])
    first_out.start()
    last_out.start()
    first_out.wait()
    last_out.wait()


def edge_fix(own, from_left, from_right, body):
    whole = pl.BlockSpec(memory_space=pltpu.VMEM)
    raw = pl.BlockSpec(memory_space=pl.ANY)
    return pl.pallas_call(
        edge_kernel,
        in_specs=[whole, whole, whole, raw],
        out_specs=raw,
        out_shape=jax.ShapeDtypeStruct(body.shape, body.dtype),
        scratch_shapes=[
            pltpu.VMEM(own.shape, jnp.float32),
            pltpu.VMEM(own.shape, jnp.float32),
            pltpu.VMEM(own.shape, jnp.float32),
            pltpu.SemaphoreType.DMA((2,)),
        ],
        input_output_aliases={3: 0},
    )(own, from_left, from_right, body)


def shards(state, noise, parents):
    count = lax.axis_size("ens")
    me = lax.axis_index("ens")
    per_dev = state.shape[0]
    dist = max(1, -(-per_dev // count))
    send_index, position = routing(parents, count, per_dev, dist, me)
    outgoing = jnp.take(state, send_index, axis=0, mode="clip")
    incoming = lax.all_to_all(outgoing, "ens", split_axis=0, concat_axis=0, tiled=True)
    own = edge_blocks(position, incoming, noise)
    ring = lax.axis_size("col")
    from_left = lax.ppermute(own, "col", [(i, (i + 1) % ring) for i in range(ring)])
    from_right = lax.ppermute(own, "col", [(i, (i - 1) % ring) for i in range(ring)])
    body = main_forecast(position, incoming, noise)
    return edge_fix(own, from_left, from_right, body)


def solution(mesh):
    placed = (P("ens", None, None, "col"), P("ens", None, None, "col"), P())
    return jax.shard_map(
        shards, mesh=mesh, in_specs=placed, out_specs=P("ens", None, None, "col"), check_vma=False
    )
```

```python
import jax
import jax.numpy as jnp
from jax import lax
from jax.experimental import pallas as pl
from jax.experimental.pallas import tpu as pltpu
from jax.sharding import PartitionSpec as P

STEPS = 4
LANES = 128
PAIR = 4
EDGE_GROUP = 32
GATHER_GROUP = 32

time_step = 0.3
coriolis = 0.2
gravity = 1.0


def routing(parents, count, per_dev, dist, me):
    blocks = parents.reshape(count, per_dev)
    owner = blocks // per_dev
    local = blocks % per_dev
    ids = jnp.arange(per_dev, dtype=jnp.int32)
    same = blocks[:, :, None] == blocks[:, None, :]
    earlier = ids[None, :] < ids[:, None]
    first = jnp.logical_not(jnp.any(same & earlier[None], axis=2))
    below = (
        (owner[:, :, None] == owner[:, None, :])
        & (blocks[:, None, :] < blocks[:, :, None])
        & first[:, None, :]
    )
    slot = jnp.sum(below.astype(jnp.int32), axis=2)
    slots = jnp.arange(dist, dtype=jnp.int32)
    pick = (owner == me)[:, None, :] & first[:, None, :] & (slot[:, None, :] == slots[None, :, None])
    send_index = jnp.sum(pick.astype(jnp.int32) * local[:, None, :], axis=2).reshape(-1)
    my_owner = lax.dynamic_index_in_dim(owner, me, 0, keepdims=False)
    my_slot = lax.dynamic_index_in_dim(slot, me, 0, keepdims=False)
    return send_index, my_owner * dist + my_slot


def update(e, u, v, xp, xm):
    rows = e.shape[-2]

    def yp(a):
        return pltpu.roll(a, rows - 1, 0)

    def ym(a):
        return pltpu.roll(a, 1, 0)

    e_xp, u_xp, v_xp = xp
    e_xm, u_xm, v_xm = xm
    e_yp, e_ym = yp(e), ym(e)
    u_yp, u_ym = yp(u), ym(u)
    v_yp, v_ym = yp(v), ym(v)
    hu_xp = (1.0 + e_xp) * u_xp
    hu_xm = (1.0 + e_xm) * u_xm
    hv_yp = (1.0 + e_yp) * v_yp
    hv_ym = (1.0 + e_ym) * v_ym
    half_step = 0.5 * time_step
    new_e = 0.25 * (e_xp + e_xm + e_yp + e_ym) - half_step * ((hu_xp - hu_xm) + (hv_yp - hv_ym))
    new_u = (
        0.25 * (u_xp + u_xm + u_yp + u_ym)
        - half_step * (u * (u_xp - u_xm) + v * (u_yp - u_ym) + gravity * (e_xp - e_xm))
        + (time_step * coriolis) * v
    )
    new_v = (
        0.25 * (v_xp + v_xm + v_yp + v_ym)
        - half_step * (u * (v_xp - v_xm) + v * (v_yp - v_ym) + gravity * (e_yp - e_ym))
        - (time_step * coriolis) * u
    )
    return new_e, new_u, new_v


def advance_vreg(e, u, v):
    xp = tuple(pltpu.roll(a, LANES - 1, 1) for a in (e, u, v))
    xm = tuple(pltpu.roll(a, 1, 1) for a in (e, u, v))
    return update(e, u, v, xp, xm)


def sweep(src, dst, ncol, extra=None):
    rows = src.shape[-2]
    lane = lax.broadcasted_iota(jnp.int32, (rows, LANES), 1)
    first_lane = lane == 0
    last_lane = lane == LANES - 1

    def load(j):
        window = pl.ds((j % ncol) * LANES, LANES)
        e = src[0, :, window]
        u = src[1, :, window]
        v = src[2, :, window]
        if extra is not None:
            e = e + extra[0, :, window]
            u = u + extra[1, :, window]
            v = v + extra[2, :, window]
        return e, u, v

    def ahead(vals):
        return tuple(pltpu.roll(a, LANES - 1, 1) for a in vals)

    def behind(vals):
        return tuple(pltpu.roll(a, 1, 1) for a in vals)

    here = load(0)
    prev_behind = behind(load(ncol - 1)) if ncol > 1 else behind(here)
    here_behind = behind(here)
    here_ahead = ahead(here)
    for j in range(ncol):
        if ncol > 1:
            nxt = load(j + 1)
            nxt_ahead = ahead(nxt)
            nxt_behind = behind(nxt)
        else:
            nxt, nxt_ahead, nxt_behind = here, here_ahead, here_behind
        xp = [jnp.where(last_lane, a, b) for a, b in zip(nxt_ahead, here_ahead)]
        xm = [jnp.where(first_lane, a, b) for a, b in zip(prev_behind, here_behind)]
        e, u, v = here
        new_e, new_u, new_v = update(e, u, v, xp, xm)
        window = pl.ds(j * LANES, LANES)
        dst[0, :, window] = new_e
        dst[1, :, window] = new_u
        dst[2, :, window] = new_v
        prev_behind = here_behind
        here, here_behind, here_ahead = nxt, nxt_behind, nxt_ahead


def run_steps(chains, extras, ncol):
    for s in range(STEPS):
        for chain, extra in zip(chains, extras):
            sweep(chain[s], chain[s + 1], ncol, extra if s == 0 else None)


def chain_of(src, out, first, second):
    return [src] + [first if s % 2 == 0 else second for s in range(STEPS - 1)] + [out]


def main_kernel(pos_ref, *refs):
    incs = refs[:-4]
    noise_ref, out_ref, first, second = refs[-4:]
    ncol = noise_ref.shape[-1] // LANES
    chains = [chain_of(incs[k].at[0], out_ref.at[k], first.at[k], second.at[k]) for k in range(len(incs))]
    extras = [noise_ref.at[k] for k in range(len(incs))]
    run_steps(chains, extras, ncol)


def main_forecast(position, incoming, noise):
    per_dev, nf, rows, cols = noise.shape
    group = PAIR if per_dev % PAIR == 0 else 1

    def row_map(k):
        return lambda i, pos: (pos[i * group + k], 0, 0, 0)

    in_specs = [pl.BlockSpec((1, nf, rows, cols), row_map(k)) for k in range(group)]
    spec = pl.BlockSpec((group, nf, rows, cols), lambda i, pos: (i, 0, 0, 0))
    grid_spec = pltpu.PrefetchScalarGridSpec(
        num_scalar_prefetch=1,
        grid=(per_dev // group,),
        in_specs=in_specs + [spec],
        out_specs=spec,
        scratch_shapes=[pltpu.VMEM((group, nf, rows, cols), jnp.float32)] * 2,
    )
    return pl.pallas_call(
        main_kernel,
        grid_spec=grid_spec,
        out_shape=jax.ShapeDtypeStruct(noise.shape, noise.dtype),
    )(position, *([incoming] * group), noise)


def edges_kernel(pos_ref, *refs):
    group = (len(refs) - 3) // 2
    left_rows, right_rows = refs[:group], refs[group:2 * group]
    noise_left, noise_right, own = refs[2 * group:]
    rows = own.shape[-2]
    lane = lax.broadcasted_iota(jnp.int32, (rows, LANES), 1)
    keep_left = (lane < 2 * STEPS) | (lane >= LANES - STEPS)
    for k in range(group):
        for f in range(3):
            left = left_rows[k][0, f] + noise_left[k, f]
            right = pltpu.roll(right_rows[k][0, f] + noise_right[k, f], LANES // 2, 1)
            own[k, f] = jnp.where(keep_left, left, right)


def edge_blocks(position, incoming, noise):
    per_dev, nf, rows, cols = noise.shape
    last = cols // LANES - 1
    group = GATHER_GROUP if per_dev % GATHER_GROUP == 0 else 1

    def row_map(k, col):
        return lambda i, pos: (pos[i * group + k], 0, 0, col)

    left_specs = [pl.BlockSpec((1, nf, rows, LANES), row_map(k, 0)) for k in range(group)]
    right_specs = [pl.BlockSpec((1, nf, rows, LANES), row_map(k, last)) for k in range(group)]
    left = pl.BlockSpec((group, nf, rows, LANES), lambda i, pos: (i, 0, 0, 0))
    right = pl.BlockSpec((group, nf, rows, LANES), lambda i, pos: (i, 0, 0, last))
    out = pl.BlockSpec((group, nf, rows, LANES), lambda i, pos: (i, 0, 0, 0))
    grid_spec = pltpu.PrefetchScalarGridSpec(
        num_scalar_prefetch=1,
        grid=(per_dev // group,),
        in_specs=left_specs + right_specs + [left, right],
        out_specs=out,
    )
    return pl.pallas_call(
        edges_kernel,
        grid_spec=grid_spec,
        out_shape=jax.ShapeDtypeStruct((per_dev, nf, rows, LANES), noise.dtype),
    )(position, *([incoming] * (2 * group)), noise, noise)


def edge_kernel(own, from_left, from_right, body, out, patch, first_buf, last_buf, sems):
    rows = own.shape[-2]
    cols = body.shape[-1]
    group = EDGE_GROUP if own.shape[0] % EDGE_GROUP == 0 else 1
    lane = lax.broadcasted_iota(jnp.int32, (rows, LANES), 1)
    halo_lanes = (lane >= LANES - STEPS) | ((lane >= LANES // 2) & (lane < LANES // 2 + STEPS))
    first_in = pltpu.make_async_copy(body.at[:, :, :, pl.ds(0, LANES)], first_buf, sems.at[0])
    last_in = pltpu.make_async_copy(body.at[:, :, :, pl.ds(cols - LANES, LANES)], last_buf, sems.at[1])
    first_in.start()
    last_in.start()

    def block(g, carry):
        base = g * group
        for k in range(group):
            i = base + k
            fields = []
            for f in range(3):
                received = jnp.where(lane < STEPS, from_right[i, f], from_left[i, f])
                received = pltpu.roll(received, LANES // 2, 1)
                fields.append(jnp.where(halo_lanes, received, own[i, f]))
            e, u, v = fields
            for _ in range(STEPS):
                e, u, v = advance_vreg(e, u, v)
            patch[i, 0] = e
            patch[i, 1] = u
            patch[i, 2] = v
        return carry

    lax.fori_loop(0, own.shape[0] // group, block, 0)
    first_in.wait()
    last_in.wait()

    def merge(i, carry):
        for f in range(3):
            values = patch[i, f]
            first_buf[i, f] = jnp.where(lane < STEPS, values, first_buf[i, f])
            last_buf[i, f] = jnp.where(
                lane >= LANES - STEPS, pltpu.roll(values, LANES // 2, 1), last_buf[i, f]
            )
        return carry

    lax.fori_loop(0, own.shape[0], merge, 0)
    first_out = pltpu.make_async_copy(first_buf, out.at[:, :, :, pl.ds(0, LANES)], sems.at[0])
    last_out = pltpu.make_async_copy(last_buf, out.at[:, :, :, pl.ds(cols - LANES, LANES)], sems.at[1])
    first_out.start()
    last_out.start()
    first_out.wait()
    last_out.wait()


def edge_fix(own, from_left, from_right, body):
    whole = pl.BlockSpec(memory_space=pltpu.VMEM)
    raw = pl.BlockSpec(memory_space=pl.ANY)
    return pl.pallas_call(
        edge_kernel,
        in_specs=[whole, whole, whole, raw],
        out_specs=raw,
        out_shape=jax.ShapeDtypeStruct(body.shape, body.dtype),
        scratch_shapes=[
            pltpu.VMEM(own.shape, jnp.float32),
            pltpu.VMEM(own.shape, jnp.float32),
            pltpu.VMEM(own.shape, jnp.float32),
            pltpu.SemaphoreType.DMA((2,)),
        ],
        input_output_aliases={3: 0},
    )(own, from_left, from_right, body)


def shards(state, noise, parents):
    count = lax.axis_size("ens")
    me = lax.axis_index("ens")
    per_dev = state.shape[0]
    dist = max(1, -(-per_dev // count))
    send_index, position = routing(parents, count, per_dev, dist, me)
    outgoing = jnp.take(state, send_index, axis=0, mode="clip")
    incoming = lax.all_to_all(outgoing, "ens", split_axis=0, concat_axis=0, tiled=True)
    own = edge_blocks(position, incoming, noise)
    ring = lax.axis_size("col")
    from_left = lax.ppermute(own, "col", [(i, (i + 1) % ring) for i in range(ring)])
    from_right = lax.ppermute(own, "col", [(i, (i - 1) % ring) for i in range(ring)])
    body = main_forecast(position, incoming, noise)
    return edge_fix(own, from_left, from_right, body)


def solution(mesh):
    placed = (P("ens", None, None, "col"), P("ens", None, None, "col"), P())
    return jax.shard_map(
        shards, mesh=mesh, in_specs=placed, out_specs=P("ens", None, None, "col"), check_vma=False
    )
```

```python
import jax
import jax.numpy as jnp
from jax import lax
from jax.experimental import pallas as pl
from jax.experimental.pallas import tpu as pltpu
from jax.sharding import PartitionSpec as P

STEPS = 4
LANES = 128
PAIR = 4
EDGE_GROUP = 8
GATHER_GROUP = 32

time_step = 0.3
coriolis = 0.2
gravity = 1.0


def routing(parents, count, per_dev, dist, me):
    blocks = parents.reshape(count, per_dev)
    owner = blocks // per_dev
    local = blocks % per_dev
    ids = jnp.arange(per_dev, dtype=jnp.int32)
    same = blocks[:, :, None] == blocks[:, None, :]
    earlier = ids[None, :] < ids[:, None]
    first = jnp.logical_not(jnp.any(same & earlier[None], axis=2))
    below = (
        (owner[:, :, None] == owner[:, None, :])
        & (blocks[:, None, :] < blocks[:, :, None])
        & first[:, None, :]
    )
    slot = jnp.sum(below.astype(jnp.int32), axis=2)
    slots = jnp.arange(dist, dtype=jnp.int32)
    pick = (owner == me)[:, None, :] & first[:, None, :] & (slot[:, None, :] == slots[None, :, None])
    send_index = jnp.sum(pick.astype(jnp.int32) * local[:, None, :], axis=2).reshape(-1)
    my_owner = lax.dynamic_index_in_dim(owner, me, 0, keepdims=False)
    my_slot = lax.dynamic_index_in_dim(slot, me, 0, keepdims=False)
    return send_index, my_owner * dist + my_slot


def update(e, u, v, xp, xm):
    rows = e.shape[-2]

    def yp(a):
        return pltpu.roll(a, rows - 1, 0)

    def ym(a):
        return pltpu.roll(a, 1, 0)

    e_xp, u_xp, v_xp = xp
    e_xm, u_xm, v_xm = xm
    e_yp, e_ym = yp(e), ym(e)
    u_yp, u_ym = yp(u), ym(u)
    v_yp, v_ym = yp(v), ym(v)
    hu_xp = (1.0 + e_xp) * u_xp
    hu_xm = (1.0 + e_xm) * u_xm
    hv_yp = (1.0 + e_yp) * v_yp
    hv_ym = (1.0 + e_ym) * v_ym
    half_step = 0.5 * time_step
    new_e = 0.25 * (e_xp + e_xm + e_yp + e_ym) - half_step * ((hu_xp - hu_xm) + (hv_yp - hv_ym))
    new_u = (
        0.25 * (u_xp + u_xm + u_yp + u_ym)
        - half_step * (u * (u_xp - u_xm) + v * (u_yp - u_ym) + gravity * (e_xp - e_xm))
        + (time_step * coriolis) * v
    )
    new_v = (
        0.25 * (v_xp + v_xm + v_yp + v_ym)
        - half_step * (u * (v_xp - v_xm) + v * (v_yp - v_ym) + gravity * (e_yp - e_ym))
        - (time_step * coriolis) * u
    )
    return new_e, new_u, new_v


def advance_vreg(e, u, v):
    xp = tuple(pltpu.roll(a, LANES - 1, 1) for a in (e, u, v))
    xm = tuple(pltpu.roll(a, 1, 1) for a in (e, u, v))
    return update(e, u, v, xp, xm)


def sweep(src, dst, ncol, extra=None):
    rows = src.shape[-2]
    lane = lax.broadcasted_iota(jnp.int32, (rows, LANES), 1)
    first_lane = lane == 0
    last_lane = lane == LANES - 1

    def load(j):
        window = pl.ds((j % ncol) * LANES, LANES)
        e = src[0, :, window]
        u = src[1, :, window]
        v = src[2, :, window]
        if extra is not None:
            e = e + extra[0, :, window]
            u = u + extra[1, :, window]
            v = v + extra[2, :, window]
        return e, u, v

    def ahead(vals):
        return tuple(pltpu.roll(a, LANES - 1, 1) for a in vals)

    def behind(vals):
        return tuple(pltpu.roll(a, 1, 1) for a in vals)

    here = load(0)
    prev_behind = behind(load(ncol - 1)) if ncol > 1 else behind(here)
    here_behind = behind(here)
    here_ahead = ahead(here)
    for j in range(ncol):
        if ncol > 1:
            nxt = load(j + 1)
            nxt_ahead = ahead(nxt)
            nxt_behind = behind(nxt)
        else:
            nxt, nxt_ahead, nxt_behind = here, here_ahead, here_behind
        xp = [jnp.where(last_lane, a, b) for a, b in zip(nxt_ahead, here_ahead)]
        xm = [jnp.where(first_lane, a, b) for a, b in zip(prev_behind, here_behind)]
        e, u, v = here
        new_e, new_u, new_v = update(e, u, v, xp, xm)
        window = pl.ds(j * LANES, LANES)
        dst[0, :, window] = new_e
        dst[1, :, window] = new_u
        dst[2, :, window] = new_v
        prev_behind = here_behind
        here, here_behind, here_ahead = nxt, nxt_behind, nxt_ahead


def run_steps(chains, extras, ncol):
    for s in range(STEPS):
        for chain, extra in zip(chains, extras):
            sweep(chain[s], chain[s + 1], ncol, extra if s == 0 else None)


def chain_of(src, out, first, second):
    return [src] + [first if s % 2 == 0 else second for s in range(STEPS - 1)] + [out]


def main_kernel(pos_ref, *refs):
    incs = refs[:-4]
    noise_ref, out_ref, first, second = refs[-4:]
    ncol = noise_ref.shape[-1] // LANES
    chains = [chain_of(incs[k].at[0], out_ref.at[k], first.at[k], second.at[k]) for k in range(len(incs))]
    extras = [noise_ref.at[k] for k in range(len(incs))]
    run_steps(chains, extras, ncol)


def main_forecast(position, incoming, noise):
    per_dev, nf, rows, cols = noise.shape
    group = PAIR if per_dev % PAIR == 0 else 1

    def row_map(k):
        return lambda i, pos: (pos[i * group + k], 0, 0, 0)

    in_specs = [pl.BlockSpec((1, nf, rows, cols), row_map(k)) for k in range(group)]
    spec = pl.BlockSpec((group, nf, rows, cols), lambda i, pos: (i, 0, 0, 0))
    grid_spec = pltpu.PrefetchScalarGridSpec(
        num_scalar_prefetch=1,
        grid=(per_dev // group,),
        in_specs=in_specs + [spec],
        out_specs=spec,
        scratch_shapes=[pltpu.VMEM((group, nf, rows, cols), jnp.float32)] * 2,
    )
    return pl.pallas_call(
        main_kernel,
        grid_spec=grid_spec,
        out_shape=jax.ShapeDtypeStruct(noise.shape, noise.dtype),
    )(position, *([incoming] * group), noise)


def edges_kernel(pos_ref, *refs):
    group = (len(refs) - 3) // 2
    left_rows, right_rows = refs[:group], refs[group:2 * group]
    noise_left, noise_right, own = refs[2 * group:]
    rows = own.shape[-2]
    lane = lax.broadcasted_iota(jnp.int32, (rows, LANES), 1)
    keep_left = (lane < 2 * STEPS) | (lane >= LANES - STEPS)
    for k in range(group):
        for f in range(3):
            left = left_rows[k][0, f] + noise_left[k, f]
            right = pltpu.roll(right_rows[k][0, f] + noise_right[k, f], LANES // 2, 1)
            own[k, f] = jnp.where(keep_left, left, right)


def edge_blocks(position, incoming, noise):
    per_dev, nf, rows, cols = noise.shape
    last = cols // LANES - 1
    group = GATHER_GROUP if per_dev % GATHER_GROUP == 0 else 1

    def row_map(k, col):
        return lambda i, pos: (pos[i * group + k], 0, 0, col)

    left_specs = [pl.BlockSpec((1, nf, rows, LANES), row_map(k, 0)) for k in range(group)]
    right_specs = [pl.BlockSpec((1, nf, rows, LANES), row_map(k, last)) for k in range(group)]
    left = pl.BlockSpec((group, nf, rows, LANES), lambda i, pos: (i, 0, 0, 0))
    right = pl.BlockSpec((group, nf, rows, LANES), lambda i, pos: (i, 0, 0, last))
    out = pl.BlockSpec((group, nf, rows, LANES), lambda i, pos: (i, 0, 0, 0))
    grid_spec = pltpu.PrefetchScalarGridSpec(
        num_scalar_prefetch=1,
        grid=(per_dev // group,),
        in_specs=left_specs + right_specs + [left, right],
        out_specs=out,
    )
    return pl.pallas_call(
        edges_kernel,
        grid_spec=grid_spec,
        out_shape=jax.ShapeDtypeStruct((per_dev, nf, rows, LANES), noise.dtype),
    )(position, *([incoming] * (2 * group)), noise, noise)


def edge_kernel(own, from_left, from_right, body, out, patch, first_buf, last_buf, sems):
    rows = own.shape[-2]
    cols = body.shape[-1]
    lane = lax.broadcasted_iota(jnp.int32, (rows, LANES), 1)
    first_in = pltpu.make_async_copy(body.at[:, :, :, pl.ds(0, LANES)], first_buf, sems.at[0])
    last_in = pltpu.make_async_copy(body.at[:, :, :, pl.ds(cols - LANES, LANES)], last_buf, sems.at[1])
    first_in.start()
    last_in.start()

    slot = 16
    per_vreg = LANES // (2 * slot)
    groups = own.shape[0] // per_vreg

    def span(lo, size):
        return (lane >= lo) & (lane < lo + size)

    def moved(x, shift):
        return pltpu.roll(x, shift % LANES, 1)

    for g in range(groups):
        fields = []
        for f in range(3):
            packed = jnp.zeros((rows, LANES), jnp.float32)
            for k in range(per_vreg):
                i = g * per_vreg + k
                b = 2 * k * slot
                c = b + slot
                mine = own[i, f]
                packed = jnp.where(span(b, STEPS), moved(from_left[i, f], b - (LANES // 2 - STEPS)), packed)
                packed = jnp.where(span(b + STEPS, 2 * STEPS), moved(mine, b + STEPS), packed)
                packed = jnp.where(span(c, 2 * STEPS), moved(mine, c - LANES // 2 + 2 * STEPS), packed)
                packed = jnp.where(span(c + 2 * STEPS, STEPS), moved(from_right[i, f], c + 2 * STEPS), packed)
            fields.append(packed)
        e, u, v = fields
        for _ in range(STEPS):
            e, u, v = advance_vreg(e, u, v)
        patch[g, 0] = e
        patch[g, 1] = u
        patch[g, 2] = v

    first_in.wait()
    last_in.wait()
    for g in range(groups):
        for k in range(per_vreg):
            i = g * per_vreg + k
            b = 2 * k * slot
            c = b + slot
            for f in range(3):
                values = patch[g, f]
                first_buf[i, f] = jnp.where(lane < STEPS, moved(values, -(b + STEPS)), first_buf[i, f])
                last_buf[i, f] = jnp.where(
                    lane >= LANES - STEPS, moved(values, LANES - 2 * STEPS - c), last_buf[i, f]
                )
    first_out = pltpu.make_async_copy(first_buf, out.at[:, :, :, pl.ds(0, LANES)], sems.at[0])
    last_out = pltpu.make_async_copy(last_buf, out.at[:, :, :, pl.ds(cols - LANES, LANES)], sems.at[1])
    first_out.start()
    last_out.start()
    first_out.wait()
    last_out.wait()


def edge_fix(own, from_left, from_right, body):
    whole = pl.BlockSpec(memory_space=pltpu.VMEM)
    raw = pl.BlockSpec(memory_space=pl.ANY)
    return pl.pallas_call(
        edge_kernel,
        in_specs=[whole, whole, whole, raw],
        out_specs=raw,
        out_shape=jax.ShapeDtypeStruct(body.shape, body.dtype),
        scratch_shapes=[
            pltpu.VMEM((own.shape[0] // 4,) + own.shape[1:], jnp.float32),
            pltpu.VMEM(own.shape, jnp.float32),
            pltpu.VMEM(own.shape, jnp.float32),
            pltpu.SemaphoreType.DMA((2,)),
        ],
        input_output_aliases={3: 0},
    )(own, from_left, from_right, body)


def shards(state, noise, parents):
    count = lax.axis_size("ens")
    me = lax.axis_index("ens")
    per_dev = state.shape[0]
    dist = max(1, -(-per_dev // count))
    send_index, position = routing(parents, count, per_dev, dist, me)
    outgoing = jnp.take(state, send_index, axis=0, mode="clip")
    incoming = lax.all_to_all(outgoing, "ens", split_axis=0, concat_axis=0, tiled=True)
    own = edge_blocks(position, incoming, noise)
    ring = lax.axis_size("col")
    from_left = lax.ppermute(own, "col", [(i, (i + 1) % ring) for i in range(ring)])
    from_right = lax.ppermute(own, "col", [(i, (i - 1) % ring) for i in range(ring)])
    body = main_forecast(position, incoming, noise)
    return edge_fix(own, from_left, from_right, body)


def solution(mesh):
    placed = (P("ens", None, None, "col"), P("ens", None, None, "col"), P())
    return jax.shard_map(
        shards, mesh=mesh, in_specs=placed, out_specs=P("ens", None, None, "col"), check_vma=False
    )
```

```python
import jax
import jax.numpy as jnp
from jax import lax
from jax.experimental import pallas as pl
from jax.experimental.pallas import tpu as pltpu
from jax.sharding import PartitionSpec as P

STEPS = 4
LANES = 128
PAIR = 4
EDGE_GROUP = 8
GATHER_GROUP = 32

time_step = 0.3
coriolis = 0.2
gravity = 1.0


def routing(parents, count, per_dev, dist, me):
    blocks = parents.reshape(count, per_dev)
    owner = blocks // per_dev
    local = blocks % per_dev
    ids = jnp.arange(per_dev, dtype=jnp.int32)
    same = blocks[:, :, None] == blocks[:, None, :]
    earlier = ids[None, :] < ids[:, None]
    first = jnp.logical_not(jnp.any(same & earlier[None], axis=2))
    below = (
        (owner[:, :, None] == owner[:, None, :])
        & (blocks[:, None, :] < blocks[:, :, None])
        & first[:, None, :]
    )
    slot = jnp.sum(below.astype(jnp.int32), axis=2)
    slots = jnp.arange(dist, dtype=jnp.int32)
    pick = (owner == me)[:, None, :] & first[:, None, :] & (slot[:, None, :] == slots[None, :, None])
    send_index = jnp.sum(pick.astype(jnp.int32) * local[:, None, :], axis=2).reshape(-1)
    my_owner = lax.dynamic_index_in_dim(owner, me, 0, keepdims=False)
    my_slot = lax.dynamic_index_in_dim(slot, me, 0, keepdims=False)
    return send_index, my_owner * dist + my_slot


def update(e, u, v, xp, xm):
    rows = e.shape[-2]

    def yp(a):
        return pltpu.roll(a, rows - 1, 0)

    def ym(a):
        return pltpu.roll(a, 1, 0)

    e_xp, u_xp, v_xp = xp
    e_xm, u_xm, v_xm = xm
    e_yp, e_ym = yp(e), ym(e)
    u_yp, u_ym = yp(u), ym(u)
    v_yp, v_ym = yp(v), ym(v)
    hu_xp = (1.0 + e_xp) * u_xp
    hu_xm = (1.0 + e_xm) * u_xm
    hv_yp = (1.0 + e_yp) * v_yp
    hv_ym = (1.0 + e_ym) * v_ym
    half_step = 0.5 * time_step
    new_e = 0.25 * (e_xp + e_xm + e_yp + e_ym) - half_step * ((hu_xp - hu_xm) + (hv_yp - hv_ym))
    new_u = (
        0.25 * (u_xp + u_xm + u_yp + u_ym)
        - half_step * (u * (u_xp - u_xm) + v * (u_yp - u_ym) + gravity * (e_xp - e_xm))
        + (time_step * coriolis) * v
    )
    new_v = (
        0.25 * (v_xp + v_xm + v_yp + v_ym)
        - half_step * (u * (v_xp - v_xm) + v * (v_yp - v_ym) + gravity * (e_yp - e_ym))
        - (time_step * coriolis) * u
    )
    return new_e, new_u, new_v


def advance_vreg(e, u, v):
    xp = tuple(pltpu.roll(a, LANES - 1, 1) for a in (e, u, v))
    xm = tuple(pltpu.roll(a, 1, 1) for a in (e, u, v))
    return update(e, u, v, xp, xm)


def sweep(src, dst, ncol, extra=None):
    rows = src.shape[-2]
    lane = lax.broadcasted_iota(jnp.int32, (rows, LANES), 1)
    first_lane = lane == 0
    last_lane = lane == LANES - 1

    def load(j):
        window = pl.ds((j % ncol) * LANES, LANES)
        e = src[0, :, window]
        u = src[1, :, window]
        v = src[2, :, window]
        if extra is not None:
            e = e + extra[0, :, window]
            u = u + extra[1, :, window]
            v = v + extra[2, :, window]
        return e, u, v

    def ahead(vals):
        return tuple(pltpu.roll(a, LANES - 1, 1) for a in vals)

    def behind(vals):
        return tuple(pltpu.roll(a, 1, 1) for a in vals)

    here = load(0)
    prev_behind = behind(load(ncol - 1)) if ncol > 1 else behind(here)
    here_behind = behind(here)
    here_ahead = ahead(here)
    for j in range(ncol):
        if ncol > 1:
            nxt = load(j + 1)
            nxt_ahead = ahead(nxt)
            nxt_behind = behind(nxt)
        else:
            nxt, nxt_ahead, nxt_behind = here, here_ahead, here_behind
        xp = [jnp.where(last_lane, a, b) for a, b in zip(nxt_ahead, here_ahead)]
        xm = [jnp.where(first_lane, a, b) for a, b in zip(prev_behind, here_behind)]
        e, u, v = here
        new_e, new_u, new_v = update(e, u, v, xp, xm)
        window = pl.ds(j * LANES, LANES)
        dst[0, :, window] = new_e
        dst[1, :, window] = new_u
        dst[2, :, window] = new_v
        prev_behind = here_behind
        here, here_behind, here_ahead = nxt, nxt_behind, nxt_ahead


def run_steps(chains, extras, ncol):
    for s in range(STEPS):
        for chain, extra in zip(chains, extras):
            sweep(chain[s], chain[s + 1], ncol, extra if s == 0 else None)


def chain_of(src, out, first, second):
    return [src] + [first if s % 2 == 0 else second for s in range(STEPS - 1)] + [out]


def main_kernel(pos_ref, *refs):
    incs = refs[:-4]
    noise_ref, out_ref, first, second = refs[-4:]
    ncol = noise_ref.shape[-1] // LANES
    chains = [chain_of(incs[k].at[0], out_ref.at[k], first.at[k], second.at[k]) for k in range(len(incs))]
    extras = [noise_ref.at[k] for k in range(len(incs))]
    run_steps(chains, extras, ncol)


def main_forecast(position, incoming, noise):
    per_dev, nf, rows, cols = noise.shape
    group = PAIR if per_dev % PAIR == 0 else 1

    def row_map(k):
        return lambda i, pos: (pos[i * group + k], 0, 0, 0)

    in_specs = [pl.BlockSpec((1, nf, rows, cols), row_map(k)) for k in range(group)]
    spec = pl.BlockSpec((group, nf, rows, cols), lambda i, pos: (i, 0, 0, 0))
    grid_spec = pltpu.PrefetchScalarGridSpec(
        num_scalar_prefetch=1,
        grid=(per_dev // group,),
        in_specs=in_specs + [spec],
        out_specs=spec,
        scratch_shapes=[pltpu.VMEM((group, nf, rows, cols), jnp.float32)] * 2,
    )
    return pl.pallas_call(
        main_kernel,
        grid_spec=grid_spec,
        out_shape=jax.ShapeDtypeStruct(noise.shape, noise.dtype),
    )(position, *([incoming] * group), noise)


def edges_kernel(pos_ref, inc_left, inc_right, noise_left, noise_right, own):
    rows = own.shape[-2]
    lane = lax.broadcasted_iota(jnp.int32, (rows, LANES), 1)
    keep_left = (lane < 2 * STEPS) | (lane >= LANES - STEPS)

    def particle(k, carry):
        row = pos_ref[k]
        for f in range(3):
            left = inc_left[row, f] + noise_left[k, f]
            right = pltpu.roll(inc_right[row, f] + noise_right[k, f], LANES // 2, 1)
            own[k, f] = jnp.where(keep_left, left, right)
        return carry

    lax.fori_loop(0, own.shape[0], particle, 0)


def edge_blocks(position, incoming, noise):
    per_dev, nf, rows, cols = noise.shape
    last = cols // LANES - 1
    sources = incoming.shape[0]
    inc_first = pl.BlockSpec((sources, nf, rows, LANES), lambda i, pos: (0, 0, 0, 0))
    inc_last = pl.BlockSpec((sources, nf, rows, LANES), lambda i, pos: (0, 0, 0, last))
    first = pl.BlockSpec((per_dev, nf, rows, LANES), lambda i, pos: (0, 0, 0, 0))
    final = pl.BlockSpec((per_dev, nf, rows, LANES), lambda i, pos: (0, 0, 0, last))
    grid_spec = pltpu.PrefetchScalarGridSpec(
        num_scalar_prefetch=1,
        grid=(1,),
        in_specs=[inc_first, inc_last, first, final],
        out_specs=first,
    )
    return pl.pallas_call(
        edges_kernel,
        grid_spec=grid_spec,
        out_shape=jax.ShapeDtypeStruct((per_dev, nf, rows, LANES), noise.dtype),
    )(position, incoming, incoming, noise, noise)


def edge_kernel(own, from_left, from_right, body, out, patch, first_buf, last_buf, sems):
    rows = own.shape[-2]
    cols = body.shape[-1]
    lane = lax.broadcasted_iota(jnp.int32, (rows, LANES), 1)
    first_in = pltpu.make_async_copy(body.at[:, :, :, pl.ds(0, LANES)], first_buf, sems.at[0])
    last_in = pltpu.make_async_copy(body.at[:, :, :, pl.ds(cols - LANES, LANES)], last_buf, sems.at[1])
    first_in.start()
    last_in.start()

    slot = 16
    per_vreg = LANES // (2 * slot)
    groups = own.shape[0] // per_vreg

    def span(lo, size):
        return (lane >= lo) & (lane < lo + size)

    def moved(x, shift):
        return pltpu.roll(x, shift % LANES, 1)

    for g in range(groups):
        fields = []
        for f in range(3):
            packed = jnp.zeros((rows, LANES), jnp.float32)
            for k in range(per_vreg):
                i = g * per_vreg + k
                b = 2 * k * slot
                c = b + slot
                mine = own[i, f]
                packed = jnp.where(span(b, STEPS), moved(from_left[i, f], b - (LANES // 2 - STEPS)), packed)
                packed = jnp.where(span(b + STEPS, 2 * STEPS), moved(mine, b + STEPS), packed)
                packed = jnp.where(span(c, 2 * STEPS), moved(mine, c - LANES // 2 + 2 * STEPS), packed)
                packed = jnp.where(span(c + 2 * STEPS, STEPS), moved(from_right[i, f], c + 2 * STEPS), packed)
            fields.append(packed)
        e, u, v = fields
        for _ in range(STEPS):
            e, u, v = advance_vreg(e, u, v)
        patch[g, 0] = e
        patch[g, 1] = u
        patch[g, 2] = v

    first_in.wait()
    last_in.wait()
    for g in range(groups):
        for k in range(per_vreg):
            i = g * per_vreg + k
            b = 2 * k * slot
            c = b + slot
            for f in range(3):
                values = patch[g, f]
                first_buf[i, f] = jnp.where(lane < STEPS, moved(values, -(b + STEPS)), first_buf[i, f])
                last_buf[i, f] = jnp.where(
                    lane >= LANES - STEPS, moved(values, LANES - 2 * STEPS - c), last_buf[i, f]
                )
    first_out = pltpu.make_async_copy(first_buf, out.at[:, :, :, pl.ds(0, LANES)], sems.at[0])
    last_out = pltpu.make_async_copy(last_buf, out.at[:, :, :, pl.ds(cols - LANES, LANES)], sems.at[1])
    first_out.start()
    last_out.start()
    first_out.wait()
    last_out.wait()


def edge_fix(own, from_left, from_right, body):
    whole = pl.BlockSpec(memory_space=pltpu.VMEM)
    raw = pl.BlockSpec(memory_space=pl.ANY)
    return pl.pallas_call(
        edge_kernel,
        in_specs=[whole, whole, whole, raw],
        out_specs=raw,
        out_shape=jax.ShapeDtypeStruct(body.shape, body.dtype),
        scratch_shapes=[
            pltpu.VMEM((own.shape[0] // 4,) + own.shape[1:], jnp.float32),
            pltpu.VMEM(own.shape, jnp.float32),
            pltpu.VMEM(own.shape, jnp.float32),
            pltpu.SemaphoreType.DMA((2,)),
        ],
        input_output_aliases={3: 0},
    )(own, from_left, from_right, body)


def shards(state, noise, parents):
    count = lax.axis_size("ens")
    me = lax.axis_index("ens")
    per_dev = state.shape[0]
    dist = max(1, -(-per_dev // count))
    send_index, position = routing(parents, count, per_dev, dist, me)
    outgoing = jnp.take(state, send_index, axis=0, mode="clip")
    incoming = lax.all_to_all(outgoing, "ens", split_axis=0, concat_axis=0, tiled=True)
    own = edge_blocks(position, incoming, noise)
    ring = lax.axis_size("col")
    from_left = lax.ppermute(own, "col", [(i, (i + 1) % ring) for i in range(ring)])
    from_right = lax.ppermute(own, "col", [(i, (i - 1) % ring) for i in range(ring)])
    body = main_forecast(position, incoming, noise)
    return edge_fix(own, from_left, from_right, body)


def solution(mesh):
    placed = (P("ens", None, None, "col"), P("ens", None, None, "col"), P())
    return jax.shard_map(
        shards, mesh=mesh, in_specs=placed, out_specs=P("ens", None, None, "col"), check_vma=False
    )
```

```python
import jax
import jax.numpy as jnp
from jax import lax
from jax.experimental import pallas as pl
from jax.experimental.pallas import tpu as pltpu
from jax.sharding import PartitionSpec as P

STEPS = 4
LANES = 128
PAIR = 8
EDGE_GROUP = 8
GATHER_GROUP = 32

time_step = 0.3
coriolis = 0.2
gravity = 1.0


def routing(parents, count, per_dev, dist, me):
    blocks = parents.reshape(count, per_dev)
    owner = blocks // per_dev
    local = blocks % per_dev
    ids = jnp.arange(per_dev, dtype=jnp.int32)
    same = blocks[:, :, None] == blocks[:, None, :]
    earlier = ids[None, :] < ids[:, None]
    first = jnp.logical_not(jnp.any(same & earlier[None], axis=2))
    below = (
        (owner[:, :, None] == owner[:, None, :])
        & (blocks[:, None, :] < blocks[:, :, None])
        & first[:, None, :]
    )
    slot = jnp.sum(below.astype(jnp.int32), axis=2)
    slots = jnp.arange(dist, dtype=jnp.int32)
    pick = (owner == me)[:, None, :] & first[:, None, :] & (slot[:, None, :] == slots[None, :, None])
    send_index = jnp.sum(pick.astype(jnp.int32) * local[:, None, :], axis=2).reshape(-1)
    my_owner = lax.dynamic_index_in_dim(owner, me, 0, keepdims=False)
    my_slot = lax.dynamic_index_in_dim(slot, me, 0, keepdims=False)
    return send_index, my_owner * dist + my_slot


def update(e, u, v, xp, xm):
    rows = e.shape[-2]

    def yp(a):
        return pltpu.roll(a, rows - 1, 0)

    def ym(a):
        return pltpu.roll(a, 1, 0)

    e_xp, u_xp, v_xp = xp
    e_xm, u_xm, v_xm = xm
    e_yp, e_ym = yp(e), ym(e)
    u_yp, u_ym = yp(u), ym(u)
    v_yp, v_ym = yp(v), ym(v)
    dx_u = u_xp - u_xm
    dy_v = v_yp - v_ym
    dx_hu = dx_u + (e_xp * u_xp - e_xm * u_xm)
    dy_hv = dy_v + (e_yp * v_yp - e_ym * v_ym)
    half_step = 0.5 * time_step
    new_e = 0.25 * (e_xp + e_xm + e_yp + e_ym) - half_step * (dx_hu + dy_hv)
    new_u = (
        0.25 * (u_xp + u_xm + u_yp + u_ym)
        - half_step * (u * dx_u + v * (u_yp - u_ym) + gravity * (e_xp - e_xm))
        + (time_step * coriolis) * v
    )
    new_v = (
        0.25 * (v_xp + v_xm + v_yp + v_ym)
        - half_step * (u * (v_xp - v_xm) + v * dy_v + gravity * (e_yp - e_ym))
        - (time_step * coriolis) * u
    )
    return new_e, new_u, new_v


def advance_vreg(e, u, v):
    xp = tuple(pltpu.roll(a, LANES - 1, 1) for a in (e, u, v))
    xm = tuple(pltpu.roll(a, 1, 1) for a in (e, u, v))
    return update(e, u, v, xp, xm)


def sweep(src, dst, ncol, extra=None):
    rows = src.shape[-2]
    lane = lax.broadcasted_iota(jnp.int32, (rows, LANES), 1)
    first_lane = lane == 0
    last_lane = lane == LANES - 1

    def load(j):
        window = pl.ds((j % ncol) * LANES, LANES)
        e = src[0, :, window]
        u = src[1, :, window]
        v = src[2, :, window]
        if extra is not None:
            e = e + extra[0, :, window]
            u = u + extra[1, :, window]
            v = v + extra[2, :, window]
        return e, u, v

    def ahead(vals):
        return tuple(pltpu.roll(a, LANES - 1, 1) for a in vals)

    def behind(vals):
        return tuple(pltpu.roll(a, 1, 1) for a in vals)

    here = load(0)
    prev_behind = behind(load(ncol - 1)) if ncol > 1 else behind(here)
    here_behind = behind(here)
    here_ahead = ahead(here)
    for j in range(ncol):
        if ncol > 1:
            nxt = load(j + 1)
            nxt_ahead = ahead(nxt)
            nxt_behind = behind(nxt)
        else:
            nxt, nxt_ahead, nxt_behind = here, here_ahead, here_behind
        xp = [jnp.where(last_lane, a, b) for a, b in zip(nxt_ahead, here_ahead)]
        xm = [jnp.where(first_lane, a, b) for a, b in zip(prev_behind, here_behind)]
        e, u, v = here
        new_e, new_u, new_v = update(e, u, v, xp, xm)
        window = pl.ds(j * LANES, LANES)
        dst[0, :, window] = new_e
        dst[1, :, window] = new_u
        dst[2, :, window] = new_v
        prev_behind = here_behind
        here, here_behind, here_ahead = nxt, nxt_behind, nxt_ahead


def run_steps(chains, extras, ncol):
    for s in range(STEPS):
        for chain, extra in zip(chains, extras):
            sweep(chain[s], chain[s + 1], ncol, extra if s == 0 else None)


def chain_of(src, out, first, second):
    return [src] + [first if s % 2 == 0 else second for s in range(STEPS - 1)] + [out]


def main_kernel(pos_ref, *refs):
    incs = refs[:-4]
    noise_ref, out_ref, first, second = refs[-4:]
    ncol = noise_ref.shape[-1] // LANES
    chains = [chain_of(incs[k].at[0], out_ref.at[k], first.at[k], second.at[k]) for k in range(len(incs))]
    extras = [noise_ref.at[k] for k in range(len(incs))]
    run_steps(chains, extras, ncol)


def main_forecast(position, incoming, noise):
    per_dev, nf, rows, cols = noise.shape
    group = PAIR if per_dev % PAIR == 0 else 1

    def row_map(k):
        return lambda i, pos: (pos[i * group + k], 0, 0, 0)

    in_specs = [pl.BlockSpec((1, nf, rows, cols), row_map(k)) for k in range(group)]
    spec = pl.BlockSpec((group, nf, rows, cols), lambda i, pos: (i, 0, 0, 0))
    grid_spec = pltpu.PrefetchScalarGridSpec(
        num_scalar_prefetch=1,
        grid=(per_dev // group,),
        in_specs=in_specs + [spec],
        out_specs=spec,
        scratch_shapes=[pltpu.VMEM((group, nf, rows, cols), jnp.float32)] * 2,
    )
    return pl.pallas_call(
        main_kernel,
        grid_spec=grid_spec,
        out_shape=jax.ShapeDtypeStruct(noise.shape, noise.dtype),
    )(position, *([incoming] * group), noise)


def edges_kernel(pos_ref, *refs):
    group = (len(refs) - 3) // 2
    left_rows, right_rows = refs[:group], refs[group:2 * group]
    noise_left, noise_right, own = refs[2 * group:]
    rows = own.shape[-2]
    lane = lax.broadcasted_iota(jnp.int32, (rows, LANES), 1)
    keep_left = (lane < 2 * STEPS) | (lane >= LANES - STEPS)
    for k in range(group):
        for f in range(3):
            left = left_rows[k][0, f] + noise_left[k, f]
            right = pltpu.roll(right_rows[k][0, f] + noise_right[k, f], LANES // 2, 1)
            own[k, f] = jnp.where(keep_left, left, right)


def edge_blocks(position, incoming, noise):
    per_dev, nf, rows, cols = noise.shape
    last = cols // LANES - 1
    group = GATHER_GROUP if per_dev % GATHER_GROUP == 0 else 1

    def row_map(k, col):
        return lambda i, pos: (pos[i * group + k], 0, 0, col)

    left_specs = [pl.BlockSpec((1, nf, rows, LANES), row_map(k, 0)) for k in range(group)]
    right_specs = [pl.BlockSpec((1, nf, rows, LANES), row_map(k, last)) for k in range(group)]
    left = pl.BlockSpec((group, nf, rows, LANES), lambda i, pos: (i, 0, 0, 0))
    right = pl.BlockSpec((group, nf, rows, LANES), lambda i, pos: (i, 0, 0, last))
    out = pl.BlockSpec((group, nf, rows, LANES), lambda i, pos: (i, 0, 0, 0))
    grid_spec = pltpu.PrefetchScalarGridSpec(
        num_scalar_prefetch=1,
        grid=(per_dev // group,),
        in_specs=left_specs + right_specs + [left, right],
        out_specs=out,
    )
    return pl.pallas_call(
        edges_kernel,
        grid_spec=grid_spec,
        out_shape=jax.ShapeDtypeStruct((per_dev, nf, rows, LANES), noise.dtype),
    )(position, *([incoming] * (2 * group)), noise, noise)


def edge_kernel(own, from_left, from_right, body, out, patch, first_buf, last_buf, sems):
    rows = own.shape[-2]
    cols = body.shape[-1]
    lane = lax.broadcasted_iota(jnp.int32, (rows, LANES), 1)
    first_in = pltpu.make_async_copy(body.at[:, :, :, pl.ds(0, LANES)], first_buf, sems.at[0])
    last_in = pltpu.make_async_copy(body.at[:, :, :, pl.ds(cols - LANES, LANES)], last_buf, sems.at[1])
    first_in.start()
    last_in.start()

    slot = 16
    per_vreg = LANES // (2 * slot)
    groups = own.shape[0] // per_vreg

    def span(lo, size):
        return (lane >= lo) & (lane < lo + size)

    def moved(x, shift):
        return pltpu.roll(x, shift % LANES, 1)

    for g in range(groups):
        fields = []
        for f in range(3):
            packed = jnp.zeros((rows, LANES), jnp.float32)
            for k in range(per_vreg):
                i = g * per_vreg + k
                b = 2 * k * slot
                c = b + slot
                mine = own[i, f]
                packed = jnp.where(span(b, STEPS), moved(from_left[i, f], b - (LANES // 2 - STEPS)), packed)
                packed = jnp.where(span(b + STEPS, 2 * STEPS), moved(mine, b + STEPS), packed)
                packed = jnp.where(span(c, 2 * STEPS), moved(mine, c - LANES // 2 + 2 * STEPS), packed)
                packed = jnp.where(span(c + 2 * STEPS, STEPS), moved(from_right[i, f], c + 2 * STEPS), packed)
            fields.append(packed)
        e, u, v = fields
        for _ in range(STEPS):
            e, u, v = advance_vreg(e, u, v)
        patch[g, 0] = e
        patch[g, 1] = u
        patch[g, 2] = v

    first_in.wait()
    last_in.wait()
    for g in range(groups):
        for k in range(per_vreg):
            i = g * per_vreg + k
            b = 2 * k * slot
            c = b + slot
            for f in range(3):
                values = patch[g, f]
                first_buf[i, f] = jnp.where(lane < STEPS, moved(values, -(b + STEPS)), first_buf[i, f])
                last_buf[i, f] = jnp.where(
                    lane >= LANES - STEPS, moved(values, LANES - 2 * STEPS - c), last_buf[i, f]
                )
    first_out = pltpu.make_async_copy(first_buf, out.at[:, :, :, pl.ds(0, LANES)], sems.at[0])
    last_out = pltpu.make_async_copy(last_buf, out.at[:, :, :, pl.ds(cols - LANES, LANES)], sems.at[1])
    first_out.start()
    last_out.start()
    first_out.wait()
    last_out.wait()


def edge_fix(own, from_left, from_right, body):
    whole = pl.BlockSpec(memory_space=pltpu.VMEM)
    raw = pl.BlockSpec(memory_space=pl.ANY)
    return pl.pallas_call(
        edge_kernel,
        in_specs=[whole, whole, whole, raw],
        out_specs=raw,
        out_shape=jax.ShapeDtypeStruct(body.shape, body.dtype),
        scratch_shapes=[
            pltpu.VMEM((own.shape[0] // 4,) + own.shape[1:], jnp.float32),
            pltpu.VMEM(own.shape, jnp.float32),
            pltpu.VMEM(own.shape, jnp.float32),
            pltpu.SemaphoreType.DMA((2,)),
        ],
        input_output_aliases={3: 0},
    )(own, from_left, from_right, body)


def shards(state, noise, parents):
    count = lax.axis_size("ens")
    me = lax.axis_index("ens")
    per_dev = state.shape[0]
    dist = max(1, -(-per_dev // count))
    send_index, position = routing(parents, count, per_dev, dist, me)
    outgoing = jnp.take(state, send_index, axis=0, mode="clip")
    incoming = lax.all_to_all(outgoing, "ens", split_axis=0, concat_axis=0, tiled=True)
    own = edge_blocks(position, incoming, noise)
    ring = lax.axis_size("col")
    from_left = lax.ppermute(own, "col", [(i, (i + 1) % ring) for i in range(ring)])
    from_right = lax.ppermute(own, "col", [(i, (i - 1) % ring) for i in range(ring)])
    body = main_forecast(position, incoming, noise)
    return edge_fix(own, from_left, from_right, body)


def solution(mesh):
    placed = (P("ens", None, None, "col"), P("ens", None, None, "col"), P())
    return jax.shard_map(
        shards, mesh=mesh, in_specs=placed, out_specs=P("ens", None, None, "col"), check_vma=False
    )
```

```python
import jax
import jax.numpy as jnp
from jax import lax
from jax.experimental import pallas as pl
from jax.experimental.pallas import tpu as pltpu
from jax.sharding import PartitionSpec as P

STEPS = 4
LANES = 128
PAIR = 8
EDGE_GROUP = 8
GATHER_GROUP = 32

time_step = 0.3
coriolis = 0.2
gravity = 1.0


def routing(parents, count, per_dev, dist, me):
    total = count * per_dev
    ids = jnp.arange(total, dtype=jnp.int32)
    block = ids // per_dev
    owner = parents // per_dev
    local = parents % per_dev
    same_block = block[:, None] == block[None, :]
    earlier = ids[None, :] < ids[:, None]
    same = parents[:, None] == parents[None, :]
    first = jnp.logical_not(jnp.any(same_block & earlier & same, axis=1))
    below = same_block & (owner[:, None] == owner[None, :]) & (parents[None, :] < parents[:, None]) & first[None, :]
    slot = jnp.sum(below.astype(jnp.int32), axis=1)
    sending = (owner == me) & first
    key = jnp.where(sending, block * dist + slot, -1)
    targets = jnp.arange(count * dist, dtype=jnp.int32)
    send_index = jnp.sum(jnp.where(key[None, :] == targets[:, None], local[None, :], 0), axis=1)
    my_owner = lax.dynamic_slice_in_dim(owner, me * per_dev, per_dev)
    my_slot = lax.dynamic_slice_in_dim(slot, me * per_dev, per_dev)
    return send_index, my_owner * dist + my_slot


def update(e, u, v, xp, xm):
    rows = e.shape[-2]

    def yp(a):
        return pltpu.roll(a, rows - 1, 0)

    def ym(a):
        return pltpu.roll(a, 1, 0)

    e_xp, u_xp, v_xp = xp
    e_xm, u_xm, v_xm = xm
    e_yp, e_ym = yp(e), ym(e)
    u_yp, u_ym = yp(u), ym(u)
    v_yp, v_ym = yp(v), ym(v)
    dx_u = u_xp - u_xm
    dy_v = v_yp - v_ym
    dx_hu = dx_u + (e_xp * u_xp - e_xm * u_xm)
    dy_hv = dy_v + (e_yp * v_yp - e_ym * v_ym)
    half_step = 0.5 * time_step
    new_e = 0.25 * (e_xp + e_xm + e_yp + e_ym) - half_step * (dx_hu + dy_hv)
    new_u = (
        0.25 * (u_xp + u_xm + u_yp + u_ym)
        - half_step * (u * dx_u + v * (u_yp - u_ym) + gravity * (e_xp - e_xm))
        + (time_step * coriolis) * v
    )
    new_v = (
        0.25 * (v_xp + v_xm + v_yp + v_ym)
        - half_step * (u * (v_xp - v_xm) + v * dy_v + gravity * (e_yp - e_ym))
        - (time_step * coriolis) * u
    )
    return new_e, new_u, new_v


def advance_vreg(e, u, v):
    xp = tuple(pltpu.roll(a, LANES - 1, 1) for a in (e, u, v))
    xm = tuple(pltpu.roll(a, 1, 1) for a in (e, u, v))
    return update(e, u, v, xp, xm)


def sweep(src, dst, ncol, extra=None):
    rows = src.shape[-2]
    lane = lax.broadcasted_iota(jnp.int32, (rows, LANES), 1)
    first_lane = lane == 0
    last_lane = lane == LANES - 1

    def load(j):
        window = pl.ds((j % ncol) * LANES, LANES)
        e = src[0, :, window]
        u = src[1, :, window]
        v = src[2, :, window]
        if extra is not None:
            e = e + extra[0, :, window]
            u = u + extra[1, :, window]
            v = v + extra[2, :, window]
        return e, u, v

    def ahead(vals):
        return tuple(pltpu.roll(a, LANES - 1, 1) for a in vals)

    def behind(vals):
        return tuple(pltpu.roll(a, 1, 1) for a in vals)

    here = load(0)
    prev_behind = behind(load(ncol - 1)) if ncol > 1 else behind(here)
    here_behind = behind(here)
    here_ahead = ahead(here)
    for j in range(ncol):
        if ncol > 1:
            nxt = load(j + 1)
            nxt_ahead = ahead(nxt)
            nxt_behind = behind(nxt)
        else:
            nxt, nxt_ahead, nxt_behind = here, here_ahead, here_behind
        xp = [jnp.where(last_lane, a, b) for a, b in zip(nxt_ahead, here_ahead)]
        xm = [jnp.where(first_lane, a, b) for a, b in zip(prev_behind, here_behind)]
        e, u, v = here
        new_e, new_u, new_v = update(e, u, v, xp, xm)
        window = pl.ds(j * LANES, LANES)
        dst[0, :, window] = new_e
        dst[1, :, window] = new_u
        dst[2, :, window] = new_v
        prev_behind = here_behind
        here, here_behind, here_ahead = nxt, nxt_behind, nxt_ahead


def run_steps(chains, extras, ncol):
    for s in range(STEPS):
        for chain, extra in zip(chains, extras):
            sweep(chain[s], chain[s + 1], ncol, extra if s == 0 else None)


def chain_of(src, out, first, second):
    return [src] + [first if s % 2 == 0 else second for s in range(STEPS - 1)] + [out]


def main_kernel(pos_ref, *refs):
    incs = refs[:-4]
    noise_ref, out_ref, first, second = refs[-4:]
    ncol = noise_ref.shape[-1] // LANES
    chains = [chain_of(incs[k].at[0], out_ref.at[k], first.at[k], second.at[k]) for k in range(len(incs))]
    extras = [noise_ref.at[k] for k in range(len(incs))]
    run_steps(chains, extras, ncol)


def main_forecast(position, incoming, noise):
    per_dev, nf, rows, cols = noise.shape
    group = PAIR if per_dev % PAIR == 0 else 1

    def row_map(k):
        return lambda i, pos: (pos[i * group + k], 0, 0, 0)

    in_specs = [pl.BlockSpec((1, nf, rows, cols), row_map(k)) for k in range(group)]
    spec = pl.BlockSpec((group, nf, rows, cols), lambda i, pos: (i, 0, 0, 0))
    grid_spec = pltpu.PrefetchScalarGridSpec(
        num_scalar_prefetch=1,
        grid=(per_dev // group,),
        in_specs=in_specs + [spec],
        out_specs=spec,
        scratch_shapes=[pltpu.VMEM((group, nf, rows, cols), jnp.float32)] * 2,
    )
    return pl.pallas_call(
        main_kernel,
        grid_spec=grid_spec,
        out_shape=jax.ShapeDtypeStruct(noise.shape, noise.dtype),
    )(position, *([incoming] * group), noise)


def edges_kernel(pos_ref, *refs):
    group = (len(refs) - 3) // 2
    left_rows, right_rows = refs[:group], refs[group:2 * group]
    noise_left, noise_right, own = refs[2 * group:]
    rows = own.shape[-2]
    lane = lax.broadcasted_iota(jnp.int32, (rows, LANES), 1)
    keep_left = (lane < 2 * STEPS) | (lane >= LANES - STEPS)
    for k in range(group):
        for f in range(3):
            left = left_rows[k][0, f] + noise_left[k, f]
            right = pltpu.roll(right_rows[k][0, f] + noise_right[k, f], LANES // 2, 1)
            own[k, f] = jnp.where(keep_left, left, right)


def edge_blocks(position, incoming, noise):
    per_dev, nf, rows, cols = noise.shape
    last = cols // LANES - 1
    group = GATHER_GROUP if per_dev % GATHER_GROUP == 0 else 1

    def row_map(k, col):
        return lambda i, pos: (pos[i * group + k], 0, 0, col)

    left_specs = [pl.BlockSpec((1, nf, rows, LANES), row_map(k, 0)) for k in range(group)]
    right_specs = [pl.BlockSpec((1, nf, rows, LANES), row_map(k, last)) for k in range(group)]
    left = pl.BlockSpec((group, nf, rows, LANES), lambda i, pos: (i, 0, 0, 0))
    right = pl.BlockSpec((group, nf, rows, LANES), lambda i, pos: (i, 0, 0, last))
    out = pl.BlockSpec((group, nf, rows, LANES), lambda i, pos: (i, 0, 0, 0))
    grid_spec = pltpu.PrefetchScalarGridSpec(
        num_scalar_prefetch=1,
        grid=(per_dev // group,),
        in_specs=left_specs + right_specs + [left, right],
        out_specs=out,
    )
    return pl.pallas_call(
        edges_kernel,
        grid_spec=grid_spec,
        out_shape=jax.ShapeDtypeStruct((per_dev, nf, rows, LANES), noise.dtype),
    )(position, *([incoming] * (2 * group)), noise, noise)


def edge_kernel(own_hbm, left_hbm, right_hbm, body, out, patch, first_buf, last_buf, own, from_left, from_right, sems):
    rows = own.shape[-2]
    cols = body.shape[-1]
    lane = lax.broadcasted_iota(jnp.int32, (rows, LANES), 1)
    staged = [
        pltpu.make_async_copy(src, dst, sems.at[2 + n])
        for n, (src, dst) in enumerate(((own_hbm, own), (left_hbm, from_left), (right_hbm, from_right)))
    ]
    for copy in staged:
        copy.start()
    first_in = pltpu.make_async_copy(body.at[:, :, :, pl.ds(0, LANES)], first_buf, sems.at[0])
    last_in = pltpu.make_async_copy(body.at[:, :, :, pl.ds(cols - LANES, LANES)], last_buf, sems.at[1])
    first_in.start()
    last_in.start()
    for copy in staged:
        copy.wait()

    slot = 16
    per_vreg = LANES // (2 * slot)
    groups = own.shape[0] // per_vreg

    def span(lo, size):
        return (lane >= lo) & (lane < lo + size)

    def moved(x, shift):
        return pltpu.roll(x, shift % LANES, 1)

    for g in range(groups):
        fields = []
        for f in range(3):
            packed = jnp.zeros((rows, LANES), jnp.float32)
            for k in range(per_vreg):
                i = g * per_vreg + k
                b = 2 * k * slot
                c = b + slot
                mine = own[i, f]
                packed = jnp.where(span(b, STEPS), moved(from_left[i, f], b - (LANES // 2 - STEPS)), packed)
                packed = jnp.where(span(b + STEPS, 2 * STEPS), moved(mine, b + STEPS), packed)
                packed = jnp.where(span(c, 2 * STEPS), moved(mine, c - LANES // 2 + 2 * STEPS), packed)
                packed = jnp.where(span(c + 2 * STEPS, STEPS), moved(from_right[i, f], c + 2 * STEPS), packed)
            fields.append(packed)
        e, u, v = fields
        for _ in range(STEPS):
            e, u, v = advance_vreg(e, u, v)
        patch[g, 0] = e
        patch[g, 1] = u
        patch[g, 2] = v

    first_in.wait()
    last_in.wait()
    for g in range(groups):
        for k in range(per_vreg):
            i = g * per_vreg + k
            b = 2 * k * slot
            c = b + slot
            for f in range(3):
                values = patch[g, f]
                first_buf[i, f] = jnp.where(lane < STEPS, moved(values, -(b + STEPS)), first_buf[i, f])
                last_buf[i, f] = jnp.where(
                    lane >= LANES - STEPS, moved(values, LANES - 2 * STEPS - c), last_buf[i, f]
                )
    first_out = pltpu.make_async_copy(first_buf, out.at[:, :, :, pl.ds(0, LANES)], sems.at[0])
    last_out = pltpu.make_async_copy(last_buf, out.at[:, :, :, pl.ds(cols - LANES, LANES)], sems.at[1])
    first_out.start()
    last_out.start()
    first_out.wait()
    last_out.wait()


def edge_fix(own, from_left, from_right, body):
    raw = pl.BlockSpec(memory_space=pl.ANY)
    return pl.pallas_call(
        edge_kernel,
        in_specs=[raw, raw, raw, raw],
        out_specs=raw,
        out_shape=jax.ShapeDtypeStruct(body.shape, body.dtype),
        scratch_shapes=[
            pltpu.VMEM((own.shape[0] // 4,) + own.shape[1:], jnp.float32),
            pltpu.VMEM(own.shape, jnp.float32),
            pltpu.VMEM(own.shape, jnp.float32),
            pltpu.VMEM(own.shape, jnp.float32),
            pltpu.VMEM(own.shape, jnp.float32),
            pltpu.VMEM(own.shape, jnp.float32),
            pltpu.SemaphoreType.DMA((5,)),
        ],
        input_output_aliases={3: 0},
    )(own, from_left, from_right, body)


def shards(state, noise, parents):
    count = lax.axis_size("ens")
    me = lax.axis_index("ens")
    per_dev = state.shape[0]
    dist = max(1, -(-per_dev // count))
    send_index, position = routing(parents, count, per_dev, dist, me)
    outgoing = jnp.take(state, send_index, axis=0, mode="clip")
    incoming = lax.all_to_all(outgoing, "ens", split_axis=0, concat_axis=0, tiled=True)
    own = edge_blocks(position, incoming, noise)
    ring = lax.axis_size("col")
    from_left = lax.ppermute(own, "col", [(i, (i + 1) % ring) for i in range(ring)])
    from_right = lax.ppermute(own, "col", [(i, (i - 1) % ring) for i in range(ring)])
    body = main_forecast(position, incoming, noise)
    return edge_fix(own, from_left, from_right, body)


def solution(mesh):
    placed = (P("ens", None, None, "col"), P("ens", None, None, "col"), P())
    return jax.shard_map(
        shards, mesh=mesh, in_specs=placed, out_specs=P("ens", None, None, "col"), check_vma=False
    )
```

```python
import jax
import jax.numpy as jnp
from jax import lax
from jax.experimental import pallas as pl
from jax.experimental.pallas import tpu as pltpu
from jax.sharding import PartitionSpec as P

STEPS = 4
LANES = 128
PAIR = 8
EDGE_GROUP = 8
GATHER_GROUP = 32

time_step = 0.3
coriolis = 0.2
gravity = 1.0


def routing(parents, count, per_dev, dist, me):
    blocks = parents.reshape(count, per_dev)
    owner = blocks // per_dev
    local = blocks % per_dev
    ids = jnp.arange(per_dev, dtype=jnp.int32)
    same = blocks[:, :, None] == blocks[:, None, :]
    earlier = ids[None, :] < ids[:, None]
    first = jnp.logical_not(jnp.any(same & earlier[None], axis=2))
    below = (
        (owner[:, :, None] == owner[:, None, :])
        & (blocks[:, None, :] < blocks[:, :, None])
        & first[:, None, :]
    )
    slot = jnp.sum(below.astype(jnp.int32), axis=2)
    slots = jnp.arange(dist, dtype=jnp.int32)
    pick = (owner == me)[:, None, :] & first[:, None, :] & (slot[:, None, :] == slots[None, :, None])
    send_index = jnp.sum(pick.astype(jnp.int32) * local[:, None, :], axis=2).reshape(-1)
    my_owner = lax.dynamic_index_in_dim(owner, me, 0, keepdims=False)
    my_slot = lax.dynamic_index_in_dim(slot, me, 0, keepdims=False)
    return send_index, my_owner * dist + my_slot


def update(e, u, v, xp, xm):
    rows = e.shape[-2]

    def yp(a):
        return pltpu.roll(a, rows - 1, 0)

    def ym(a):
        return pltpu.roll(a, 1, 0)

    e_xp, u_xp, v_xp = xp
    e_xm, u_xm, v_xm = xm
    e_yp, e_ym = yp(e), ym(e)
    u_yp, u_ym = yp(u), ym(u)
    v_yp, v_ym = yp(v), ym(v)
    dx_u = u_xp - u_xm
    dy_v = v_yp - v_ym
    dx_hu = dx_u + (e_xp * u_xp - e_xm * u_xm)
    dy_hv = dy_v + (e_yp * v_yp - e_ym * v_ym)
    half_step = 0.5 * time_step
    new_e = 0.25 * (e_xp + e_xm + e_yp + e_ym) - half_step * (dx_hu + dy_hv)
    new_u = (
        0.25 * (u_xp + u_xm + u_yp + u_ym)
        - half_step * (u * dx_u + v * (u_yp - u_ym) + gravity * (e_xp - e_xm))
        + (time_step * coriolis) * v
    )
    new_v = (
        0.25 * (v_xp + v_xm + v_yp + v_ym)
        - half_step * (u * (v_xp - v_xm) + v * dy_v + gravity * (e_yp - e_ym))
        - (time_step * coriolis) * u
    )
    return new_e, new_u, new_v


def advance_vreg(e, u, v):
    xp = tuple(pltpu.roll(a, LANES - 1, 1) for a in (e, u, v))
    xm = tuple(pltpu.roll(a, 1, 1) for a in (e, u, v))
    return update(e, u, v, xp, xm)


def sweep(src, dst, ncol, extra=None):
    rows = src.shape[-2]
    lane = lax.broadcasted_iota(jnp.int32, (rows, LANES), 1)
    first_lane = lane == 0
    last_lane = lane == LANES - 1

    def load(j):
        window = pl.ds((j % ncol) * LANES, LANES)
        e = src[0, :, window]
        u = src[1, :, window]
        v = src[2, :, window]
        if extra is not None:
            e = e + extra[0, :, window]
            u = u + extra[1, :, window]
            v = v + extra[2, :, window]
        return e, u, v

    def ahead(vals):
        return tuple(pltpu.roll(a, LANES - 1, 1) for a in vals)

    def behind(vals):
        return tuple(pltpu.roll(a, 1, 1) for a in vals)

    here = load(0)
    prev_behind = behind(load(ncol - 1)) if ncol > 1 else behind(here)
    here_behind = behind(here)
    here_ahead = ahead(here)
    for j in range(ncol):
        if ncol > 1:
            nxt = load(j + 1)
            nxt_ahead = ahead(nxt)
            nxt_behind = behind(nxt)
        else:
            nxt, nxt_ahead, nxt_behind = here, here_ahead, here_behind
        xp = [jnp.where(last_lane, a, b) for a, b in zip(nxt_ahead, here_ahead)]
        xm = [jnp.where(first_lane, a, b) for a, b in zip(prev_behind, here_behind)]
        e, u, v = here
        new_e, new_u, new_v = update(e, u, v, xp, xm)
        window = pl.ds(j * LANES, LANES)
        dst[0, :, window] = new_e
        dst[1, :, window] = new_u
        dst[2, :, window] = new_v
        prev_behind = here_behind
        here, here_behind, here_ahead = nxt, nxt_behind, nxt_ahead


def run_steps(chains, extras, ncol):
    for s in range(STEPS):
        for chain, extra in zip(chains, extras):
            sweep(chain[s], chain[s + 1], ncol, extra if s == 0 else None)


def chain_of(src, out, first, second):
    return [src] + [first if s % 2 == 0 else second for s in range(STEPS - 1)] + [out]


def main_kernel(pos_ref, *refs):
    incs = refs[:-4]
    noise_ref, out_ref, first, second = refs[-4:]
    ncol = noise_ref.shape[-1] // LANES
    chains = [chain_of(incs[k].at[0], out_ref.at[k], first.at[k], second.at[k]) for k in range(len(incs))]
    extras = [noise_ref.at[k] for k in range(len(incs))]
    run_steps(chains, extras, ncol)


def main_forecast(position, incoming, noise):
    per_dev, nf, rows, cols = noise.shape
    group = PAIR if per_dev % PAIR == 0 else 1

    def row_map(k):
        return lambda i, pos: (pos[i * group + k], 0, 0, 0)

    in_specs = [pl.BlockSpec((1, nf, rows, cols), row_map(k)) for k in range(group)]
    spec = pl.BlockSpec((group, nf, rows, cols), lambda i, pos: (i, 0, 0, 0))
    grid_spec = pltpu.PrefetchScalarGridSpec(
        num_scalar_prefetch=1,
        grid=(per_dev // group,),
        in_specs=in_specs + [spec],
        out_specs=spec,
        scratch_shapes=[pltpu.VMEM((group, nf, rows, cols), jnp.float32)] * 2,
    )
    return pl.pallas_call(
        main_kernel,
        grid_spec=grid_spec,
        out_shape=jax.ShapeDtypeStruct(noise.shape, noise.dtype),
    )(position, *([incoming] * group), noise)


def edges_kernel(pos_ref, *refs):
    group = (len(refs) - 3) // 2
    left_rows, right_rows = refs[:group], refs[group:2 * group]
    noise_left, noise_right, own = refs[2 * group:]
    rows = own.shape[-2]
    lane = lax.broadcasted_iota(jnp.int32, (rows, LANES), 1)
    keep_left = (lane < 2 * STEPS) | (lane >= LANES - STEPS)
    for k in range(group):
        for f in range(3):
            left = left_rows[k][0, f] + noise_left[k, f]
            right = pltpu.roll(right_rows[k][0, f] + noise_right[k, f], LANES // 2, 1)
            own[k, f] = jnp.where(keep_left, left, right)


def edge_blocks(position, incoming, noise):
    per_dev, nf, rows, cols = noise.shape
    last = cols // LANES - 1
    group = GATHER_GROUP if per_dev % GATHER_GROUP == 0 else 1

    def row_map(k, col):
        return lambda i, pos: (pos[i * group + k], 0, 0, col)

    left_specs = [pl.BlockSpec((1, nf, rows, LANES), row_map(k, 0)) for k in range(group)]
    right_specs = [pl.BlockSpec((1, nf, rows, LANES), row_map(k, last)) for k in range(group)]
    left = pl.BlockSpec((group, nf, rows, LANES), lambda i, pos: (i, 0, 0, 0))
    right = pl.BlockSpec((group, nf, rows, LANES), lambda i, pos: (i, 0, 0, last))
    out = pl.BlockSpec((group, nf, rows, LANES), lambda i, pos: (i, 0, 0, 0))
    grid_spec = pltpu.PrefetchScalarGridSpec(
        num_scalar_prefetch=1,
        grid=(per_dev // group,),
        in_specs=left_specs + right_specs + [left, right],
        out_specs=out,
    )
    return pl.pallas_call(
        edges_kernel,
        grid_spec=grid_spec,
        out_shape=jax.ShapeDtypeStruct((per_dev, nf, rows, LANES), noise.dtype),
    )(position, *([incoming] * (2 * group)), noise, noise)


def edge_kernel(own, from_left, from_right, body, out, patch, first_buf, last_buf, sems):
    rows = own.shape[-2]
    cols = body.shape[-1]
    lane = lax.broadcasted_iota(jnp.int32, (rows, LANES), 1)
    first_in = pltpu.make_async_copy(body.at[:, :, :, pl.ds(0, LANES)], first_buf, sems.at[0])
    last_in = pltpu.make_async_copy(body.at[:, :, :, pl.ds(cols - LANES, LANES)], last_buf, sems.at[1])
    first_in.start()
    last_in.start()

    slot = 16
    per_vreg = LANES // (2 * slot)
    groups = own.shape[0] // per_vreg

    def span(lo, size):
        return (lane >= lo) & (lane < lo + size)

    def moved(x, shift):
        return pltpu.roll(x, shift % LANES, 1)

    for g in range(groups):
        fields = []
        for f in range(3):
            packed = jnp.zeros((rows, LANES), jnp.float32)
            for k in range(per_vreg):
                i = g * per_vreg + k
                b = 2 * k * slot
                c = b + slot
                mine = own[i, f]
                packed = jnp.where(span(b, STEPS), moved(from_left[i, f], b - (LANES // 2 - STEPS)), packed)
                packed = jnp.where(span(b + STEPS, 2 * STEPS), moved(mine, b + STEPS), packed)
                packed = jnp.where(span(c, 2 * STEPS), moved(mine, c - LANES // 2 + 2 * STEPS), packed)
                packed = jnp.where(span(c + 2 * STEPS, STEPS), moved(from_right[i, f], c + 2 * STEPS), packed)
            fields.append(packed)
        e, u, v = fields
        for _ in range(STEPS):
            e, u, v = advance_vreg(e, u, v)
        patch[g, 0] = e
        patch[g, 1] = u
        patch[g, 2] = v

    first_in.wait()
    last_in.wait()
    for g in range(groups):
        for k in range(per_vreg):
            i = g * per_vreg + k
            b = 2 * k * slot
            c = b + slot
            for f in range(3):
                values = patch[g, f]
                first_buf[i, f] = jnp.where(lane < STEPS, moved(values, -(b + STEPS)), first_buf[i, f])
                last_buf[i, f] = jnp.where(
                    lane >= LANES - STEPS, moved(values, LANES - 2 * STEPS - c), last_buf[i, f]
                )
    first_out = pltpu.make_async_copy(first_buf, out.at[:, :, :, pl.ds(0, LANES)], sems.at[0])
    last_out = pltpu.make_async_copy(last_buf, out.at[:, :, :, pl.ds(cols - LANES, LANES)], sems.at[1])
    first_out.start()
    last_out.start()
    first_out.wait()
    last_out.wait()


def edge_fix(own, from_left, from_right, body):
    whole = pl.BlockSpec(memory_space=pltpu.VMEM)
    raw = pl.BlockSpec(memory_space=pl.ANY)
    return pl.pallas_call(
        edge_kernel,
        in_specs=[whole, whole, whole, raw],
        out_specs=raw,
        out_shape=jax.ShapeDtypeStruct(body.shape, body.dtype),
        scratch_shapes=[
            pltpu.VMEM((own.shape[0] // 4,) + own.shape[1:], jnp.float32),
            pltpu.VMEM(own.shape, jnp.float32),
            pltpu.VMEM(own.shape, jnp.float32),
            pltpu.SemaphoreType.DMA((2,)),
        ],
        input_output_aliases={3: 0},
    )(own, from_left, from_right, body)


def shards(state, noise, parents):
    count = lax.axis_size("ens")
    me = lax.axis_index("ens")
    per_dev = state.shape[0]
    dist = max(1, -(-per_dev // count))
    send_index, position = routing(parents, count, per_dev, dist, me)
    shifts = jnp.arange(count * dist, dtype=jnp.int32)
    by_shift = ((shifts // dist + me) % count) * dist + shifts % dist
    outgoing = jnp.take(state, jnp.take(send_index, by_shift), axis=0, mode="clip")
    chunks = [outgoing[:dist]]
    for k in range(1, count):
        pairs = [(i, (i + k) % count) for i in range(count)]
        chunks.append(lax.ppermute(outgoing[k * dist:(k + 1) * dist], "ens", pairs))
    incoming = jnp.concatenate(chunks, axis=0)
    owner = position // dist
    position = ((me - owner) % count) * dist + position % dist
    own = edge_blocks(position, incoming, noise)
    ring = lax.axis_size("col")
    from_left = lax.ppermute(own, "col", [(i, (i + 1) % ring) for i in range(ring)])
    from_right = lax.ppermute(own, "col", [(i, (i - 1) % ring) for i in range(ring)])
    body = main_forecast(position, incoming, noise)
    return edge_fix(own, from_left, from_right, body)


def solution(mesh):
    placed = (P("ens", None, None, "col"), P("ens", None, None, "col"), P())
    return jax.shard_map(
        shards, mesh=mesh, in_specs=placed, out_specs=P("ens", None, None, "col"), check_vma=False
    )
```

```python
import jax
import jax.numpy as jnp
from jax import lax
from jax.experimental import pallas as pl
from jax.experimental.pallas import tpu as pltpu
from jax.sharding import PartitionSpec as P

STEPS = 4
LANES = 128
PAIR = 8
EDGE_GROUP = 8
GATHER_GROUP = 32

time_step = 0.3
coriolis = 0.2
gravity = 1.0


def routing(parents, count, per_dev, dist, me):
    blocks = parents.reshape(count, per_dev)
    owner = blocks // per_dev
    local = blocks % per_dev
    ids = jnp.arange(per_dev, dtype=jnp.int32)
    same = blocks[:, :, None] == blocks[:, None, :]
    earlier = ids[None, :] < ids[:, None]
    first = jnp.logical_not(jnp.any(same & earlier[None], axis=2))
    below = (
        (owner[:, :, None] == owner[:, None, :])
        & (blocks[:, None, :] < blocks[:, :, None])
        & first[:, None, :]
    )
    slot = jnp.sum(below.astype(jnp.int32), axis=2)
    slots = jnp.arange(dist, dtype=jnp.int32)
    pick = (owner == me)[:, None, :] & first[:, None, :] & (slot[:, None, :] == slots[None, :, None])
    send_index = jnp.sum(pick.astype(jnp.int32) * local[:, None, :], axis=2).reshape(-1)
    my_owner = lax.dynamic_index_in_dim(owner, me, 0, keepdims=False)
    my_slot = lax.dynamic_index_in_dim(slot, me, 0, keepdims=False)
    return send_index, my_owner * dist + my_slot


def update(e, u, v, xp, xm):
    rows = e.shape[-2]

    def yp(a):
        return pltpu.roll(a, rows - 1, 0)

    def ym(a):
        return pltpu.roll(a, 1, 0)

    e_xp, u_xp, v_xp = xp
    e_xm, u_xm, v_xm = xm
    e_yp, e_ym = yp(e), ym(e)
    u_yp, u_ym = yp(u), ym(u)
    v_yp, v_ym = yp(v), ym(v)
    dx_u = u_xp - u_xm
    dy_v = v_yp - v_ym
    dx_hu = dx_u + (e_xp * u_xp - e_xm * u_xm)
    dy_hv = dy_v + (e_yp * v_yp - e_ym * v_ym)
    half_step = 0.5 * time_step
    new_e = 0.25 * (e_xp + e_xm + e_yp + e_ym) - half_step * (dx_hu + dy_hv)
    new_u = (
        0.25 * (u_xp + u_xm + u_yp + u_ym)
        - half_step * (u * dx_u + v * (u_yp - u_ym) + gravity * (e_xp - e_xm))
        + (time_step * coriolis) * v
    )
    new_v = (
        0.25 * (v_xp + v_xm + v_yp + v_ym)
        - half_step * (u * (v_xp - v_xm) + v * dy_v + gravity * (e_yp - e_ym))
        - (time_step * coriolis) * u
    )
    return new_e, new_u, new_v


def advance_vreg(e, u, v):
    xp = tuple(pltpu.roll(a, LANES - 1, 1) for a in (e, u, v))
    xm = tuple(pltpu.roll(a, 1, 1) for a in (e, u, v))
    return update(e, u, v, xp, xm)


def sweep(src, dst, ncol, extra=None):
    rows = src.shape[-2]
    lane = lax.broadcasted_iota(jnp.int32, (rows, LANES), 1)
    first_lane = lane == 0
    last_lane = lane == LANES - 1

    def load(j):
        window = pl.ds((j % ncol) * LANES, LANES)
        e = src[0, :, window]
        u = src[1, :, window]
        v = src[2, :, window]
        if extra is not None:
            e = e + extra[0, :, window]
            u = u + extra[1, :, window]
            v = v + extra[2, :, window]
        return e, u, v

    def ahead(vals):
        return tuple(pltpu.roll(a, LANES - 1, 1) for a in vals)

    def behind(vals):
        return tuple(pltpu.roll(a, 1, 1) for a in vals)

    here = load(0)
    prev_behind = behind(load(ncol - 1)) if ncol > 1 else behind(here)
    here_behind = behind(here)
    here_ahead = ahead(here)
    for j in range(ncol):
        if ncol > 1:
            nxt = load(j + 1)
            nxt_ahead = ahead(nxt)
            nxt_behind = behind(nxt)
        else:
            nxt, nxt_ahead, nxt_behind = here, here_ahead, here_behind
        xp = [jnp.where(last_lane, a, b) for a, b in zip(nxt_ahead, here_ahead)]
        xm = [jnp.where(first_lane, a, b) for a, b in zip(prev_behind, here_behind)]
        e, u, v = here
        new_e, new_u, new_v = update(e, u, v, xp, xm)
        window = pl.ds(j * LANES, LANES)
        dst[0, :, window] = new_e
        dst[1, :, window] = new_u
        dst[2, :, window] = new_v
        prev_behind = here_behind
        here, here_behind, here_ahead = nxt, nxt_behind, nxt_ahead


def run_steps(chains, extras, ncol):
    for s in range(STEPS):
        for chain, extra in zip(chains, extras):
            sweep(chain[s], chain[s + 1], ncol, extra if s == 0 else None)


def chain_of(src, out, first, second):
    return [src] + [first if s % 2 == 0 else second for s in range(STEPS - 1)] + [out]


def main_kernel(pos_ref, *refs):
    incs = refs[:-4]
    noise_ref, out_ref, first, second = refs[-4:]
    ncol = noise_ref.shape[-1] // LANES
    chains = [chain_of(incs[k].at[0], out_ref.at[k], first.at[k], second.at[k]) for k in range(len(incs))]
    extras = [noise_ref.at[k] for k in range(len(incs))]
    run_steps(chains, extras, ncol)


def main_forecast(position, incoming, noise):
    per_dev, nf, rows, cols = noise.shape
    group = PAIR if per_dev % PAIR == 0 else 1

    def row_map(k):
        return lambda i, pos: (pos[i * group + k], 0, 0, 0)

    in_specs = [pl.BlockSpec((1, nf, rows, cols), row_map(k)) for k in range(group)]
    spec = pl.BlockSpec((group, nf, rows, cols), lambda i, pos: (i, 0, 0, 0))
    grid_spec = pltpu.PrefetchScalarGridSpec(
        num_scalar_prefetch=1,
        grid=(per_dev // group,),
        in_specs=in_specs + [spec],
        out_specs=spec,
        scratch_shapes=[pltpu.VMEM((group, nf, rows, cols), jnp.float32)] * 2,
    )
    return pl.pallas_call(
        main_kernel,
        grid_spec=grid_spec,
        out_shape=jax.ShapeDtypeStruct(noise.shape, noise.dtype),
    )(position, *([incoming] * group), noise)


def edges_kernel(pos_ref, inc, noise_left, noise_right, own):
    rows = own.shape[-2]
    cols = inc.shape[-1]
    lane = lax.broadcasted_iota(jnp.int32, (rows, LANES), 1)
    keep_left = (lane < 2 * STEPS) | (lane >= LANES - STEPS)
    for k in range(own.shape[0]):
        row = pos_ref[k]
        for f in range(3):
            left = inc[row, f, :, pl.ds(0, LANES)] + noise_left[k, f]
            right = inc[row, f, :, pl.ds(cols - LANES, LANES)] + noise_right[k, f]
            own[k, f] = jnp.where(keep_left, left, pltpu.roll(right, LANES // 2, 1))


def edge_blocks(position, incoming, noise):
    per_dev, nf, rows, cols = noise.shape
    last = cols // LANES - 1
    whole = pl.BlockSpec(incoming.shape, lambda i, pos: (0, 0, 0, 0))
    left = pl.BlockSpec((per_dev, nf, rows, LANES), lambda i, pos: (0, 0, 0, 0))
    right = pl.BlockSpec((per_dev, nf, rows, LANES), lambda i, pos: (0, 0, 0, last))
    grid_spec = pltpu.PrefetchScalarGridSpec(
        num_scalar_prefetch=1,
        grid=(1,),
        in_specs=[whole, left, right],
        out_specs=left,
    )
    return pl.pallas_call(
        edges_kernel,
        grid_spec=grid_spec,
        out_shape=jax.ShapeDtypeStruct((per_dev, nf, rows, LANES), noise.dtype),
    )(position, incoming, noise, noise)


def edge_kernel(own, from_left, from_right, body, out, patch, first_buf, last_buf, sems):
    rows = own.shape[-2]
    cols = body.shape[-1]
    lane = lax.broadcasted_iota(jnp.int32, (rows, LANES), 1)
    first_in = pltpu.make_async_copy(body.at[:, :, :, pl.ds(0, LANES)], first_buf, sems.at[0])
    last_in = pltpu.make_async_copy(body.at[:, :, :, pl.ds(cols - LANES, LANES)], last_buf, sems.at[1])
    first_in.start()
    last_in.start()

    slot = 16
    per_vreg = LANES // (2 * slot)
    groups = own.shape[0] // per_vreg

    def span(lo, size):
        return (lane >= lo) & (lane < lo + size)

    def moved(x, shift):
        return pltpu.roll(x, shift % LANES, 1)

    for g in range(groups):
        fields = []
        for f in range(3):
            packed = jnp.zeros((rows, LANES), jnp.float32)
            for k in range(per_vreg):
                i = g * per_vreg + k
                b = 2 * k * slot
                c = b + slot
                mine = own[i, f]
                packed = jnp.where(span(b, STEPS), moved(from_left[i, f], b - (LANES // 2 - STEPS)), packed)
                packed = jnp.where(span(b + STEPS, 2 * STEPS), moved(mine, b + STEPS), packed)
                packed = jnp.where(span(c, 2 * STEPS), moved(mine, c - LANES // 2 + 2 * STEPS), packed)
                packed = jnp.where(span(c + 2 * STEPS, STEPS), moved(from_right[i, f], c + 2 * STEPS), packed)
            fields.append(packed)
        e, u, v = fields
        for _ in range(STEPS):
            e, u, v = advance_vreg(e, u, v)
        patch[g, 0] = e
        patch[g, 1] = u
        patch[g, 2] = v

    first_in.wait()
    last_in.wait()
    for g in range(groups):
        for k in range(per_vreg):
            i = g * per_vreg + k
            b = 2 * k * slot
            c = b + slot
            for f in range(3):
                values = patch[g, f]
                first_buf[i, f] = jnp.where(lane < STEPS, moved(values, -(b + STEPS)), first_buf[i, f])
                last_buf[i, f] = jnp.where(
                    lane >= LANES - STEPS, moved(values, LANES - 2 * STEPS - c), last_buf[i, f]
                )
    first_out = pltpu.make_async_copy(first_buf, out.at[:, :, :, pl.ds(0, LANES)], sems.at[0])
    last_out = pltpu.make_async_copy(last_buf, out.at[:, :, :, pl.ds(cols - LANES, LANES)], sems.at[1])
    first_out.start()
    last_out.start()
    first_out.wait()
    last_out.wait()


def edge_fix(own, from_left, from_right, body):
    whole = pl.BlockSpec(memory_space=pltpu.VMEM)
    raw = pl.BlockSpec(memory_space=pl.ANY)
    return pl.pallas_call(
        edge_kernel,
        in_specs=[whole, whole, whole, raw],
        out_specs=raw,
        out_shape=jax.ShapeDtypeStruct(body.shape, body.dtype),
        scratch_shapes=[
            pltpu.VMEM((own.shape[0] // 4,) + own.shape[1:], jnp.float32),
            pltpu.VMEM(own.shape, jnp.float32),
            pltpu.VMEM(own.shape, jnp.float32),
            pltpu.SemaphoreType.DMA((2,)),
        ],
        input_output_aliases={3: 0},
    )(own, from_left, from_right, body)


def shards(state, noise, parents):
    count = lax.axis_size("ens")
    me = lax.axis_index("ens")
    per_dev = state.shape[0]
    dist = max(1, -(-per_dev // count))
    send_index, position = routing(parents, count, per_dev, dist, me)
    outgoing = jnp.take(state, send_index, axis=0, mode="clip")
    incoming = lax.all_to_all(outgoing, "ens", split_axis=0, concat_axis=0, tiled=True)
    own = edge_blocks(position, incoming, noise)
    ring = lax.axis_size("col")
    from_left = lax.ppermute(own, "col", [(i, (i + 1) % ring) for i in range(ring)])
    from_right = lax.ppermute(own, "col", [(i, (i - 1) % ring) for i in range(ring)])
    body = main_forecast(position, incoming, noise)
    return edge_fix(own, from_left, from_right, body)


def solution(mesh):
    placed = (P("ens", None, None, "col"), P("ens", None, None, "col"), P())
    return jax.shard_map(
        shards, mesh=mesh, in_specs=placed, out_specs=P("ens", None, None, "col"), check_vma=False
    )
```

```python
import jax
import jax.numpy as jnp
from jax import lax
from jax.experimental import pallas as pl
from jax.experimental.pallas import tpu as pltpu
from jax.sharding import PartitionSpec as P

STEPS = 4
LANES = 128
PAIR = 8
EDGE_GROUP = 8
GATHER_GROUP = 32

time_step = 0.3
coriolis = 0.2
gravity = 1.0


def routing(parents, count, per_dev, dist, me):
    blocks = parents.reshape(count, per_dev)
    owner = blocks // per_dev
    local = blocks % per_dev
    ids = jnp.arange(per_dev, dtype=jnp.int32)
    same = blocks[:, :, None] == blocks[:, None, :]
    earlier = ids[None, :] < ids[:, None]
    first = jnp.logical_not(jnp.any(same & earlier[None], axis=2))
    below = (
        (owner[:, :, None] == owner[:, None, :])
        & (blocks[:, None, :] < blocks[:, :, None])
        & first[:, None, :]
    )
    slot = jnp.sum(below.astype(jnp.int32), axis=2)
    slots = jnp.arange(dist, dtype=jnp.int32)
    pick = (owner == me)[:, None, :] & first[:, None, :] & (slot[:, None, :] == slots[None, :, None])
    send_index = jnp.sum(pick.astype(jnp.int32) * local[:, None, :], axis=2).reshape(-1)
    my_owner = lax.dynamic_index_in_dim(owner, me, 0, keepdims=False)
    my_slot = lax.dynamic_index_in_dim(slot, me, 0, keepdims=False)
    return send_index, my_owner * dist + my_slot


def update(e, u, v, xp, xm):
    rows = e.shape[-2]

    def yp(a):
        return pltpu.roll(a, rows - 1, 0)

    def ym(a):
        return pltpu.roll(a, 1, 0)

    e_xp, u_xp, v_xp = xp
    e_xm, u_xm, v_xm = xm
    e_yp, e_ym = yp(e), ym(e)
    u_yp, u_ym = yp(u), ym(u)
    v_yp, v_ym = yp(v), ym(v)
    dx_u = u_xp - u_xm
    dy_v = v_yp - v_ym
    dx_hu = dx_u + (e_xp * u_xp - e_xm * u_xm)
    dy_hv = dy_v + (e_yp * v_yp - e_ym * v_ym)
    half_step = 0.5 * time_step
    new_e = 0.25 * (e_xp + e_xm + e_yp + e_ym) - half_step * (dx_hu + dy_hv)
    new_u = (
        0.25 * (u_xp + u_xm + u_yp + u_ym)
        - half_step * (u * dx_u + v * (u_yp - u_ym) + gravity * (e_xp - e_xm))
        + (time_step * coriolis) * v
    )
    new_v = (
        0.25 * (v_xp + v_xm + v_yp + v_ym)
        - half_step * (u * (v_xp - v_xm) + v * dy_v + gravity * (e_yp - e_ym))
        - (time_step * coriolis) * u
    )
    return new_e, new_u, new_v


def advance_vreg(e, u, v):
    xp = tuple(pltpu.roll(a, LANES - 1, 1) for a in (e, u, v))
    xm = tuple(pltpu.roll(a, 1, 1) for a in (e, u, v))
    return update(e, u, v, xp, xm)


def sweep(src, dst, ncol, extra=None):
    rows = src.shape[-2]
    lane = lax.broadcasted_iota(jnp.int32, (rows, LANES), 1)
    first_lane = lane == 0
    last_lane = lane == LANES - 1

    def load(j):
        window = pl.ds((j % ncol) * LANES, LANES)
        e = src[0, :, window]
        u = src[1, :, window]
        v = src[2, :, window]
        if extra is not None:
            e = e + extra[0, :, window]
            u = u + extra[1, :, window]
            v = v + extra[2, :, window]
        return e, u, v

    def ahead(vals):
        return tuple(pltpu.roll(a, LANES - 1, 1) for a in vals)

    def behind(vals):
        return tuple(pltpu.roll(a, 1, 1) for a in vals)

    here = load(0)
    prev_behind = behind(load(ncol - 1)) if ncol > 1 else behind(here)
    here_behind = behind(here)
    here_ahead = ahead(here)
    for j in range(ncol):
        if ncol > 1:
            nxt = load(j + 1)
            nxt_ahead = ahead(nxt)
            nxt_behind = behind(nxt)
        else:
            nxt, nxt_ahead, nxt_behind = here, here_ahead, here_behind
        xp = [jnp.where(last_lane, a, b) for a, b in zip(nxt_ahead, here_ahead)]
        xm = [jnp.where(first_lane, a, b) for a, b in zip(prev_behind, here_behind)]
        e, u, v = here
        new_e, new_u, new_v = update(e, u, v, xp, xm)
        window = pl.ds(j * LANES, LANES)
        dst[0, :, window] = new_e
        dst[1, :, window] = new_u
        dst[2, :, window] = new_v
        prev_behind = here_behind
        here, here_behind, here_ahead = nxt, nxt_behind, nxt_ahead


def run_steps(chains, extras, ncol):
    for s in range(STEPS):
        for chain, extra in zip(chains, extras):
            sweep(chain[s], chain[s + 1], ncol, extra if s == 0 else None)


def chain_of(src, out, first, second):
    return [src] + [first if s % 2 == 0 else second for s in range(STEPS - 1)] + [out]


def main_kernel(pos_ref, *refs):
    incs = refs[:-4]
    noise_ref, out_ref, first, second = refs[-4:]
    ncol = noise_ref.shape[-1] // LANES
    chains = [chain_of(incs[k].at[0], out_ref.at[k], first.at[k], second.at[k]) for k in range(len(incs))]
    extras = [noise_ref.at[k] for k in range(len(incs))]
    run_steps(chains, extras, ncol)


def main_forecast(position, incoming, noise):
    per_dev, nf, rows, cols = noise.shape
    group = PAIR if per_dev % PAIR == 0 else 1

    def row_map(k):
        return lambda i, pos: (pos[i * group + k], 0, 0, 0)

    in_specs = [pl.BlockSpec((1, nf, rows, cols), row_map(k)) for k in range(group)]
    spec = pl.BlockSpec((group, nf, rows, cols), lambda i, pos: (i, 0, 0, 0))
    grid_spec = pltpu.PrefetchScalarGridSpec(
        num_scalar_prefetch=1,
        grid=(per_dev // group,),
        in_specs=in_specs + [spec],
        out_specs=spec,
        scratch_shapes=[pltpu.VMEM((group, nf, rows, cols), jnp.float32)] * 2,
    )
    return pl.pallas_call(
        main_kernel,
        grid_spec=grid_spec,
        out_shape=jax.ShapeDtypeStruct(noise.shape, noise.dtype),
    )(position, *([incoming] * group), noise)


def edges_kernel(pos_ref, *refs):
    group = (len(refs) - 2) // 2
    left_rows, right_rows = refs[:group], refs[group:2 * group]
    noise_packed, own = refs[2 * group:]
    rows = own.shape[-2]
    lane = lax.broadcasted_iota(jnp.int32, (rows, LANES), 1)
    keep_left = (lane < 2 * STEPS) | (lane >= LANES - STEPS)
    for k in range(group):
        for f in range(3):
            right = pltpu.roll(right_rows[k][0, f], LANES // 2, 1)
            own[k, f] = jnp.where(keep_left, left_rows[k][0, f], right) + noise_packed[k, f]


def edge_blocks(position, incoming, noise_packed):
    per_dev, nf, rows, _ = noise_packed.shape
    last = incoming.shape[-1] // LANES - 1
    group = GATHER_GROUP if per_dev % GATHER_GROUP == 0 else 1

    def row_map(k, col):
        return lambda i, pos: (pos[i * group + k], 0, 0, col)

    left_specs = [pl.BlockSpec((1, nf, rows, LANES), row_map(k, 0)) for k in range(group)]
    right_specs = [pl.BlockSpec((1, nf, rows, LANES), row_map(k, last)) for k in range(group)]
    packed = pl.BlockSpec((group, nf, rows, LANES), lambda i, pos: (i, 0, 0, 0))
    grid_spec = pltpu.PrefetchScalarGridSpec(
        num_scalar_prefetch=1,
        grid=(per_dev // group,),
        in_specs=left_specs + right_specs + [packed],
        out_specs=packed,
    )
    return pl.pallas_call(
        edges_kernel,
        grid_spec=grid_spec,
        out_shape=jax.ShapeDtypeStruct(noise_packed.shape, noise_packed.dtype),
    )(position, *([incoming] * (2 * group)), noise_packed)


def pack_edges(a):
    lane = lax.broadcasted_iota(jnp.int32, a.shape[:-1] + (LANES,), a.ndim - 1)
    keep_left = (lane < 2 * STEPS) | (lane >= LANES - STEPS)
    return jnp.where(keep_left, a[..., :LANES], jnp.roll(a[..., -LANES:], LANES // 2, axis=-1))


def edge_kernel(own, from_left, from_right, body, out, patch, first_buf, last_buf, sems):
    rows = own.shape[-2]
    cols = body.shape[-1]
    lane = lax.broadcasted_iota(jnp.int32, (rows, LANES), 1)
    first_in = pltpu.make_async_copy(body.at[:, :, :, pl.ds(0, LANES)], first_buf, sems.at[0])
    last_in = pltpu.make_async_copy(body.at[:, :, :, pl.ds(cols - LANES, LANES)], last_buf, sems.at[1])
    first_in.start()
    last_in.start()

    slot = 16
    per_vreg = LANES // (2 * slot)
    groups = own.shape[0] // per_vreg

    def span(lo, size):
        return (lane >= lo) & (lane < lo + size)

    def moved(x, shift):
        return pltpu.roll(x, shift % LANES, 1)

    for g in range(groups):
        fields = []
        for f in range(3):
            packed = jnp.zeros((rows, LANES), jnp.float32)
            for k in range(per_vreg):
                i = g * per_vreg + k
                b = 2 * k * slot
                c = b + slot
                mine = own[i, f]
                packed = jnp.where(span(b, STEPS), moved(from_left[i, f], b - (LANES // 2 - STEPS)), packed)
                packed = jnp.where(span(b + STEPS, 2 * STEPS), moved(mine, b + STEPS), packed)
                packed = jnp.where(span(c, 2 * STEPS), moved(mine, c - LANES // 2 + 2 * STEPS), packed)
                packed = jnp.where(span(c + 2 * STEPS, STEPS), moved(from_right[i, f], c + 2 * STEPS), packed)
            fields.append(packed)
        e, u, v = fields
        for _ in range(STEPS):
            e, u, v = advance_vreg(e, u, v)
        patch[g, 0] = e
        patch[g, 1] = u
        patch[g, 2] = v

    first_in.wait()
    last_in.wait()
    for g in range(groups):
        for k in range(per_vreg):
            i = g * per_vreg + k
            b = 2 * k * slot
            c = b + slot
            for f in range(3):
                values = patch[g, f]
                first_buf[i, f] = jnp.where(lane < STEPS, moved(values, -(b + STEPS)), first_buf[i, f])
                last_buf[i, f] = jnp.where(
                    lane >= LANES - STEPS, moved(values, LANES - 2 * STEPS - c), last_buf[i, f]
                )
    first_out = pltpu.make_async_copy(first_buf, out.at[:, :, :, pl.ds(0, LANES)], sems.at[0])
    last_out = pltpu.make_async_copy(last_buf, out.at[:, :, :, pl.ds(cols - LANES, LANES)], sems.at[1])
    first_out.start()
    last_out.start()
    first_out.wait()
    last_out.wait()


def edge_fix(own, from_left, from_right, body):
    whole = pl.BlockSpec(memory_space=pltpu.VMEM)
    raw = pl.BlockSpec(memory_space=pl.ANY)
    return pl.pallas_call(
        edge_kernel,
        in_specs=[whole, whole, whole, raw],
        out_specs=raw,
        out_shape=jax.ShapeDtypeStruct(body.shape, body.dtype),
        scratch_shapes=[
            pltpu.VMEM((own.shape[0] // 4,) + own.shape[1:], jnp.float32),
            pltpu.VMEM(own.shape, jnp.float32),
            pltpu.VMEM(own.shape, jnp.float32),
            pltpu.SemaphoreType.DMA((2,)),
        ],
        input_output_aliases={3: 0},
    )(own, from_left, from_right, body)


def shards(state, noise, parents):
    count = lax.axis_size("ens")
    me = lax.axis_index("ens")
    per_dev = state.shape[0]
    dist = max(1, -(-per_dev // count))
    send_index, position = routing(parents, count, per_dev, dist, me)
    outgoing = jnp.take(state, send_index, axis=0, mode="clip")
    incoming = lax.all_to_all(outgoing, "ens", split_axis=0, concat_axis=0, tiled=True)
    own = edge_blocks(position, incoming, pack_edges(noise))
    ring = lax.axis_size("col")
    from_left = lax.ppermute(own, "col", [(i, (i + 1) % ring) for i in range(ring)])
    from_right = lax.ppermute(own, "col", [(i, (i - 1) % ring) for i in range(ring)])
    body = main_forecast(position, incoming, noise)
    return edge_fix(own, from_left, from_right, body)


def solution(mesh):
    placed = (P("ens", None, None, "col"), P("ens", None, None, "col"), P())
    return jax.shard_map(
        shards, mesh=mesh, in_specs=placed, out_specs=P("ens", None, None, "col"), check_vma=False
    )
```

```python
import jax
import jax.numpy as jnp
from jax import lax
from jax.experimental import pallas as pl
from jax.experimental.pallas import tpu as pltpu
from jax.sharding import PartitionSpec as P

STEPS = 4
LANES = 128
PAIR = 8
EDGE_GROUP = 8
GATHER_GROUP = 32

time_step = 0.3
coriolis = 0.2
gravity = 1.0


def routing(parents, count, per_dev, dist, me):
    blocks = parents.reshape(count, per_dev)
    owner = blocks // per_dev
    local = blocks % per_dev
    ids = jnp.arange(per_dev, dtype=jnp.int32)
    same = blocks[:, :, None] == blocks[:, None, :]
    earlier = ids[None, :] < ids[:, None]
    first = jnp.logical_not(jnp.any(same & earlier[None], axis=2))
    below = (
        (owner[:, :, None] == owner[:, None, :])
        & (blocks[:, None, :] < blocks[:, :, None])
        & first[:, None, :]
    )
    slot = jnp.sum(below.astype(jnp.int32), axis=2)
    slots = jnp.arange(dist, dtype=jnp.int32)
    pick = (owner == me)[:, None, :] & first[:, None, :] & (slot[:, None, :] == slots[None, :, None])
    send_index = jnp.sum(pick.astype(jnp.int32) * local[:, None, :], axis=2).reshape(-1)
    my_owner = lax.dynamic_index_in_dim(owner, me, 0, keepdims=False)
    my_slot = lax.dynamic_index_in_dim(slot, me, 0, keepdims=False)
    my_first = lax.dynamic_index_in_dim(first, me, 0, keepdims=False)
    position = my_owner * dist + my_slot
    order = jnp.cumsum(my_first.astype(jnp.int32)) - 1
    matches = (position[:, None] == position[None, :]) & my_first[None, :]
    which = jnp.sum(jnp.where(matches, order[None, :], 0), axis=1)
    distinct = jnp.arange(per_dev // 2, dtype=jnp.int32)
    unique = jnp.sum(jnp.where(my_first[None, :] & (order[None, :] == distinct[:, None]), position[None, :], 0), axis=1)
    return send_index, position, unique, which


def update(e, u, v, xp, xm):
    rows = e.shape[-2]

    def yp(a):
        return pltpu.roll(a, rows - 1, 0)

    def ym(a):
        return pltpu.roll(a, 1, 0)

    e_xp, u_xp, v_xp = xp
    e_xm, u_xm, v_xm = xm
    e_yp, e_ym = yp(e), ym(e)
    u_yp, u_ym = yp(u), ym(u)
    v_yp, v_ym = yp(v), ym(v)
    dx_u = u_xp - u_xm
    dy_v = v_yp - v_ym
    dx_hu = dx_u + (e_xp * u_xp - e_xm * u_xm)
    dy_hv = dy_v + (e_yp * v_yp - e_ym * v_ym)
    half_step = 0.5 * time_step
    new_e = 0.25 * (e_xp + e_xm + e_yp + e_ym) - half_step * (dx_hu + dy_hv)
    new_u = (
        0.25 * (u_xp + u_xm + u_yp + u_ym)
        - half_step * (u * dx_u + v * (u_yp - u_ym) + gravity * (e_xp - e_xm))
        + (time_step * coriolis) * v
    )
    new_v = (
        0.25 * (v_xp + v_xm + v_yp + v_ym)
        - half_step * (u * (v_xp - v_xm) + v * dy_v + gravity * (e_yp - e_ym))
        - (time_step * coriolis) * u
    )
    return new_e, new_u, new_v


def advance_vreg(e, u, v):
    xp = tuple(pltpu.roll(a, LANES - 1, 1) for a in (e, u, v))
    xm = tuple(pltpu.roll(a, 1, 1) for a in (e, u, v))
    return update(e, u, v, xp, xm)


def sweep(src, dst, ncol, extra=None):
    rows = src.shape[-2]
    lane = lax.broadcasted_iota(jnp.int32, (rows, LANES), 1)
    first_lane = lane == 0
    last_lane = lane == LANES - 1

    def load(j):
        window = pl.ds((j % ncol) * LANES, LANES)
        e = src[0, :, window]
        u = src[1, :, window]
        v = src[2, :, window]
        if extra is not None:
            e = e + extra[0, :, window]
            u = u + extra[1, :, window]
            v = v + extra[2, :, window]
        return e, u, v

    def ahead(vals):
        return tuple(pltpu.roll(a, LANES - 1, 1) for a in vals)

    def behind(vals):
        return tuple(pltpu.roll(a, 1, 1) for a in vals)

    here = load(0)
    prev_behind = behind(load(ncol - 1)) if ncol > 1 else behind(here)
    here_behind = behind(here)
    here_ahead = ahead(here)
    for j in range(ncol):
        if ncol > 1:
            nxt = load(j + 1)
            nxt_ahead = ahead(nxt)
            nxt_behind = behind(nxt)
        else:
            nxt, nxt_ahead, nxt_behind = here, here_ahead, here_behind
        xp = [jnp.where(last_lane, a, b) for a, b in zip(nxt_ahead, here_ahead)]
        xm = [jnp.where(first_lane, a, b) for a, b in zip(prev_behind, here_behind)]
        e, u, v = here
        new_e, new_u, new_v = update(e, u, v, xp, xm)
        window = pl.ds(j * LANES, LANES)
        dst[0, :, window] = new_e
        dst[1, :, window] = new_u
        dst[2, :, window] = new_v
        prev_behind = here_behind
        here, here_behind, here_ahead = nxt, nxt_behind, nxt_ahead


def run_steps(chains, extras, ncol):
    for s in range(STEPS):
        for chain, extra in zip(chains, extras):
            sweep(chain[s], chain[s + 1], ncol, extra if s == 0 else None)


def chain_of(src, out, first, second):
    return [src] + [first if s % 2 == 0 else second for s in range(STEPS - 1)] + [out]


def main_kernel(pos_ref, *refs):
    incs = refs[:-4]
    noise_ref, out_ref, first, second = refs[-4:]
    ncol = noise_ref.shape[-1] // LANES
    chains = [chain_of(incs[k].at[0], out_ref.at[k], first.at[k], second.at[k]) for k in range(len(incs))]
    extras = [noise_ref.at[k] for k in range(len(incs))]
    run_steps(chains, extras, ncol)


def main_forecast(position, incoming, noise):
    per_dev, nf, rows, cols = noise.shape
    group = PAIR if per_dev % PAIR == 0 else 1

    def row_map(k):
        return lambda i, pos: (pos[i * group + k], 0, 0, 0)

    in_specs = [pl.BlockSpec((1, nf, rows, cols), row_map(k)) for k in range(group)]
    spec = pl.BlockSpec((group, nf, rows, cols), lambda i, pos: (i, 0, 0, 0))
    grid_spec = pltpu.PrefetchScalarGridSpec(
        num_scalar_prefetch=1,
        grid=(per_dev // group,),
        in_specs=in_specs + [spec],
        out_specs=spec,
        scratch_shapes=[pltpu.VMEM((group, nf, rows, cols), jnp.float32)] * 2,
    )
    return pl.pallas_call(
        main_kernel,
        grid_spec=grid_spec,
        out_shape=jax.ShapeDtypeStruct(noise.shape, noise.dtype),
    )(position, *([incoming] * group), noise)


def edges_kernel(unique_ref, which_ref, *refs):
    count = (len(refs) - 3) // 2
    left_rows, right_rows = refs[:count], refs[count:2 * count]
    noise_packed, own, stage = refs[2 * count:]
    rows = own.shape[-2]
    lane = lax.broadcasted_iota(jnp.int32, (rows, LANES), 1)
    keep_left = (lane < 2 * STEPS) | (lane >= LANES - STEPS)
    for j in range(count):
        for f in range(3):
            right = pltpu.roll(right_rows[j][0, f], LANES // 2, 1)
            stage[j, f] = jnp.where(keep_left, left_rows[j][0, f], right)
    for k in range(own.shape[0]):
        row = which_ref[k]
        for f in range(3):
            own[k, f] = stage[row, f] + noise_packed[k, f]


def edge_blocks(unique, which, incoming, noise_packed):
    per_dev, nf, rows, _ = noise_packed.shape
    last = incoming.shape[-1] // LANES - 1
    count = unique.shape[0]

    def row_map(j, col):
        return lambda i, uniq, wh: (uniq[j], 0, 0, col)

    left_specs = [pl.BlockSpec((1, nf, rows, LANES), row_map(j, 0)) for j in range(count)]
    right_specs = [pl.BlockSpec((1, nf, rows, LANES), row_map(j, last)) for j in range(count)]
    packed = pl.BlockSpec((per_dev, nf, rows, LANES), lambda i, uniq, wh: (0, 0, 0, 0))
    grid_spec = pltpu.PrefetchScalarGridSpec(
        num_scalar_prefetch=2,
        grid=(1,),
        in_specs=left_specs + right_specs + [packed],
        out_specs=packed,
        scratch_shapes=[pltpu.VMEM((count, nf, rows, LANES), jnp.float32)],
    )
    return pl.pallas_call(
        edges_kernel,
        grid_spec=grid_spec,
        out_shape=jax.ShapeDtypeStruct(noise_packed.shape, noise_packed.dtype),
    )(unique, which, *([incoming] * (2 * count)), noise_packed)


def pack_edges(a):
    lane = lax.broadcasted_iota(jnp.int32, a.shape[:-1] + (LANES,), a.ndim - 1)
    keep_left = (lane < 2 * STEPS) | (lane >= LANES - STEPS)
    return jnp.where(keep_left, a[..., :LANES], jnp.roll(a[..., -LANES:], LANES // 2, axis=-1))


def edge_kernel(own, from_left, from_right, body, out, patch, first_buf, last_buf, sems):
    rows = own.shape[-2]
    cols = body.shape[-1]
    lane = lax.broadcasted_iota(jnp.int32, (rows, LANES), 1)
    first_in = pltpu.make_async_copy(body.at[:, :, :, pl.ds(0, LANES)], first_buf, sems.at[0])
    last_in = pltpu.make_async_copy(body.at[:, :, :, pl.ds(cols - LANES, LANES)], last_buf, sems.at[1])
    first_in.start()
    last_in.start()

    slot = 16
    per_vreg = LANES // (2 * slot)
    groups = own.shape[0] // per_vreg

    def span(lo, size):
        return (lane >= lo) & (lane < lo + size)

    def moved(x, shift):
        return pltpu.roll(x, shift % LANES, 1)

    for g in range(groups):
        fields = []
        for f in range(3):
            packed = jnp.zeros((rows, LANES), jnp.float32)
            for k in range(per_vreg):
                i = g * per_vreg + k
                b = 2 * k * slot
                c = b + slot
                mine = own[i, f]
                packed = jnp.where(span(b, STEPS), moved(from_left[i, f], b - (LANES // 2 - STEPS)), packed)
                packed = jnp.where(span(b + STEPS, 2 * STEPS), moved(mine, b + STEPS), packed)
                packed = jnp.where(span(c, 2 * STEPS), moved(mine, c - LANES // 2 + 2 * STEPS), packed)
                packed = jnp.where(span(c + 2 * STEPS, STEPS), moved(from_right[i, f], c + 2 * STEPS), packed)
            fields.append(packed)
        e, u, v = fields
        for _ in range(STEPS):
            e, u, v = advance_vreg(e, u, v)
        patch[g, 0] = e
        patch[g, 1] = u
        patch[g, 2] = v

    first_in.wait()
    last_in.wait()
    for g in range(groups):
        for k in range(per_vreg):
            i = g * per_vreg + k
            b = 2 * k * slot
            c = b + slot
            for f in range(3):
                values = patch[g, f]
                first_buf[i, f] = jnp.where(lane < STEPS, moved(values, -(b + STEPS)), first_buf[i, f])
                last_buf[i, f] = jnp.where(
                    lane >= LANES - STEPS, moved(values, LANES - 2 * STEPS - c), last_buf[i, f]
                )
    first_out = pltpu.make_async_copy(first_buf, out.at[:, :, :, pl.ds(0, LANES)], sems.at[0])
    last_out = pltpu.make_async_copy(last_buf, out.at[:, :, :, pl.ds(cols - LANES, LANES)], sems.at[1])
    first_out.start()
    last_out.start()
    first_out.wait()
    last_out.wait()


def edge_fix(own, from_left, from_right, body):
    whole = pl.BlockSpec(memory_space=pltpu.VMEM)
    raw = pl.BlockSpec(memory_space=pl.ANY)
    return pl.pallas_call(
        edge_kernel,
        in_specs=[whole, whole, whole, raw],
        out_specs=raw,
        out_shape=jax.ShapeDtypeStruct(body.shape, body.dtype),
        scratch_shapes=[
            pltpu.VMEM((own.shape[0] // 4,) + own.shape[1:], jnp.float32),
            pltpu.VMEM(own.shape, jnp.float32),
            pltpu.VMEM(own.shape, jnp.float32),
            pltpu.SemaphoreType.DMA((2,)),
        ],
        input_output_aliases={3: 0},
    )(own, from_left, from_right, body)


def shards(state, noise, parents):
    count = lax.axis_size("ens")
    me = lax.axis_index("ens")
    per_dev = state.shape[0]
    dist = max(1, -(-per_dev // count))
    send_index, position, unique, which = routing(parents, count, per_dev, dist, me)
    outgoing = jnp.take(state, send_index, axis=0, mode="clip")
    incoming = lax.all_to_all(outgoing, "ens", split_axis=0, concat_axis=0, tiled=True)
    own = edge_blocks(unique, which, incoming, pack_edges(noise))
    ring = lax.axis_size("col")
    from_left = lax.ppermute(own, "col", [(i, (i + 1) % ring) for i in range(ring)])
    from_right = lax.ppermute(own, "col", [(i, (i - 1) % ring) for i in range(ring)])
    body = main_forecast(position, incoming, noise)
    return edge_fix(own, from_left, from_right, body)


def solution(mesh):
    placed = (P("ens", None, None, "col"), P("ens", None, None, "col"), P())
    return jax.shard_map(
        shards, mesh=mesh, in_specs=placed, out_specs=P("ens", None, None, "col"), check_vma=False
    )
```
